32 devices in a mesh: blk: 8 (over z, core), grp: 4 (over y, x).
Axes of the slice: x: 2, y: 2, z: 4, core: 2. Of those that a mesh axis runs over, the one named last changes fastest.
Arguments:
- block_values: bfloat16 [1536, 16, 64, 64], P('blk', 'grp'), may hold values from -1.5 to 1.5
- block_columns: int32 [1536, 16], P('blk', 'grp'), may hold values from 0 to 1535, as said below
- row_counts: int32 [1536], P('blk'), may hold values from 6 to 16
- prolong_blocks: bfloat16 [1536, 64, 64], P(('blk', 'grp')), may hold values from -0.75 to 0.75
- aggregates: int32 [1536], P(('blk', 'grp')), may hold values from 0 to 31, as said below
Outputs:
- coarse_blocks: float32 [32, 32, 64, 64], P('grp', 'blk')
The draws below stay inside these ranges and needn't reach their ends.
Inputs may be any that keep to these rules, and one draw needn't show every extreme that they name: `aggregates`: the aggregate of a fine block row of panel p, rows p * 192 to (p + 1) * 192 - 1, lies in p * 4 to (p + 1) * 4 - 1. `block_columns`: A block column of a row of panel p lies in a panel p + d modulo the number of panels, for some d of -2 to 2; slot 0 of each row holds the row itself.
All inputs are finite; a program needn't handle non-finite values.
Results may differ from the reference program's by a relative error of at most 0.0029.
Values may be sent and summed in bfloat16 or wider, within the bound.
No kernel may reach another device: no remote copies, remote signals or barrier semaphores. Data moves between devices by JAX's collectives and lax.ppermute only.
A program may use at most 192 MiB of HBM per device.

```python
import jax
import jax.numpy as jnp
from jax import lax

BS = 64
K = 16
CB = 4
RBG = 48
RB = 192
NB = 1536
N_BLK = 8
N_GRP = 4


def draw_aggregates(key, part):
    positions = jnp.arange(NB, dtype=jnp.int32)
    panel = positions // RB
    within = positions % RB
    picked = jax.random.randint(key, (NB,), 0, CB, dtype=jnp.int32)
    picked = jnp.where(within == 0, 0, picked)
    picked = jnp.where(within == RB - 1, CB - 1, picked)
    return (panel * CB + picked).astype(jnp.int32)


def draw_block_columns(key, part):
    key_offset = jax.random.fold_in(key, 11)
    key_within = jax.random.fold_in(key, 12)
    rows = jnp.arange(NB, dtype=jnp.int32)[:, None]
    slots = jnp.arange(K, dtype=jnp.int32)[None, :]
    panel = rows // RB
    offset = jax.random.randint(key_offset, (NB, K), -2, 3, dtype=jnp.int32)
    within = jax.random.randint(key_within, (NB, K), 0, RB, dtype=jnp.int32)
    panels_total = NB // RB
    columns = jnp.mod(panel + offset, panels_total) * RB + within
    columns = jnp.where(slots == 0, rows, columns)
    corner = jnp.logical_and(rows == 0, slots == K - 1)
    columns = jnp.where(corner, NB - 1, columns)
    return columns.astype(jnp.int32)


def touch_ends(result, rng, smallest, largest):
    index_at = [jax.random.randint(jax.random.fold_in(rng, axis), (), 0, length) for axis, length in enumerate(result.shape)]
    widest = result.shape.index(max(result.shape))
    next_to = index_at[:widest] + [(index_at[widest] + 1) % result.shape[widest]] + index_at[widest + 1:]
    return result.at[tuple(index_at)].set(smallest).at[tuple(next_to)].set(largest)


def levels(own_key, dims, split, low, high):
    factor_of = 1.0
    for dim, blocks in split:
        steps = jax.random.uniform(jax.random.fold_in(jax.random.fold_in(own_key, 6), dim), (blocks,), jnp.float32, low / len(split), high / len(split))
        factor_of = factor_of * jnp.repeat(jnp.exp(steps), dims[dim] // blocks).reshape((-1,) + (1,) * (len(dims) - 1 - dim))
    return factor_of


def centred(key, extent, width, reach, cuts=(), kind=jnp.bfloat16):
    drawn = width * jax.random.normal(key, extent, jnp.float32)
    if cuts:
        drawn = drawn * levels(key, extent, cuts, -0.22, 0.18)
    return jnp.clip(drawn, -reach, reach).astype(kind)


def setup_inputs(seed: int = 0) -> dict:
    arg_keys = jax.random.split(jax.random.key(seed), 6)
    block_values = centred(arg_keys[0], (NB, K, BS, BS), 0.25, 1.5, ((0, 8), (1, 4)))
    block_columns = draw_block_columns(jax.random.fold_in(arg_keys[5], 71), 0)
    row_counts = touch_ends(jax.random.randint(arg_keys[2], (NB,), 6, K + 1), jax.random.fold_in(arg_keys[2], 1), 6, K).astype(jnp.int32)
    prolong_blocks = centred(arg_keys[3], (NB, BS, BS), BS ** -0.5, 0.75, ((0, 32),))
    aggregates = draw_aggregates(jax.random.fold_in(arg_keys[5], 71), 0)
    return {"block_values": block_values, "block_columns": block_columns, "row_counts": row_counts, "prolong_blocks": prolong_blocks, "aggregates": aggregates}


def reference(block_values, block_columns, row_counts, prolong_blocks, aggregates):
    panel_rows = RBG * N_GRP
    coarse_count = CB * N_BLK
    slot_index = jnp.arange(K, dtype=jnp.int32)

    def panel_step(accumulated, panel):
        start = (panel * panel_rows).astype(jnp.int32)
        values = lax.dynamic_slice_in_dim(block_values, start, panel_rows, 0).astype(jnp.float32)
        columns = lax.dynamic_slice_in_dim(block_columns, start, panel_rows, 0)
        counts_here = lax.dynamic_slice_in_dim(row_counts, start, panel_rows, 0)
        own_blocks = lax.dynamic_slice_in_dim(prolong_blocks, start, panel_rows, 0).astype(jnp.float32)
        own_aggs = lax.dynamic_slice_in_dim(aggregates, start, panel_rows, 0)
        picked = jnp.take(prolong_blocks, columns, axis=0).astype(jnp.float32)
        picked_aggs = jnp.take(aggregates, columns, axis=0)
        product = jnp.einsum('rkab,rkbc->rkac', values, picked)
        live = slot_index[None, :] < counts_here[:, None]
        product = jnp.where(live[:, :, None, None], product, 0.0).astype(jnp.bfloat16)
        product = lax.optimization_barrier(product).astype(jnp.float32)
        restricted = jnp.einsum('rba,rkbc->rkac', own_blocks, product)
        target = picked_aggs * coarse_count + own_aggs[:, None]
        accumulated = accumulated.at[target.reshape(-1)].add(restricted.reshape(-1, BS, BS))
        return accumulated, None

    total = jnp.zeros((coarse_count * coarse_count, BS, BS), jnp.float32)
    total, _ = lax.scan(panel_step, total, jnp.arange(N_BLK, dtype=jnp.int32))
    return total.reshape(coarse_count, coarse_count, BS, BS)
```

```python
import functools

import jax
import jax.numpy as jnp
from jax import lax
from jax.experimental import pallas as pl
from jax.experimental.pallas import tpu as pltpu
from jax.sharding import PartitionSpec as P

CB = 4
ROWS_PER_STEP = 16


def passed_along(block, axis, distance):
    devices = range(lax.axis_size(axis))
    route = [((i - distance) % len(devices), i) for i in devices]
    return lax.ppermute(block, axis, route)


def coarse_kernel(rows_ref, target_ref, live_ref, values_ref, own_t_ref, *rest):
    pieces = rest[:5]
    acc_ref, window, sems = rest[5:]
    step = pl.program_id(0)
    rows_here, slots, bs, _ = values_ref.shape
    panel_length = pieces[0].shape[0]

    @pl.when(step == 0)
    def _():
        copies = []
        for k, piece in enumerate(pieces):
            cp = pltpu.make_async_copy(
                piece, window.at[pl.ds(k * panel_length, panel_length)], sems.at[k]
            )
            cp.start()
            copies.append(cp)
        for cp in copies:
            cp.wait()
        acc_ref[...] = jnp.zeros_like(acc_ref)

    def row_body(r, carry):
        row = step * rows_here + r
        own_t = own_t_ref[row]
        for s in range(slots):
            n = row * slots + s
            picked = window[rows_ref[n]]
            product = jnp.dot(
                values_ref[r, s], picked, preferred_element_type=jnp.float32
            )
            product = jnp.where(live_ref[n] > 0, product, 0.0).astype(jnp.bfloat16)
            restricted = jnp.dot(own_t, product, preferred_element_type=jnp.float32)
            t = target_ref[n]
            acc_ref[t] = acc_ref[t] + restricted
        return carry

    lax.fori_loop(0, rows_here, row_body, 0)


def coarse_partial(rows, target, live, values, own_t, pieces, n_targets):
    panel_length, slots, bs, _ = values.shape
    rows_per_step = min(ROWS_PER_STEP, panel_length)
    grid = (panel_length // rows_per_step,)
    window_rows = 5 * pieces[0].shape[0]
    return pl.pallas_call(
        coarse_kernel,
        out_shape=jax.ShapeDtypeStruct((n_targets, bs, bs), jnp.float32),
        grid_spec=pltpu.PrefetchScalarGridSpec(
            num_scalar_prefetch=3,
            grid=grid,
            in_specs=[
                pl.BlockSpec((rows_per_step, slots, bs, bs), lambda i, *_: (i, 0, 0, 0)),
                pl.BlockSpec(memory_space=pltpu.VMEM),
            ]
            + [pl.BlockSpec(memory_space=pl.ANY)] * 5,
            out_specs=pl.BlockSpec((n_targets, bs, bs), lambda i, *_: (0, 0, 0)),
            scratch_shapes=[
                pltpu.VMEM((window_rows, bs, bs), jnp.bfloat16),
                pltpu.SemaphoreType.DMA((5,)),
            ],
        ),
        compiler_params=pltpu.CompilerParams(
            dimension_semantics=("arbitrary",),
            vmem_limit_bytes=56 * 1024 * 1024,
        ),
    )(rows, target, live, values, own_t, *pieces)


def local(block_values, block_columns, row_counts, prolong_blocks, aggregates):
    panel_length = row_counts.shape[0]
    slots_here = block_values.shape[1]
    slot_total = panel_length * slots_here
    block_size = block_values.shape[2]
    group_size = lax.axis_size("grp")
    panel_total = lax.axis_size("blk")
    coarse_count = CB * panel_total
    me = lax.axis_index("blk")
    panel_blocks, panel_aggs = (
        lax.all_gather(prolong_blocks, "grp", axis=0, tiled=True),
        lax.all_gather(aggregates, "grp", axis=0, tiled=True),
    )
    lower = []
    upper = []
    going_down = (panel_blocks, panel_aggs)
    going_up = (panel_blocks, panel_aggs)
    for hop in range(2):
        going_down = passed_along((going_down[0], going_down[1]), "blk", 1)
        lower.insert(0, going_down)
        going_up = passed_along((going_up[0], going_up[1]), "blk", -1)
        upper.append(going_up)
    pieces = lower + [(panel_blocks, panel_aggs)] + upper
    window_aggs = jnp.concatenate([piece[1] for piece in pieces], axis=0)
    wanted = block_columns.reshape(slot_total)
    column_panel = wanted // panel_length
    distance = jnp.mod(column_panel - me + 2, panel_total)
    local_rows = distance * panel_length + wanted % panel_length
    fetched_aggs = jnp.take(window_aggs, local_rows, axis=0)
    slot_ids = lax.axis_index("grp") * slots_here + jnp.arange(slots_here, dtype=jnp.int32)
    live = (slot_ids[None, :] < row_counts[:, None]).astype(jnp.int32).reshape(slot_total)
    local_coarse = panel_aggs - me * CB
    target = fetched_aggs * CB + jnp.broadcast_to(
        local_coarse[:, None], (panel_length, slots_here)
    ).reshape(slot_total)
    own_t = jnp.swapaxes(panel_blocks, 1, 2)
    summed = coarse_partial(
        local_rows.astype(jnp.int32),
        target.astype(jnp.int32),
        live,
        block_values,
        own_t,
        [piece[0] for piece in pieces],
        coarse_count * CB,
    )
    return lax.psum_scatter(
        summed.reshape(coarse_count, CB, block_size, block_size),
        "grp",
        scatter_dimension=0,
        tiled=True,
    )


def solution(mesh):
    return jax.shard_map(
        local,
        mesh=mesh,
        in_specs=(
            P("blk", "grp", None, None),
            P("blk", "grp"),
            P("blk"),
            P(("blk", "grp"), None, None),
            P(("blk", "grp")),
        ),
        out_specs=P("grp", "blk", None, None),
        check_vma=False,
    )
```

```python
import functools

import jax
import jax.numpy as jnp
from jax import lax
from jax.experimental import pallas as pl
from jax.experimental.pallas import tpu as pltpu
from jax.sharding import PartitionSpec as P

CB = 4
ROWS_PER_STEP = 16


def passed_along(block, axis, distance):
    devices = range(lax.axis_size(axis))
    route = [((i - distance) % len(devices), i) for i in devices]
    return lax.ppermute(block, axis, route)


def coarse_kernel(rows_ref, target_ref, live_ref, values_ref, own_t_ref, *rest):
    pieces = rest[:5]
    acc_ref, window, sems = rest[5:]
    step = pl.program_id(0)
    rows_here, slots, bs, _ = values_ref.shape
    panel_length = pieces[0].shape[0]

    @pl.when(step == 0)
    def _():
        copies = []
        for k, piece in enumerate(pieces):
            cp = pltpu.make_async_copy(
                piece, window.at[pl.ds(k * panel_length, panel_length)], sems.at[k]
            )
            cp.start()
            copies.append(cp)
        for cp in copies:
            cp.wait()
        acc_ref[...] = jnp.zeros_like(acc_ref)

    def row_body(r, carry):
        row = step * rows_here + r
        own_t = own_t_ref[row]
        for s in range(slots):
            n = row * slots + s
            picked = window[rows_ref[n]]
            product = jnp.dot(
                values_ref[r, s], picked, preferred_element_type=jnp.float32
            )
            product = jnp.where(live_ref[n] > 0, product, 0.0).astype(jnp.bfloat16)
            restricted = jnp.dot(own_t, product, preferred_element_type=jnp.float32)
            t = target_ref[n]
            acc_ref[t] = acc_ref[t] + restricted
        return carry

    lax.fori_loop(0, rows_here, row_body, 0)


def coarse_partial(rows, target, live, values, own_t, pieces, n_targets):
    panel_length, slots, bs, _ = values.shape
    rows_per_step = min(ROWS_PER_STEP, panel_length)
    grid = (panel_length // rows_per_step,)
    window_rows = 5 * pieces[0].shape[0]
    return pl.pallas_call(
        coarse_kernel,
        out_shape=jax.ShapeDtypeStruct((n_targets, bs, bs), jnp.float32),
        grid_spec=pltpu.PrefetchScalarGridSpec(
            num_scalar_prefetch=3,
            grid=grid,
            in_specs=[
                pl.BlockSpec((rows_per_step, slots, bs, bs), lambda i, *_: (i, 0, 0, 0)),
                pl.BlockSpec(memory_space=pltpu.VMEM),
            ]
            + [pl.BlockSpec(memory_space=pl.ANY)] * 5,
            out_specs=pl.BlockSpec((n_targets, bs, bs), lambda i, *_: (0, 0, 0)),
            scratch_shapes=[
                pltpu.VMEM((window_rows, bs, bs), jnp.bfloat16),
                pltpu.SemaphoreType.DMA((5,)),
            ],
        ),
        compiler_params=pltpu.CompilerParams(
            dimension_semantics=("arbitrary",),
            vmem_limit_bytes=56 * 1024 * 1024,
        ),
    )(rows, target, live, values, own_t, *pieces)


def local(block_values, block_columns, row_counts, prolong_blocks, aggregates):
    panel_length = row_counts.shape[0]
    slots_here = block_values.shape[1]
    slot_total = panel_length * slots_here
    block_size = block_values.shape[2]
    group_size = lax.axis_size("grp")
    panel_total = lax.axis_size("blk")
    coarse_count = CB * panel_total
    me = lax.axis_index("blk")
    group_me = lax.axis_index("grp")
    received = [(prolong_blocks, aggregates)]
    for k in range(1, group_size):
        received.append(
            lax.ppermute(
                (prolong_blocks, aggregates),
                "grp",
                [(i, (i + k) % group_size) for i in range(group_size)],
            )
        )
    order = jnp.mod(group_me - jnp.arange(group_size, dtype=jnp.int32), group_size)
    panel_blocks = jnp.take(
        jnp.stack([piece[0] for piece in received]), order, axis=0
    ).reshape(panel_length, block_size, block_size)
    panel_aggs = jnp.take(
        jnp.stack([piece[1] for piece in received]), order, axis=0
    ).reshape(panel_length)
    lower = []
    upper = []
    going_down = (panel_blocks, panel_aggs)
    going_up = (panel_blocks, panel_aggs)
    for hop in range(2):
        going_down = passed_along((going_down[0], going_down[1]), "blk", 1)
        lower.insert(0, going_down)
        going_up = passed_along((going_up[0], going_up[1]), "blk", -1)
        upper.append(going_up)
    pieces = lower + [(panel_blocks, panel_aggs)] + upper
    window_aggs = jnp.concatenate([piece[1] for piece in pieces], axis=0)
    wanted = block_columns.reshape(slot_total)
    column_panel = wanted // panel_length
    distance = jnp.mod(column_panel - me + 2, panel_total)
    local_rows = distance * panel_length + wanted % panel_length
    fetched_aggs = jnp.take(window_aggs, local_rows, axis=0)
    slot_ids = lax.axis_index("grp") * slots_here + jnp.arange(slots_here, dtype=jnp.int32)
    live = (slot_ids[None, :] < row_counts[:, None]).astype(jnp.int32).reshape(slot_total)
    local_coarse = panel_aggs - me * CB
    target = fetched_aggs * CB + jnp.broadcast_to(
        local_coarse[:, None], (panel_length, slots_here)
    ).reshape(slot_total)
    own_t = jnp.swapaxes(panel_blocks, 1, 2)
    summed = coarse_partial(
        local_rows.astype(jnp.int32),
        target.astype(jnp.int32),
        live,
        block_values,
        own_t,
        [piece[0] for piece in pieces],
        coarse_count * CB,
    )
    share = coarse_count // group_size
    summed = summed.reshape(group_size, share, CB, block_size, block_size)
    total = jnp.take(summed, group_me, axis=0)
    for k in range(1, group_size):
        outgoing = jnp.take(summed, jnp.mod(group_me + k, group_size), axis=0)
        total = total + lax.ppermute(
            outgoing, "grp", [(i, (i + k) % group_size) for i in range(group_size)]
        )
    return total


def solution(mesh):
    return jax.shard_map(
        local,
        mesh=mesh,
        in_specs=(
            P("blk", "grp", None, None),
            P("blk", "grp"),
            P("blk"),
            P(("blk", "grp"), None, None),
            P(("blk", "grp")),
        ),
        out_specs=P("grp", "blk", None, None),
        check_vma=False,
    )
```

```python
import functools

import jax
import jax.numpy as jnp
from jax import lax
from jax.experimental import pallas as pl
from jax.experimental.pallas import tpu as pltpu
from jax.sharding import PartitionSpec as P

CB = 4
ROWS_PER_STEP = 16


def passed_along(block, axis, distance):
    devices = range(lax.axis_size(axis))
    route = [((i - distance) % len(devices), i) for i in devices]
    return lax.ppermute(block, axis, route)


def coarse_kernel(pair_ref, half_ref, target_ref, live_ref, values_ref, own_t_ref, *rest):
    pieces = rest[:5]
    out_ref, acc_ref, window, sems = rest[5:]
    step = pl.program_id(0)
    rows_here, slots, bs, _ = values_ref.shape
    piece_rows = pieces[0].shape[0]
    lanes = window.shape[2]

    @pl.when(step == 0)
    def _():
        copies = []
        for k, piece in enumerate(pieces):
            cp = pltpu.make_async_copy(
                piece, window.at[pl.ds(k * piece_rows, piece_rows)], sems.at[k]
            )
            cp.start()
            copies.append(cp)
        acc_ref[...] = jnp.zeros_like(acc_ref)
        for cp in copies:
            cp.wait()

    lane_half = lax.broadcasted_iota(jnp.int32, (bs, lanes), 1) // bs

    def row_body(r, carry):
        row = step * rows_here + r
        own_t = own_t_ref[row]
        results = []
        for s in range(slots):
            n = row * slots + s
            pair = window[pair_ref[n]]
            picked = jnp.where(lane_half == half_ref[n], pair, jnp.zeros_like(pair))
            product = jnp.dot(
                values_ref[r, s], picked, preferred_element_type=jnp.float32
            )
            product = jnp.where(live_ref[n] > 0, product, 0.0).astype(jnp.bfloat16)
            results.append(
                jnp.dot(own_t, product, preferred_element_type=jnp.float32)
            )
        for s in range(slots):
            t = target_ref[row * slots + s]
            acc_ref[t] = acc_ref[t] + results[s]
        return carry

    lax.fori_loop(0, rows_here, row_body, 0, unroll=2)

    @pl.when(step == pl.num_programs(0) - 1)
    def _():
        def pack(m, carry):
            first = acc_ref[2 * m]
            second = acc_ref[2 * m + 1]
            first = first + pltpu.roll(first, bs, 1)
            second = second + pltpu.roll(second, bs, 1)
            out_ref[m] = jnp.where(lane_half == 0, first, second)
            return carry

        lax.fori_loop(0, out_ref.shape[0], pack, 0)


def coarse_partial(pair, half, target, live, values, own_t, pieces, n_targets):
    panel_length, slots, bs, _ = values.shape
    rows_per_step = min(ROWS_PER_STEP, panel_length)
    grid = (panel_length // rows_per_step,)
    piece_rows, _, lanes = pieces[0].shape
    return pl.pallas_call(
        coarse_kernel,
        out_shape=jax.ShapeDtypeStruct((n_targets // 2, bs, lanes), jnp.float32),
        grid_spec=pltpu.PrefetchScalarGridSpec(
            num_scalar_prefetch=4,
            grid=grid,
            in_specs=[
                pl.BlockSpec((rows_per_step, slots, bs, bs), lambda i, *_: (i, 0, 0, 0)),
                pl.BlockSpec(memory_space=pltpu.VMEM),
            ]
            + [pl.BlockSpec(memory_space=pl.ANY)] * 5,
            out_specs=pl.BlockSpec((n_targets // 2, bs, lanes), lambda i, *_: (0, 0, 0)),
            scratch_shapes=[
                pltpu.VMEM((n_targets, bs, lanes), jnp.float32),
                pltpu.VMEM((5 * piece_rows, bs, lanes), jnp.bfloat16),
                pltpu.SemaphoreType.DMA((5,)),
            ],
        ),
        compiler_params=pltpu.CompilerParams(
            dimension_semantics=("arbitrary",),
            vmem_limit_bytes=60 * 1024 * 1024,
        ),
    )(pair, half, target, live, values, own_t, *pieces)


def local(block_values, block_columns, row_counts, prolong_blocks, aggregates):
    panel_length = row_counts.shape[0]
    slots_here = block_values.shape[1]
    slot_total = panel_length * slots_here
    block_size = block_values.shape[2]
    group_size = lax.axis_size("grp")
    panel_total = lax.axis_size("blk")
    coarse_count = CB * panel_total
    me = lax.axis_index("blk")
    group_me = lax.axis_index("grp")
    received = [(prolong_blocks, aggregates)]
    for k in range(1, group_size):
        received.append(
            lax.ppermute(
                (prolong_blocks, aggregates),
                "grp",
                [(i, (i + k) % group_size) for i in range(group_size)],
            )
        )
    order = jnp.mod(group_me - jnp.arange(group_size, dtype=jnp.int32), group_size)
    panel_blocks = jnp.take(
        jnp.stack([piece[0] for piece in received]), order, axis=0
    ).reshape(panel_length, block_size, block_size)
    panel_aggs = jnp.take(
        jnp.stack([piece[1] for piece in received]), order, axis=0
    ).reshape(panel_length)
    paired = (
        panel_blocks.reshape(panel_length // 2, 2, block_size, block_size)
        .transpose(0, 2, 1, 3)
        .reshape(panel_length // 2, block_size, 2 * block_size)
    )
    lower = []
    upper = []
    going_down = (paired, panel_aggs)
    going_up = (paired, panel_aggs)
    for hop in range(2):
        going_down = passed_along((going_down[0], going_down[1]), "blk", 1)
        lower.insert(0, going_down)
        going_up = passed_along((going_up[0], going_up[1]), "blk", -1)
        upper.append(going_up)
    pieces = lower + [(paired, panel_aggs)] + upper
    window_aggs = jnp.concatenate([piece[1] for piece in pieces], axis=0)
    wanted = block_columns.reshape(slot_total)
    column_panel = wanted // panel_length
    distance = jnp.mod(column_panel - me + 2, panel_total)
    local_rows = distance * panel_length + wanted % panel_length
    fetched_aggs = jnp.take(window_aggs, local_rows, axis=0)
    slot_ids = lax.axis_index("grp") * slots_here + jnp.arange(slots_here, dtype=jnp.int32)
    live = (slot_ids[None, :] < row_counts[:, None]).astype(jnp.int32).reshape(slot_total)
    local_coarse = panel_aggs - me * CB
    target = fetched_aggs * CB + jnp.broadcast_to(
        local_coarse[:, None], (panel_length, slots_here)
    ).reshape(slot_total)
    own_t = jnp.swapaxes(panel_blocks, 1, 2)
    summed = coarse_partial(
        (local_rows // 2).astype(jnp.int32),
        (local_rows % 2).astype(jnp.int32),
        target.astype(jnp.int32),
        live,
        block_values,
        own_t,
        [piece[0] for piece in pieces],
        coarse_count * CB,
    )
    share = coarse_count // group_size
    summed = summed.reshape(group_size, share, CB // 2, block_size, 2 * block_size)
    total = jnp.take(summed, group_me, axis=0)
    for k in range(1, group_size):
        outgoing = jnp.take(summed, jnp.mod(group_me + k, group_size), axis=0)
        total = total + lax.ppermute(
            outgoing, "grp", [(i, (i + k) % group_size) for i in range(group_size)]
        )
    total = total.reshape(share, CB // 2, block_size, 2, block_size)
    return total.transpose(0, 1, 3, 2, 4).reshape(share, CB, block_size, block_size)


def solution(mesh):
    return jax.shard_map(
        local,
        mesh=mesh,
        in_specs=(
            P("blk", "grp", None, None),
            P("blk", "grp"),
            P("blk"),
            P(("blk", "grp"), None, None),
            P(("blk", "grp")),
        ),
        out_specs=P("grp", "blk", None, None),
        check_vma=False,
    )
```

```python
import functools

import jax
import jax.numpy as jnp
from jax import lax
from jax.experimental import pallas as pl
from jax.experimental.pallas import tpu as pltpu
from jax.sharding import PartitionSpec as P

CB = 4
ROWS_PER_STEP = 16


def passed_along(block, axis, distance):
    devices = range(lax.axis_size(axis))
    route = [((i - distance) % len(devices), i) for i in devices]
    return lax.ppermute(block, axis, route)


def coarse_kernel(pair_ref, half_ref, target_ref, live_ref, own_pos_ref, values_ref, own_t_ref, *rest):
    pieces = rest[:5]
    out_ref, acc_ref, window, sems = rest[5:]
    step = pl.program_id(0)
    rows_here, slots, bs, _ = values_ref.shape
    piece_rows = pieces[0].shape[0]
    lanes = window.shape[2]

    @pl.when(step == 0)
    def _():
        copies = []
        for k, piece in enumerate(pieces):
            cp = pltpu.make_async_copy(
                piece, window.at[pl.ds(k * piece_rows, piece_rows)], sems.at[k]
            )
            cp.start()
            copies.append(cp)
        acc_ref[...] = jnp.zeros_like(acc_ref)
        for cp in copies:
            cp.wait()

    lane_half = lax.broadcasted_iota(jnp.int32, (bs, lanes), 1) // bs

    def row_body(r, carry):
        row = step * rows_here + r
        own_t = own_t_ref[own_pos_ref[row]]
        results = []
        for s in range(slots):
            n = row * slots + s
            pair = window[pair_ref[n]]
            picked = jnp.where(lane_half == half_ref[n], pair, jnp.zeros_like(pair))
            product = jnp.dot(
                values_ref[r, s], picked, preferred_element_type=jnp.float32
            )
            product = jnp.where(live_ref[n] > 0, product, 0.0).astype(jnp.bfloat16)
            results.append(
                jnp.dot(own_t, product, preferred_element_type=jnp.float32)
            )
        for s in range(slots):
            t = target_ref[row * slots + s]
            acc_ref[t] = acc_ref[t] + results[s]
        return carry

    lax.fori_loop(0, rows_here, row_body, 0, unroll=2)

    @pl.when(step == pl.num_programs(0) - 1)
    def _():
        def pack(m, carry):
            first = acc_ref[2 * m]
            second = acc_ref[2 * m + 1]
            first = first + pltpu.roll(first, bs, 1)
            second = second + pltpu.roll(second, bs, 1)
            out_ref[m] = jnp.where(lane_half == 0, first, second)
            return carry

        lax.fori_loop(0, out_ref.shape[0], pack, 0)


def coarse_partial(pair, half, target, live, own_pos, values, own_t, pieces, n_targets):
    panel_length, slots, bs, _ = values.shape
    rows_per_step = min(ROWS_PER_STEP, panel_length)
    grid = (panel_length // rows_per_step,)
    piece_rows, _, lanes = pieces[0].shape
    return pl.pallas_call(
        coarse_kernel,
        out_shape=jax.ShapeDtypeStruct((n_targets // 2, bs, lanes), jnp.float32),
        grid_spec=pltpu.PrefetchScalarGridSpec(
            num_scalar_prefetch=5,
            grid=grid,
            in_specs=[
                pl.BlockSpec((rows_per_step, slots, bs, bs), lambda i, *_: (i, 0, 0, 0)),
                pl.BlockSpec(memory_space=pltpu.VMEM),
            ]
            + [pl.BlockSpec(memory_space=pl.ANY)] * 5,
            out_specs=pl.BlockSpec((n_targets // 2, bs, lanes), lambda i, *_: (0, 0, 0)),
            scratch_shapes=[
                pltpu.VMEM((n_targets, bs, lanes), jnp.float32),
                pltpu.VMEM((5 * piece_rows, bs, lanes), jnp.bfloat16),
                pltpu.SemaphoreType.DMA((5,)),
            ],
        ),
        compiler_params=pltpu.CompilerParams(
            dimension_semantics=("arbitrary",),
            vmem_limit_bytes=60 * 1024 * 1024,
        ),
    )(pair, half, target, live, own_pos, values, own_t, *pieces)


def local(block_values, block_columns, row_counts, prolong_blocks, aggregates):
    panel_length = row_counts.shape[0]
    slots_here = block_values.shape[1]
    slot_total = panel_length * slots_here
    block_size = block_values.shape[2]
    group_size = lax.axis_size("grp")
    panel_total = lax.axis_size("blk")
    coarse_count = CB * panel_total
    me = lax.axis_index("blk")
    group_me = lax.axis_index("grp")
    share_rows = prolong_blocks.shape[0]
    local_pairs = (
        prolong_blocks.reshape(share_rows // 2, 2, block_size, block_size)
        .transpose(0, 2, 1, 3)
        .reshape(share_rows // 2, block_size, 2 * block_size)
    )
    received = [(local_pairs, aggregates)]
    for k in range(1, group_size):
        received.append(
            lax.ppermute(
                (local_pairs, aggregates),
                "grp",
                [(i, (i + k) % group_size) for i in range(group_size)],
            )
        )
    paired = jnp.concatenate([piece[0] for piece in received], axis=0)
    panel_aggs = jnp.concatenate([piece[1] for piece in received], axis=0)

    def rotated(r):
        return jnp.mod(group_me - r // share_rows, group_size) * share_rows + r % share_rows

    lower = []
    upper = []
    going_down = (paired, panel_aggs)
    going_up = (paired, panel_aggs)
    for hop in range(2):
        going_down = passed_along((going_down[0], going_down[1]), "blk", 1)
        lower.insert(0, going_down)
        going_up = passed_along((going_up[0], going_up[1]), "blk", -1)
        upper.append(going_up)
    pieces = lower + [(paired, panel_aggs)] + upper
    window_aggs = jnp.concatenate([piece[1] for piece in pieces], axis=0)
    wanted = block_columns.reshape(slot_total)
    column_panel = wanted // panel_length
    distance = jnp.mod(column_panel - me + 2, panel_total)
    local_rows = distance * panel_length + rotated(wanted % panel_length)
    own_pos = rotated(jnp.arange(panel_length, dtype=jnp.int32))
    fetched_aggs = jnp.take(window_aggs, local_rows, axis=0)
    slot_ids = lax.axis_index("grp") * slots_here + jnp.arange(slots_here, dtype=jnp.int32)
    live = (slot_ids[None, :] < row_counts[:, None]).astype(jnp.int32).reshape(slot_total)
    local_coarse = jnp.take(panel_aggs, own_pos, axis=0) - me * CB
    target = fetched_aggs * CB + jnp.broadcast_to(
        local_coarse[:, None], (panel_length, slots_here)
    ).reshape(slot_total)
    own_t = (
        paired.reshape(panel_length // 2, block_size, 2, block_size)
        .transpose(0, 2, 3, 1)
        .reshape(panel_length, block_size, block_size)
    )
    summed = coarse_partial(
        (local_rows // 2).astype(jnp.int32),
        (local_rows % 2).astype(jnp.int32),
        target.astype(jnp.int32),
        live,
        own_pos,
        block_values,
        own_t,
        [piece[0] for piece in pieces],
        coarse_count * CB,
    )
    share = coarse_count // group_size
    summed = summed.reshape(group_size, share, CB // 2, block_size, 2 * block_size)
    total = jnp.take(summed, group_me, axis=0)
    for k in range(1, group_size):
        outgoing = jnp.take(summed, jnp.mod(group_me + k, group_size), axis=0)
        total = total + lax.ppermute(
            outgoing, "grp", [(i, (i + k) % group_size) for i in range(group_size)]
        )
    total = total.reshape(share, CB // 2, block_size, 2, block_size)
    return total.transpose(0, 1, 3, 2, 4).reshape(share, CB, block_size, block_size)


def solution(mesh):
    return jax.shard_map(
        local,
        mesh=mesh,
        in_specs=(
            P("blk", "grp", None, None),
            P("blk", "grp"),
            P("blk"),
            P(("blk", "grp"), None, None),
            P(("blk", "grp")),
        ),
        out_specs=P("grp", "blk", None, None),
        check_vma=False,
    )
```

```python
import functools

import jax
import jax.numpy as jnp
from jax import lax
from jax.experimental import pallas as pl
from jax.experimental.pallas import tpu as pltpu
from jax.sharding import PartitionSpec as P

CB = 4
ROWS_PER_STEP = 16


def passed_along(block, axis, distance):
    devices = range(lax.axis_size(axis))
    route = [((i - distance) % len(devices), i) for i in devices]
    return lax.ppermute(block, axis, route)


def coarse_kernel(pair_ref, half_ref, target_ref, live_ref, own_pos_ref, values_ref, *rest):
    pieces = rest[:5]
    out_ref, acc_ref, window, sems = rest[5:]
    step = pl.program_id(0)
    rows_here, slots, bs, _ = values_ref.shape
    piece_rows = pieces[0].shape[0]
    lanes = window.shape[2]

    @pl.when(step == 0)
    def _():
        copies = []
        for k, piece in enumerate(pieces):
            cp = pltpu.make_async_copy(
                piece, window.at[pl.ds(k * piece_rows, piece_rows)], sems.at[k]
            )
            cp.start()
            copies.append(cp)
        acc_ref[...] = jnp.zeros_like(acc_ref)
        for cp in copies:
            cp.wait()

    lane_half = lax.broadcasted_iota(jnp.int32, (bs, lanes), 1) // bs

    def row_body(r, carry):
        row = step * rows_here + r
        own_pair = window[2 * piece_rows + own_pos_ref[row] // 2].astype(jnp.float32)
        spread = jnp.concatenate([own_pair, jnp.zeros_like(own_pair)], axis=0).T
        own_t = jnp.where(row % 2 == 0, spread[:bs], spread[bs:])[:, :bs]
        own_t = own_t.astype(jnp.bfloat16)
        results = []
        for s in range(slots):
            n = row * slots + s
            pair = window[pair_ref[n]]
            picked = jnp.where(lane_half == half_ref[n], pair, jnp.zeros_like(pair))
            product = jnp.dot(
                values_ref[r, s], picked, preferred_element_type=jnp.float32
            )
            product = jnp.where(live_ref[n] > 0, product, 0.0).astype(jnp.bfloat16)
            results.append(
                jnp.dot(own_t, product, preferred_element_type=jnp.float32)
            )
        for s in range(slots):
            t = target_ref[row * slots + s]
            acc_ref[t] = acc_ref[t] + results[s]
        return carry

    lax.fori_loop(0, rows_here, row_body, 0, unroll=2)

    @pl.when(step == pl.num_programs(0) - 1)
    def _():
        def pack(m, carry):
            first = acc_ref[2 * m]
            second = acc_ref[2 * m + 1]
            first = first + pltpu.roll(first, bs, 1)
            second = second + pltpu.roll(second, bs, 1)
            out_ref[m] = jnp.where(lane_half == 0, first, second)
            return carry

        lax.fori_loop(0, out_ref.shape[0], pack, 0)


def coarse_partial(pair, half, target, live, own_pos, values, pieces, n_targets):
    panel_length, slots, bs, _ = values.shape
    rows_per_step = min(ROWS_PER_STEP, panel_length)
    grid = (panel_length // rows_per_step,)
    piece_rows, _, lanes = pieces[0].shape
    return pl.pallas_call(
        coarse_kernel,
        out_shape=jax.ShapeDtypeStruct((n_targets // 2, bs, lanes), jnp.float32),
        grid_spec=pltpu.PrefetchScalarGridSpec(
            num_scalar_prefetch=5,
            grid=grid,
            in_specs=[
                pl.BlockSpec((rows_per_step, slots, bs, bs), lambda i, *_: (i, 0, 0, 0)),
            ]
            + [pl.BlockSpec(memory_space=pl.ANY)] * 5,
            out_specs=pl.BlockSpec((n_targets // 2, bs, lanes), lambda i, *_: (0, 0, 0)),
            scratch_shapes=[
                pltpu.VMEM((n_targets, bs, lanes), jnp.float32),
                pltpu.VMEM((5 * piece_rows, bs, lanes), jnp.bfloat16),
                pltpu.SemaphoreType.DMA((5,)),
            ],
        ),
        compiler_params=pltpu.CompilerParams(
            dimension_semantics=("arbitrary",),
            vmem_limit_bytes=60 * 1024 * 1024,
        ),
    )(pair, half, target, live, own_pos, values, *pieces)


def local(block_values, block_columns, row_counts, prolong_blocks, aggregates):
    panel_length = row_counts.shape[0]
    slots_here = block_values.shape[1]
    slot_total = panel_length * slots_here
    block_size = block_values.shape[2]
    group_size = lax.axis_size("grp")
    panel_total = lax.axis_size("blk")
    coarse_count = CB * panel_total
    me = lax.axis_index("blk")
    group_me = lax.axis_index("grp")
    share_rows = prolong_blocks.shape[0]
    local_pairs = (
        prolong_blocks.reshape(share_rows // 2, 2, block_size, block_size)
        .transpose(0, 2, 1, 3)
        .reshape(share_rows // 2, block_size, 2 * block_size)
    )
    received = [(local_pairs, aggregates)]
    for k in range(1, group_size):
        received.append(
            lax.ppermute(
                (local_pairs, aggregates),
                "grp",
                [(i, (i + k) % group_size) for i in range(group_size)],
            )
        )
    paired = jnp.concatenate([piece[0] for piece in received], axis=0)
    panel_aggs = jnp.concatenate([piece[1] for piece in received], axis=0)

    def rotated(r):
        return jnp.mod(group_me - r // share_rows, group_size) * share_rows + r % share_rows

    lower = []
    upper = []
    going_down = (paired, panel_aggs)
    going_up = (paired, panel_aggs)
    for hop in range(2):
        going_down = passed_along((going_down[0], going_down[1]), "blk", 1)
        lower.insert(0, going_down)
        going_up = passed_along((going_up[0], going_up[1]), "blk", -1)
        upper.append(going_up)
    pieces = lower + [(paired, panel_aggs)] + upper
    window_aggs = jnp.concatenate([piece[1] for piece in pieces], axis=0)
    wanted = block_columns.reshape(slot_total)
    column_panel = wanted // panel_length
    distance = jnp.mod(column_panel - me + 2, panel_total)
    local_rows = distance * panel_length + rotated(wanted % panel_length)
    own_pos = rotated(jnp.arange(panel_length, dtype=jnp.int32))
    fetched_aggs = jnp.take(window_aggs, local_rows, axis=0)
    slot_ids = lax.axis_index("grp") * slots_here + jnp.arange(slots_here, dtype=jnp.int32)
    live = (slot_ids[None, :] < row_counts[:, None]).astype(jnp.int32).reshape(slot_total)
    local_coarse = jnp.take(panel_aggs, own_pos, axis=0) - me * CB
    target = fetched_aggs * CB + jnp.broadcast_to(
        local_coarse[:, None], (panel_length, slots_here)
    ).reshape(slot_total)
    summed = coarse_partial(
        (local_rows // 2).astype(jnp.int32),
        (local_rows % 2).astype(jnp.int32),
        target.astype(jnp.int32),
        live,
        own_pos,
        block_values,
        [piece[0] for piece in pieces],
        coarse_count * CB,
    )
    share = coarse_count // group_size
    summed = summed.reshape(group_size, share, CB // 2, block_size, 2 * block_size)
    total = jnp.take(summed, group_me, axis=0)
    for k in range(1, group_size):
        outgoing = jnp.take(summed, jnp.mod(group_me + k, group_size), axis=0)
        total = total + lax.ppermute(
            outgoing, "grp", [(i, (i + k) % group_size) for i in range(group_size)]
        )
    total = total.reshape(share, CB // 2, block_size, 2, block_size)
    return total.transpose(0, 1, 3, 2, 4).reshape(share, CB, block_size, block_size)


def solution(mesh):
    return jax.shard_map(
        local,
        mesh=mesh,
        in_specs=(
            P("blk", "grp", None, None),
            P("blk", "grp"),
            P("blk"),
            P(("blk", "grp"), None, None),
            P(("blk", "grp")),
        ),
        out_specs=P("grp", "blk", None, None),
        check_vma=False,
    )
```

```python
import functools

import jax
import jax.numpy as jnp
from jax import lax
from jax.experimental import pallas as pl
from jax.experimental.pallas import tpu as pltpu
from jax.sharding import PartitionSpec as P

CB = 4
ROWS_PER_STEP = 16


def passed_along(block, axis, distance):
    devices = range(lax.axis_size(axis))
    route = [((i - distance) % len(devices), i) for i in devices]
    return lax.ppermute(block, axis, route)


def coarse_kernel(pair_ref, half_ref, target_ref, live_ref, own_pos_ref, values_ref, *rest):
    pieces = rest[:-4]
    out_ref, acc_ref, window, sems = rest[-4:]
    step = pl.program_id(0)
    rows_here, slots, bs, _ = values_ref.shape
    piece_rows = pieces[0].shape[0]
    lanes = window.shape[2]

    @pl.when(step == 0)
    def _():
        copies = []
        for k, piece in enumerate(pieces):
            cp = pltpu.make_async_copy(
                piece, window.at[pl.ds(k * piece_rows, piece_rows)], sems.at[k]
            )
            cp.start()
            copies.append(cp)
        acc_ref[...] = jnp.zeros_like(acc_ref)
        for cp in copies:
            cp.wait()

    lane_half = lax.broadcasted_iota(jnp.int32, (bs, lanes), 1) // bs

    def row_body(r, carry):
        row = step * rows_here + r
        own_pair = window[own_pos_ref[row]].astype(jnp.float32)
        spread = jnp.concatenate([own_pair, jnp.zeros_like(own_pair)], axis=0).T
        own_t = jnp.where(row % 2 == 0, spread[:bs], spread[bs:])[:, :bs]
        own_t = own_t.astype(jnp.bfloat16)
        results = []
        for s in range(slots):
            n = row * slots + s
            pair = window[pair_ref[n]]
            picked = jnp.where(lane_half == half_ref[n], pair, jnp.zeros_like(pair))
            product = jnp.dot(
                values_ref[r, s], picked, preferred_element_type=jnp.float32
            )
            product = jnp.where(live_ref[n] > 0, product, 0.0).astype(jnp.bfloat16)
            results.append(
                jnp.dot(own_t, product, preferred_element_type=jnp.float32)
            )
        for s in range(slots):
            t = target_ref[row * slots + s]
            acc_ref[t] = acc_ref[t] + results[s]
        return carry

    lax.fori_loop(0, rows_here, row_body, 0, unroll=2)

    @pl.when(step == pl.num_programs(0) - 1)
    def _():
        def pack(m, carry):
            first = acc_ref[2 * m]
            second = acc_ref[2 * m + 1]
            first = first + pltpu.roll(first, bs, 1)
            second = second + pltpu.roll(second, bs, 1)
            out_ref[m] = jnp.where(lane_half == 0, first, second)
            return carry

        lax.fori_loop(0, out_ref.shape[0], pack, 0)


def coarse_partial(pair, half, target, live, own_pos, values, pieces, n_targets):
    panel_length, slots, bs, _ = values.shape
    rows_per_step = min(ROWS_PER_STEP, panel_length)
    grid = (panel_length // rows_per_step,)
    piece_rows, _, lanes = pieces[0].shape
    return pl.pallas_call(
        coarse_kernel,
        out_shape=jax.ShapeDtypeStruct((n_targets // 2, bs, lanes), jnp.float32),
        grid_spec=pltpu.PrefetchScalarGridSpec(
            num_scalar_prefetch=5,
            grid=grid,
            in_specs=[
                pl.BlockSpec((rows_per_step, slots, bs, bs), lambda i, *_: (i, 0, 0, 0)),
            ]
            + [pl.BlockSpec(memory_space=pl.ANY)] * len(pieces),
            out_specs=pl.BlockSpec((n_targets // 2, bs, lanes), lambda i, *_: (0, 0, 0)),
            scratch_shapes=[
                pltpu.VMEM((n_targets, bs, lanes), jnp.float32),
                pltpu.VMEM((len(pieces) * piece_rows, bs, lanes), jnp.bfloat16),
                pltpu.SemaphoreType.DMA((len(pieces),)),
            ],
        ),
        compiler_params=pltpu.CompilerParams(
            dimension_semantics=("arbitrary",),
            vmem_limit_bytes=60 * 1024 * 1024,
        ),
    )(pair, half, target, live, own_pos, values, *pieces)


def local(block_values, block_columns, row_counts, prolong_blocks, aggregates):
    panel_length = row_counts.shape[0]
    slots_here = block_values.shape[1]
    slot_total = panel_length * slots_here
    block_size = block_values.shape[2]
    group_size = lax.axis_size("grp")
    panel_total = lax.axis_size("blk")
    coarse_count = CB * panel_total
    me = lax.axis_index("blk")
    group_me = lax.axis_index("grp")
    share_rows = prolong_blocks.shape[0]
    local_pairs = (
        prolong_blocks.reshape(share_rows // 2, 2, block_size, block_size)
        .transpose(0, 2, 1, 3)
        .reshape(share_rows // 2, block_size, 2 * block_size)
    )
    agg_row = (
        jnp.zeros((1, block_size, 2 * block_size), jnp.bfloat16)
        .at[0, 0, :share_rows]
        .set(aggregates.astype(jnp.bfloat16))
    )
    local_ext = jnp.concatenate([local_pairs, agg_row], axis=0)
    piece_rows = local_ext.shape[0]
    received = [local_ext]
    for k in range(1, group_size):
        received.append(
            lax.ppermute(
                local_ext, "grp", [(i, (i + k) % group_size) for i in range(group_size)]
            )
        )
    down1 = [passed_along(piece, "blk", 1) for piece in received]
    up1 = [passed_along(piece, "blk", -1) for piece in received]
    down2 = [passed_along(piece, "blk", 1) for piece in down1]
    up2 = [passed_along(piece, "blk", -1) for piece in up1]
    pieces = down2 + down1 + received + up1 + up2
    flat_aggs = jnp.stack([piece[share_rows // 2, 0, :share_rows] for piece in pieces])
    flat_aggs = flat_aggs.astype(jnp.int32).reshape(-1)

    def placed(d, r):
        k = jnp.mod(group_me - r // share_rows, group_size)
        return d * group_size + k, r % share_rows

    wanted = block_columns.reshape(slot_total)
    column_panel = wanted // panel_length
    distance = jnp.mod(column_panel - me + 2, panel_total)
    piece_of, within = placed(distance, wanted % panel_length)
    window_pair = piece_of * piece_rows + within // 2
    fetched_aggs = jnp.take(flat_aggs, piece_of * share_rows + within, axis=0)
    own_piece, own_within = placed(2, jnp.arange(panel_length, dtype=jnp.int32))
    own_pos = own_piece * piece_rows + own_within // 2
    own_aggs = jnp.take(flat_aggs, own_piece * share_rows + own_within, axis=0)
    slot_ids = lax.axis_index("grp") * slots_here + jnp.arange(slots_here, dtype=jnp.int32)
    live = (slot_ids[None, :] < row_counts[:, None]).astype(jnp.int32).reshape(slot_total)
    local_coarse = own_aggs - me * CB
    target = fetched_aggs * CB + jnp.broadcast_to(
        local_coarse[:, None], (panel_length, slots_here)
    ).reshape(slot_total)
    summed = coarse_partial(
        window_pair.astype(jnp.int32),
        (within % 2).astype(jnp.int32),
        target.astype(jnp.int32),
        live,
        own_pos,
        block_values,
        pieces,
        coarse_count * CB,
    )
    share = coarse_count // group_size
    summed = summed.reshape(group_size, share, CB // 2, block_size, 2 * block_size)
    total = jnp.take(summed, group_me, axis=0)
    for k in range(1, group_size):
        outgoing = jnp.take(summed, jnp.mod(group_me + k, group_size), axis=0)
        total = total + lax.ppermute(
            outgoing, "grp", [(i, (i + k) % group_size) for i in range(group_size)]
        )
    total = total.reshape(share, CB // 2, block_size, 2, block_size)
    return total.transpose(0, 1, 3, 2, 4).reshape(share, CB, block_size, block_size)


def solution(mesh):
    return jax.shard_map(
        local,
        mesh=mesh,
        in_specs=(
            P("blk", "grp", None, None),
            P("blk", "grp"),
            P("blk"),
            P(("blk", "grp"), None, None),
            P(("blk", "grp")),
        ),
        out_specs=P("grp", "blk", None, None),
        check_vma=False,
    )
```

```python
import functools

import jax
import jax.numpy as jnp
from jax import lax
from jax.experimental import pallas as pl
from jax.experimental.pallas import tpu as pltpu
from jax.sharding import PartitionSpec as P

CB = 4
ROWS_PER_STEP = 16


def passed_along(block, axis, distance):
    devices = range(lax.axis_size(axis))
    route = [((i - distance) % len(devices), i) for i in devices]
    return lax.ppermute(block, axis, route)


def coarse_kernel(
    pair_ref, half_ref, target_ref, live_ref, own_pos_ref, fix_ref, values_ref, *rest
):
    out_ref, acc_ref, window, sems = rest[-4:]
    n_pieces = sems.shape[0]
    groups = n_pieces // 5
    pieces = rest[:n_pieces]
    fixed = rest[n_pieces:-4]
    step = pl.program_id(0)
    rows_here, slots, bs, _ = values_ref.shape
    piece_rows = pieces[0].shape[0]
    lanes = window.shape[2]

    @pl.when(step == 0)
    def _():
        copies = []
        for j, piece in enumerate(pieces):
            dst = window.at[pl.ds(j * piece_rows, piece_rows)]
            cp = pltpu.make_async_copy(piece, dst, sems.at[j])
            d, k = divmod(j, groups)
            if k == 0:
                cp.start()
            else:
                flag = fix_ref[d]

                @pl.when(flag < 0)
                def _():
                    cp.start()

                for slot in range(2):
                    @pl.when(flag == slot)
                    def _():
                        pltpu.make_async_copy(
                            fixed[k - 1].at[slot], dst, sems.at[j]
                        ).start()

            copies.append(cp)
        acc_ref[...] = jnp.zeros_like(acc_ref)
        for cp in copies:
            cp.wait()

    lane_half = lax.broadcasted_iota(jnp.int32, (bs, lanes), 1) // bs

    def row_body(r, carry):
        row = step * rows_here + r
        own_pair = window[own_pos_ref[row]].astype(jnp.float32)
        spread = jnp.concatenate([own_pair, jnp.zeros_like(own_pair)], axis=0).T
        own_t = jnp.where(row % 2 == 0, spread[:bs], spread[bs:])[:, :bs]
        own_t = own_t.astype(jnp.bfloat16)
        results = []
        for s in range(slots):
            n = row * slots + s
            pair = window[pair_ref[n]]
            picked = jnp.where(lane_half == half_ref[n], pair, jnp.zeros_like(pair))
            product = jnp.dot(
                values_ref[r, s], picked, preferred_element_type=jnp.float32
            )
            product = jnp.where(live_ref[n] > 0, product, 0.0).astype(jnp.bfloat16)
            results.append(
                jnp.dot(own_t, product, preferred_element_type=jnp.float32)
            )
        for s in range(slots):
            t = target_ref[row * slots + s]
            acc_ref[t] = acc_ref[t] + results[s]
        return carry

    lax.fori_loop(0, rows_here, row_body, 0, unroll=2)

    @pl.when(step == pl.num_programs(0) - 1)
    def _():
        def pack(m, carry):
            first = acc_ref[2 * m]
            second = acc_ref[2 * m + 1]
            first = first + pltpu.roll(first, bs, 1)
            second = second + pltpu.roll(second, bs, 1)
            out_ref[m] = jnp.where(lane_half == 0, first, second)
            return carry

        lax.fori_loop(0, out_ref.shape[0], pack, 0)


def coarse_partial(pair, half, target, live, own_pos, fix, values, pieces, fixed, n_targets):
    panel_length, slots, bs, _ = values.shape
    rows_per_step = min(ROWS_PER_STEP, panel_length)
    grid = (panel_length // rows_per_step,)
    piece_rows, _, lanes = pieces[0].shape
    return pl.pallas_call(
        coarse_kernel,
        out_shape=jax.ShapeDtypeStruct((n_targets // 2, bs, lanes), jnp.float32),
        grid_spec=pltpu.PrefetchScalarGridSpec(
            num_scalar_prefetch=6,
            grid=grid,
            in_specs=[
                pl.BlockSpec((rows_per_step, slots, bs, bs), lambda i, *_: (i, 0, 0, 0)),
            ]
            + [pl.BlockSpec(memory_space=pl.ANY)] * (len(pieces) + len(fixed)),
            out_specs=pl.BlockSpec((n_targets // 2, bs, lanes), lambda i, *_: (0, 0, 0)),
            scratch_shapes=[
                pltpu.VMEM((n_targets, bs, lanes), jnp.float32),
                pltpu.VMEM((len(pieces) * piece_rows, bs, lanes), jnp.bfloat16),
                pltpu.SemaphoreType.DMA((len(pieces),)),
            ],
        ),
        compiler_params=pltpu.CompilerParams(
            dimension_semantics=("arbitrary",),
            vmem_limit_bytes=60 * 1024 * 1024,
        ),
    )(pair, half, target, live, own_pos, fix, values, *pieces, *fixed)


def local(block_values, block_columns, row_counts, prolong_blocks, aggregates):
    panel_length = row_counts.shape[0]
    slots_here = block_values.shape[1]
    slot_total = panel_length * slots_here
    block_size = block_values.shape[2]
    group_size = lax.axis_size("grp")
    panel_total = lax.axis_size("blk")
    coarse_count = CB * panel_total
    me = lax.axis_index("blk")
    group_me = lax.axis_index("grp")
    share_rows = prolong_blocks.shape[0]
    local_pairs = (
        prolong_blocks.reshape(share_rows // 2, 2, block_size, block_size)
        .transpose(0, 2, 1, 3)
        .reshape(share_rows // 2, block_size, 2 * block_size)
    )
    agg_row = (
        jnp.zeros((1, block_size, 2 * block_size), jnp.bfloat16)
        .at[0, 0, :share_rows]
        .set(aggregates.astype(jnp.bfloat16))
    )
    local_ext = jnp.concatenate([local_pairs, agg_row], axis=0)
    piece_rows = local_ext.shape[0]
    received = [local_ext]
    for k in range(1, group_size):
        received.append(
            lax.ppermute(
                local_ext, "grp", [(i, (i + k) % group_size) for i in range(group_size)]
            )
        )
    n = panel_total
    down_skip = ({(n - 1, 0)}, {(n - 1, 0), (0, 1)})
    up_skip = ({(0, n - 1)}, {(0, n - 1), (n - 1, n - 2)})

    def ring(piece, step, hop, full):
        skip = set() if full else (down_skip if step == 1 else up_skip)[hop]
        route = [((i - step) % n, i) for i in range(n)]
        route = [pair for pair in route if pair not in skip]
        return lax.ppermute(piece, "blk", route)

    down1 = [ring(piece, 1, 0, k == 0) for k, piece in enumerate(received)]
    up1 = [ring(piece, -1, 0, k == 0) for k, piece in enumerate(received)]
    down2 = [ring(piece, 1, 1, k == 0) for k, piece in enumerate(down1)]
    up2 = [ring(piece, -1, 1, k == 0) for k, piece in enumerate(up1)]
    pieces = down2 + down1 + received + up1 + up2
    low_end = me <= 1
    fix_first = jnp.where(low_end, down2[0], up2[0])
    fix_second = jnp.where(me == 0, down1[0], up1[0])
    fix_src = jnp.stack([fix_first, fix_second])
    ends = [0, 1, n - 2, n - 1]
    fixed = []
    for k in range(1, group_size):
        route = [
            (b * group_size + g, b * group_size + (g + k) % group_size)
            for b in ends
            for g in range(group_size)
        ]
        fixed.append(lax.ppermute(fix_src, ("blk", "grp"), route))
    minus = jnp.int32(-1)
    fix = jnp.stack([
        jnp.where(low_end, 0, minus),
        jnp.where(me == 0, 1, minus),
        minus,
        jnp.where(me == n - 1, 1, minus),
        jnp.where(me >= n - 2, 0, minus),
    ]).astype(jnp.int32)
    agg_rows = []
    for d in range(5):
        for k in range(group_size):
            row = pieces[d * group_size + k][share_rows // 2, 0, :share_rows]
            if k > 0:
                row = jnp.where(
                    fix[d] >= 0,
                    jnp.where(
                        fix[d] == 0,
                        fixed[k - 1][0, share_rows // 2, 0, :share_rows],
                        fixed[k - 1][1, share_rows // 2, 0, :share_rows],
                    ),
                    row,
                )
            agg_rows.append(row)
    flat_aggs = jnp.stack(agg_rows).astype(jnp.int32).reshape(-1)

    def placed(d, r):
        k = jnp.mod(group_me - r // share_rows, group_size)
        return d * group_size + k, r % share_rows

    wanted = block_columns.reshape(slot_total)
    column_panel = wanted // panel_length
    distance = jnp.mod(column_panel - me + 2, panel_total)
    piece_of, within = placed(distance, wanted % panel_length)
    window_pair = piece_of * piece_rows + within // 2
    fetched_aggs = jnp.take(flat_aggs, piece_of * share_rows + within, axis=0)
    own_piece, own_within = placed(2, jnp.arange(panel_length, dtype=jnp.int32))
    own_pos = own_piece * piece_rows + own_within // 2
    own_aggs = jnp.take(flat_aggs, own_piece * share_rows + own_within, axis=0)
    slot_ids = lax.axis_index("grp") * slots_here + jnp.arange(slots_here, dtype=jnp.int32)
    live = (slot_ids[None, :] < row_counts[:, None]).astype(jnp.int32).reshape(slot_total)
    local_coarse = own_aggs - me * CB
    target = fetched_aggs * CB + jnp.broadcast_to(
        local_coarse[:, None], (panel_length, slots_here)
    ).reshape(slot_total)
    summed = coarse_partial(
        window_pair.astype(jnp.int32),
        (within % 2).astype(jnp.int32),
        target.astype(jnp.int32),
        live,
        own_pos,
        fix,
        block_values,
        pieces,
        fixed,
        coarse_count * CB,
    )
    share = coarse_count // group_size
    summed = summed.reshape(group_size, share, CB // 2, block_size, 2 * block_size)
    total = jnp.take(summed, group_me, axis=0)
    for k in range(1, group_size):
        outgoing = jnp.take(summed, jnp.mod(group_me + k, group_size), axis=0)
        total = total + lax.ppermute(
            outgoing, "grp", [(i, (i + k) % group_size) for i in range(group_size)]
        )
    total = total.reshape(share, CB // 2, block_size, 2, block_size)
    return total.transpose(0, 1, 3, 2, 4).reshape(share, CB, block_size, block_size)


def solution(mesh):
    return jax.shard_map(
        local,
        mesh=mesh,
        in_specs=(
            P("blk", "grp", None, None),
            P("blk", "grp"),
            P("blk"),
            P(("blk", "grp"), None, None),
            P(("blk", "grp")),
        ),
        out_specs=P("grp", "blk", None, None),
        check_vma=False,
    )
```

```python
import functools

import jax
import jax.numpy as jnp
from jax import lax
from jax.experimental import pallas as pl
from jax.experimental.pallas import tpu as pltpu
from jax.sharding import PartitionSpec as P

CB = 4
ROWS_PER_STEP = 16


def passed_along(block, axis, distance):
    devices = range(lax.axis_size(axis))
    route = [((i - distance) % len(devices), i) for i in devices]
    return lax.ppermute(block, axis, route)


def coarse_kernel(
    pair_ref, half_ref, target_ref, live_ref, own_pos_ref, fix_ref, values_ref, *rest
):
    out_ref, acc_ref, window, sems = rest[-4:]
    n_pieces = sems.shape[0]
    groups = n_pieces // 5
    pieces = rest[:n_pieces]
    fixed = rest[n_pieces:-4]
    step = pl.program_id(0)
    rows_here, slots, bs, _ = values_ref.shape
    piece_rows = pieces[0].shape[0]
    lanes = window.shape[2]

    @pl.when(step == 0)
    def _():
        copies = []
        for j, piece in enumerate(pieces):
            dst = window.at[pl.ds(j * piece_rows, piece_rows)]
            cp = pltpu.make_async_copy(piece, dst, sems.at[j])
            d, k = divmod(j, groups)
            if k == 0:
                cp.start()
            else:
                flag = fix_ref[d]

                @pl.when(flag < 0)
                def _():
                    cp.start()

                for slot in range(2):
                    @pl.when(flag == slot)
                    def _():
                        pltpu.make_async_copy(
                            fixed[k - 1].at[slot], dst, sems.at[j]
                        ).start()

            copies.append(cp)
        acc_ref[...] = jnp.zeros_like(acc_ref)
        for cp in copies:
            cp.wait()

    lane_half = lax.broadcasted_iota(jnp.int32, (bs, lanes), 1) // bs

    def row_body(r, carry):
        row = step * rows_here + r
        own_pair = window[own_pos_ref[row]].astype(jnp.float32)
        spread = jnp.concatenate([own_pair, jnp.zeros_like(own_pair)], axis=0).T
        own_t = jnp.where(row % 2 == 0, spread[:bs], spread[bs:])[:, :bs]
        own_t = own_t.astype(jnp.bfloat16)
        base = row * slots
        lhs = values_ref[r].reshape(slots * bs, bs)
        left_lane = lane_half == 0
        columns = []
        for j in range(slots // 2):
            placed = []
            for side in range(2):
                n = base + 2 * j + side
                pair = window[pair_ref[n]].astype(jnp.float32)
                swapped = pltpu.roll(pair, bs, 1)
                placed.append(jnp.where(half_ref[n] == side, pair, swapped))
            columns.append(jnp.where(left_lane, placed[0], placed[1]))
        weights = jnp.concatenate(columns, axis=1).astype(jnp.bfloat16)
        out = jnp.dot(lhs, weights, preferred_element_type=jnp.float32)
        diagonal = []
        for j in range(slots // 2):
            lanes_j = slice(2 * bs * j, 2 * bs * (j + 1))
            top = out[2 * bs * j : 2 * bs * j + bs, lanes_j]
            bottom = out[2 * bs * j + bs : 2 * bs * (j + 1), lanes_j]
            top = jnp.where(live_ref[base + 2 * j] > 0, top, 0.0)
            bottom = jnp.where(live_ref[base + 2 * j + 1] > 0, bottom, 0.0)
            diagonal.append(jnp.where(left_lane, top, bottom))
        product = jnp.concatenate(diagonal, axis=1).astype(jnp.bfloat16)
        restricted = jnp.dot(own_t, product, preferred_element_type=jnp.float32)
        for k in range(slots):
            j, side = divmod(k, 2)
            part = restricted[:, 2 * bs * j : 2 * bs * (j + 1)]
            t = target_ref[base + k]
            acc_ref[t] = acc_ref[t] + jnp.where(lane_half == side, part, 0.0)
        return carry

    lax.fori_loop(0, rows_here, row_body, 0, unroll=2)

    @pl.when(step == pl.num_programs(0) - 1)
    def _():
        def pack(m, carry):
            first = acc_ref[2 * m]
            second = acc_ref[2 * m + 1]
            first = first + pltpu.roll(first, bs, 1)
            second = second + pltpu.roll(second, bs, 1)
            out_ref[m] = jnp.where(lane_half == 0, first, second)
            return carry

        lax.fori_loop(0, out_ref.shape[0], pack, 0)


def coarse_partial(pair, half, target, live, own_pos, fix, values, pieces, fixed, n_targets):
    panel_length, slots, bs, _ = values.shape
    rows_per_step = min(ROWS_PER_STEP, panel_length)
    grid = (panel_length // rows_per_step,)
    piece_rows, _, lanes = pieces[0].shape
    return pl.pallas_call(
        coarse_kernel,
        out_shape=jax.ShapeDtypeStruct((n_targets // 2, bs, lanes), jnp.float32),
        grid_spec=pltpu.PrefetchScalarGridSpec(
            num_scalar_prefetch=6,
            grid=grid,
            in_specs=[
                pl.BlockSpec((rows_per_step, slots, bs, bs), lambda i, *_: (i, 0, 0, 0)),
            ]
            + [pl.BlockSpec(memory_space=pl.ANY)] * (len(pieces) + len(fixed)),
            out_specs=pl.BlockSpec((n_targets // 2, bs, lanes), lambda i, *_: (0, 0, 0)),
            scratch_shapes=[
                pltpu.VMEM((n_targets, bs, lanes), jnp.float32),
                pltpu.VMEM((len(pieces) * piece_rows, bs, lanes), jnp.bfloat16),
                pltpu.SemaphoreType.DMA((len(pieces),)),
            ],
        ),
        compiler_params=pltpu.CompilerParams(
            dimension_semantics=("arbitrary",),
            vmem_limit_bytes=60 * 1024 * 1024,
        ),
    )(pair, half, target, live, own_pos, fix, values, *pieces, *fixed)


def local(block_values, block_columns, row_counts, prolong_blocks, aggregates):
    panel_length = row_counts.shape[0]
    slots_here = block_values.shape[1]
    slot_total = panel_length * slots_here
    block_size = block_values.shape[2]
    group_size = lax.axis_size("grp")
    panel_total = lax.axis_size("blk")
    coarse_count = CB * panel_total
    me = lax.axis_index("blk")
    group_me = lax.axis_index("grp")
    share_rows = prolong_blocks.shape[0]
    local_pairs = (
        prolong_blocks.reshape(share_rows // 2, 2, block_size, block_size)
        .transpose(0, 2, 1, 3)
        .reshape(share_rows // 2, block_size, 2 * block_size)
    )
    agg_row = (
        jnp.zeros((1, block_size, 2 * block_size), jnp.bfloat16)
        .at[0, 0, :share_rows]
        .set(aggregates.astype(jnp.bfloat16))
    )
    local_ext = jnp.concatenate([local_pairs, agg_row], axis=0)
    piece_rows = local_ext.shape[0]
    received = [local_ext]
    for k in range(1, group_size):
        received.append(
            lax.ppermute(
                local_ext, "grp", [(i, (i + k) % group_size) for i in range(group_size)]
            )
        )
    n = panel_total
    down_skip = ({(n - 1, 0)}, {(n - 1, 0), (0, 1)})
    up_skip = ({(0, n - 1)}, {(0, n - 1), (n - 1, n - 2)})

    def ring(piece, step, hop, full):
        skip = set() if full else (down_skip if step == 1 else up_skip)[hop]
        route = [((i - step) % n, i) for i in range(n)]
        route = [pair for pair in route if pair not in skip]
        return lax.ppermute(piece, "blk", route)

    down1 = [ring(piece, 1, 0, k == 0) for k, piece in enumerate(received)]
    up1 = [ring(piece, -1, 0, k == 0) for k, piece in enumerate(received)]
    down2 = [ring(piece, 1, 1, k == 0) for k, piece in enumerate(down1)]
    up2 = [ring(piece, -1, 1, k == 0) for k, piece in enumerate(up1)]
    pieces = down2 + down1 + received + up1 + up2
    low_end = me <= 1
    fix_first = jnp.where(low_end, down2[0], up2[0])
    fix_second = jnp.where(me == 0, down1[0], up1[0])
    fix_src = jnp.stack([fix_first, fix_second])
    ends = [0, 1, n - 2, n - 1]
    fixed = []
    for k in range(1, group_size):
        route = [
            (b * group_size + g, b * group_size + (g + k) % group_size)
            for b in ends
            for g in range(group_size)
        ]
        fixed.append(lax.ppermute(fix_src, ("blk", "grp"), route))
    minus = jnp.int32(-1)
    fix = jnp.stack([
        jnp.where(low_end, 0, minus),
        jnp.where(me == 0, 1, minus),
        minus,
        jnp.where(me == n - 1, 1, minus),
        jnp.where(me >= n - 2, 0, minus),
    ]).astype(jnp.int32)
    agg_rows = []
    for d in range(5):
        for k in range(group_size):
            row = pieces[d * group_size + k][share_rows // 2, 0, :share_rows]
            if k > 0:
                row = jnp.where(
                    fix[d] >= 0,
                    jnp.where(
                        fix[d] == 0,
                        fixed[k - 1][0, share_rows // 2, 0, :share_rows],
                        fixed[k - 1][1, share_rows // 2, 0, :share_rows],
                    ),
                    row,
                )
            agg_rows.append(row)
    flat_aggs = jnp.stack(agg_rows).astype(jnp.int32).reshape(-1)

    def placed(d, r):
        k = jnp.mod(group_me - r // share_rows, group_size)
        return d * group_size + k, r % share_rows

    wanted = block_columns.reshape(slot_total)
    column_panel = wanted // panel_length
    distance = jnp.mod(column_panel - me + 2, panel_total)
    piece_of, within = placed(distance, wanted % panel_length)
    window_pair = piece_of * piece_rows + within // 2
    fetched_aggs = jnp.take(flat_aggs, piece_of * share_rows + within, axis=0)
    own_piece, own_within = placed(2, jnp.arange(panel_length, dtype=jnp.int32))
    own_pos = own_piece * piece_rows + own_within // 2
    own_aggs = jnp.take(flat_aggs, own_piece * share_rows + own_within, axis=0)
    slot_ids = lax.axis_index("grp") * slots_here + jnp.arange(slots_here, dtype=jnp.int32)
    live = (slot_ids[None, :] < row_counts[:, None]).astype(jnp.int32).reshape(slot_total)
    local_coarse = own_aggs - me * CB
    target = fetched_aggs * CB + jnp.broadcast_to(
        local_coarse[:, None], (panel_length, slots_here)
    ).reshape(slot_total)
    summed = coarse_partial(
        window_pair.astype(jnp.int32),
        (within % 2).astype(jnp.int32),
        target.astype(jnp.int32),
        live,
        own_pos,
        fix,
        block_values,
        pieces,
        fixed,
        coarse_count * CB,
    )
    share = coarse_count // group_size
    summed = summed.reshape(group_size, share, CB // 2, block_size, 2 * block_size)
    total = jnp.take(summed, group_me, axis=0)
    for k in range(1, group_size):
        outgoing = jnp.take(summed, jnp.mod(group_me + k, group_size), axis=0)
        total = total + lax.ppermute(
            outgoing, "grp", [(i, (i + k) % group_size) for i in range(group_size)]
        )
    total = total.reshape(share, CB // 2, block_size, 2, block_size)
    return total.transpose(0, 1, 3, 2, 4).reshape(share, CB, block_size, block_size)


def solution(mesh):
    return jax.shard_map(
        local,
        mesh=mesh,
        in_specs=(
            P("blk", "grp", None, None),
            P("blk", "grp"),
            P("blk"),
            P(("blk", "grp"), None, None),
            P(("blk", "grp")),
        ),
        out_specs=P("grp", "blk", None, None),
        check_vma=False,
    )
```

```python
import functools

import jax
import jax.numpy as jnp
from jax import lax
from jax.experimental import pallas as pl
from jax.experimental.pallas import tpu as pltpu
from jax.sharding import PartitionSpec as P

CB = 4
ROWS_PER_STEP = 16


def passed_along(block, axis, distance):
    devices = range(lax.axis_size(axis))
    route = [((i - distance) % len(devices), i) for i in devices]
    return lax.ppermute(block, axis, route)


def coarse_kernel(
    pair_ref, half_ref, target_ref, live_ref, own_pos_ref, fix_ref, values_ref, *rest
):
    out_ref, acc_ref, window, own_scratch, sems = rest[-5:]
    n_pieces = sems.shape[0]
    groups = n_pieces // 5
    pieces = rest[:n_pieces]
    fixed = rest[n_pieces:-5]
    step = pl.program_id(0)
    rows_here, slots, bs, _ = values_ref.shape
    piece_rows = pieces[0].shape[0]
    lanes = window.shape[2]

    @pl.when(step == 0)
    def _():
        copies = []
        for j, piece in enumerate(pieces):
            dst = window.at[pl.ds(j * piece_rows, piece_rows)]
            cp = pltpu.make_async_copy(piece, dst, sems.at[j])
            d, k = divmod(j, groups)
            if k == 0:
                cp.start()
            else:
                flag = fix_ref[d]

                @pl.when(flag < 0)
                def _():
                    cp.start()

                for slot in range(2):
                    @pl.when(flag == slot)
                    def _():
                        pltpu.make_async_copy(
                            fixed[k - 1].at[slot], dst, sems.at[j]
                        ).start()

            copies.append(cp)
        acc_ref[...] = jnp.zeros_like(acc_ref)
        for cp in copies:
            cp.wait()

        def transpose_pair(m, carry):
            own_pair = window[own_pos_ref[2 * m]].astype(jnp.float32)
            spread = jnp.concatenate([own_pair, jnp.zeros_like(own_pair)], axis=0).T
            own_scratch[2 * m] = spread[:bs, :bs].astype(jnp.bfloat16)
            own_scratch[2 * m + 1] = spread[bs:, :bs].astype(jnp.bfloat16)
            return carry

        lax.fori_loop(0, own_scratch.shape[0] // 2, transpose_pair, 0)

    lane_half = lax.broadcasted_iota(jnp.int32, (bs, lanes), 1) // bs

    def row_body(r, carry):
        row = step * rows_here + r
        own_t = own_scratch[row]
        results = []
        for s in range(slots):
            n = row * slots + s
            pair = window[pair_ref[n]]
            picked = jnp.where(lane_half == half_ref[n], pair, jnp.zeros_like(pair))
            product = jnp.dot(
                values_ref[r, s], picked, preferred_element_type=jnp.float32
            )
            product = jnp.where(live_ref[n] > 0, product, 0.0).astype(jnp.bfloat16)
            results.append(
                jnp.dot(own_t, product, preferred_element_type=jnp.float32)
            )
        for s in range(slots):
            t = target_ref[row * slots + s]
            acc_ref[t] = acc_ref[t] + results[s]
        return carry

    lax.fori_loop(0, rows_here, row_body, 0, unroll=2)

    @pl.when(step == pl.num_programs(0) - 1)
    def _():
        def pack(m, carry):
            first = acc_ref[2 * m]
            second = acc_ref[2 * m + 1]
            first = first + pltpu.roll(first, bs, 1)
            second = second + pltpu.roll(second, bs, 1)
            out_ref[m] = jnp.where(lane_half == 0, first, second)
            return carry

        lax.fori_loop(0, out_ref.shape[0], pack, 0)


def coarse_partial(pair, half, target, live, own_pos, fix, values, pieces, fixed, n_targets):
    panel_length, slots, bs, _ = values.shape
    rows_per_step = min(ROWS_PER_STEP, panel_length)
    grid = (panel_length // rows_per_step,)
    piece_rows, _, lanes = pieces[0].shape
    return pl.pallas_call(
        coarse_kernel,
        out_shape=jax.ShapeDtypeStruct((n_targets // 2, bs, lanes), jnp.float32),
        grid_spec=pltpu.PrefetchScalarGridSpec(
            num_scalar_prefetch=6,
            grid=grid,
            in_specs=[
                pl.BlockSpec((rows_per_step, slots, bs, bs), lambda i, *_: (i, 0, 0, 0)),
            ]
            + [pl.BlockSpec(memory_space=pl.ANY)] * (len(pieces) + len(fixed)),
            out_specs=pl.BlockSpec((n_targets // 2, bs, lanes), lambda i, *_: (0, 0, 0)),
            scratch_shapes=[
                pltpu.VMEM((n_targets, bs, lanes), jnp.float32),
                pltpu.VMEM((len(pieces) * piece_rows, bs, lanes), jnp.bfloat16),
                pltpu.VMEM((panel_length, bs, bs), jnp.bfloat16),
                pltpu.SemaphoreType.DMA((len(pieces),)),
            ],
        ),
        compiler_params=pltpu.CompilerParams(
            dimension_semantics=("arbitrary",),
            vmem_limit_bytes=60 * 1024 * 1024,
        ),
    )(pair, half, target, live, own_pos, fix, values, *pieces, *fixed)


def local(block_values, block_columns, row_counts, prolong_blocks, aggregates):
    panel_length = row_counts.shape[0]
    slots_here = block_values.shape[1]
    slot_total = panel_length * slots_here
    block_size = block_values.shape[2]
    group_size = lax.axis_size("grp")
    panel_total = lax.axis_size("blk")
    coarse_count = CB * panel_total
    me = lax.axis_index("blk")
    group_me = lax.axis_index("grp")
    share_rows = prolong_blocks.shape[0]
    local_pairs = (
        prolong_blocks.reshape(share_rows // 2, 2, block_size, block_size)
        .transpose(0, 2, 1, 3)
        .reshape(share_rows // 2, block_size, 2 * block_size)
    )
    agg_row = (
        jnp.zeros((1, block_size, 2 * block_size), jnp.bfloat16)
        .at[0, 0, :share_rows]
        .set(aggregates.astype(jnp.bfloat16))
    )
    local_ext = jnp.concatenate([local_pairs, agg_row], axis=0)
    piece_rows = local_ext.shape[0]
    received = [local_ext]
    for k in range(1, group_size):
        received.append(
            lax.ppermute(
                local_ext, "grp", [(i, (i + k) % group_size) for i in range(group_size)]
            )
        )
    n = panel_total
    down_skip = ({(n - 1, 0)}, {(n - 1, 0), (0, 1)})
    up_skip = ({(0, n - 1)}, {(0, n - 1), (n - 1, n - 2)})

    def ring(piece, step, hop, full):
        skip = set() if full else (down_skip if step == 1 else up_skip)[hop]
        route = [((i - step) % n, i) for i in range(n)]
        route = [pair for pair in route if pair not in skip]
        return lax.ppermute(piece, "blk", route)

    down1 = [ring(piece, 1, 0, k == 0) for k, piece in enumerate(received)]
    up1 = [ring(piece, -1, 0, k == 0) for k, piece in enumerate(received)]
    down2 = [ring(piece, 1, 1, k == 0) for k, piece in enumerate(down1)]
    up2 = [ring(piece, -1, 1, k == 0) for k, piece in enumerate(up1)]
    pieces = down2 + down1 + received + up1 + up2
    low_end = me <= 1
    fix_first = jnp.where(low_end, down2[0], up2[0])
    fix_second = jnp.where(me == 0, down1[0], up1[0])
    fix_src = jnp.stack([fix_first, fix_second])
    ends = [0, 1, n - 2, n - 1]
    fixed = []
    for k in range(1, group_size):
        route = [
            (b * group_size + g, b * group_size + (g + k) % group_size)
            for b in ends
            for g in range(group_size)
        ]
        fixed.append(lax.ppermute(fix_src, ("blk", "grp"), route))
    minus = jnp.int32(-1)
    fix = jnp.stack([
        jnp.where(low_end, 0, minus),
        jnp.where(me == 0, 1, minus),
        minus,
        jnp.where(me == n - 1, 1, minus),
        jnp.where(me >= n - 2, 0, minus),
    ]).astype(jnp.int32)
    agg_rows = []
    for d in range(5):
        for k in range(group_size):
            row = pieces[d * group_size + k][share_rows // 2, 0, :share_rows]
            if k > 0:
                row = jnp.where(
                    fix[d] >= 0,
                    jnp.where(
                        fix[d] == 0,
                        fixed[k - 1][0, share_rows // 2, 0, :share_rows],
                        fixed[k - 1][1, share_rows // 2, 0, :share_rows],
                    ),
                    row,
                )
            agg_rows.append(row)
    flat_aggs = jnp.stack(agg_rows).astype(jnp.int32).reshape(-1)

    def placed(d, r):
        k = jnp.mod(group_me - r // share_rows, group_size)
        return d * group_size + k, r % share_rows

    wanted = block_columns.reshape(slot_total)
    column_panel = wanted // panel_length
    distance = jnp.mod(column_panel - me + 2, panel_total)
    piece_of, within = placed(distance, wanted % panel_length)
    window_pair = piece_of * piece_rows + within // 2
    fetched_aggs = jnp.take(flat_aggs, piece_of * share_rows + within, axis=0)
    own_piece, own_within = placed(2, jnp.arange(panel_length, dtype=jnp.int32))
    own_pos = own_piece * piece_rows + own_within // 2
    own_aggs = jnp.take(flat_aggs, own_piece * share_rows + own_within, axis=0)
    slot_ids = lax.axis_index("grp") * slots_here + jnp.arange(slots_here, dtype=jnp.int32)
    live = (slot_ids[None, :] < row_counts[:, None]).astype(jnp.int32).reshape(slot_total)
    local_coarse = own_aggs - me * CB
    target = fetched_aggs * CB + jnp.broadcast_to(
        local_coarse[:, None], (panel_length, slots_here)
    ).reshape(slot_total)
    summed = coarse_partial(
        window_pair.astype(jnp.int32),
        (within % 2).astype(jnp.int32),
        target.astype(jnp.int32),
        live,
        own_pos,
        fix,
        block_values,
        pieces,
        fixed,
        coarse_count * CB,
    )
    share = coarse_count // group_size
    summed = summed.reshape(group_size, share, CB // 2, block_size, 2 * block_size)
    total = jnp.take(summed, group_me, axis=0)
    for k in range(1, group_size):
        outgoing = jnp.take(summed, jnp.mod(group_me + k, group_size), axis=0)
        total = total + lax.ppermute(
            outgoing, "grp", [(i, (i + k) % group_size) for i in range(group_size)]
        )
    total = total.reshape(share, CB // 2, block_size, 2, block_size)
    return total.transpose(0, 1, 3, 2, 4).reshape(share, CB, block_size, block_size)


def solution(mesh):
    return jax.shard_map(
        local,
        mesh=mesh,
        in_specs=(
            P("blk", "grp", None, None),
            P("blk", "grp"),
            P("blk"),
            P(("blk", "grp"), None, None),
            P(("blk", "grp")),
        ),
        out_specs=P("grp", "blk", None, None),
        check_vma=False,
    )
```

```python
import functools

import jax
import jax.numpy as jnp
from jax import lax
from jax.experimental import pallas as pl
from jax.experimental.pallas import tpu as pltpu
from jax.sharding import PartitionSpec as P

CB = 4
ROWS_PER_STEP = 16


def passed_along(block, axis, distance):
    devices = range(lax.axis_size(axis))
    route = [((i - distance) % len(devices), i) for i in devices]
    return lax.ppermute(block, axis, route)


def coarse_kernel(
    pair_ref, half_ref, target_ref, live_ref, own_pos_ref, fix_ref, values_ref, *rest
):
    window, sems = rest[-2:]
    n_pieces = sems.shape[0]
    groups = n_pieces // 5
    pieces = rest[:n_pieces]
    n_fixed = groups - 1
    fixed = rest[n_pieces : n_pieces + n_fixed]
    out_ref = rest[n_pieces + n_fixed]
    accs = rest[n_pieces + n_fixed + 1 : -2]
    step = pl.program_id(0)
    rows_here, slots, bs, _ = values_ref.shape
    piece_rows = pieces[0].shape[0]
    lanes = window.shape[2]

    @pl.when(step == 0)
    def _():
        copies = []
        for j, piece in enumerate(pieces):
            dst = window.at[pl.ds(j * piece_rows, piece_rows)]
            cp = pltpu.make_async_copy(piece, dst, sems.at[j])
            d, k = divmod(j, groups)
            if k == 0:
                cp.start()
            else:
                flag = fix_ref[d]

                @pl.when(flag < 0)
                def _():
                    cp.start()

                for slot in range(2):
                    @pl.when(flag == slot)
                    def _():
                        pltpu.make_async_copy(
                            fixed[k - 1].at[slot], dst, sems.at[j]
                        ).start()

            copies.append(cp)
        for acc_ref in accs:
            acc_ref[...] = jnp.zeros_like(acc_ref)
        for cp in copies:
            cp.wait()

    lane_half = lax.broadcasted_iota(jnp.int32, (bs, lanes), 1) // bs

    def row_body(r, carry):
        row = step * rows_here + r
        own_pair = window[own_pos_ref[row]].astype(jnp.float32)
        spread = jnp.concatenate([own_pair, jnp.zeros_like(own_pair)], axis=0).T
        own_t = jnp.where(row % 2 == 0, spread[:bs], spread[bs:])[:, :bs]
        own_t = own_t.astype(jnp.bfloat16)
        results = []
        for s in range(slots):
            n = row * slots + s
            pair = window[pair_ref[n]]
            picked = jnp.where(lane_half == half_ref[n], pair, jnp.zeros_like(pair))
            product = jnp.dot(
                values_ref[r, s], picked, preferred_element_type=jnp.float32
            )
            product = jnp.where(live_ref[n] > 0, product, 0.0).astype(jnp.bfloat16)
            results.append(
                jnp.dot(own_t, product, preferred_element_type=jnp.float32)
            )
        for s in range(slots):
            t = target_ref[row * slots + s]
            accs[s][t] = accs[s][t] + results[s]
        return carry

    lax.fori_loop(0, rows_here, row_body, 0, unroll=2)

    @pl.when(step == pl.num_programs(0) - 1)
    def _():
        def pack(m, carry):
            first = sum(acc_ref[2 * m] for acc_ref in accs)
            second = sum(acc_ref[2 * m + 1] for acc_ref in accs)
            first = first + pltpu.roll(first, bs, 1)
            second = second + pltpu.roll(second, bs, 1)
            out_ref[m] = jnp.where(lane_half == 0, first, second)
            return carry

        lax.fori_loop(0, out_ref.shape[0], pack, 0)


def coarse_partial(pair, half, target, live, own_pos, fix, values, pieces, fixed, n_targets):
    panel_length, slots, bs, _ = values.shape
    rows_per_step = min(ROWS_PER_STEP, panel_length)
    grid = (panel_length // rows_per_step,)
    piece_rows, _, lanes = pieces[0].shape
    return pl.pallas_call(
        coarse_kernel,
        out_shape=jax.ShapeDtypeStruct((n_targets // 2, bs, lanes), jnp.float32),
        grid_spec=pltpu.PrefetchScalarGridSpec(
            num_scalar_prefetch=6,
            grid=grid,
            in_specs=[
                pl.BlockSpec((rows_per_step, slots, bs, bs), lambda i, *_: (i, 0, 0, 0)),
            ]
            + [pl.BlockSpec(memory_space=pl.ANY)] * (len(pieces) + len(fixed)),
            out_specs=pl.BlockSpec((n_targets // 2, bs, lanes), lambda i, *_: (0, 0, 0)),
            scratch_shapes=[pltpu.VMEM((n_targets, bs, lanes), jnp.float32)] * slots
            + [
                pltpu.VMEM((len(pieces) * piece_rows, bs, lanes), jnp.bfloat16),
                pltpu.SemaphoreType.DMA((len(pieces),)),
            ],
        ),
        compiler_params=pltpu.CompilerParams(
            dimension_semantics=("arbitrary",),
            vmem_limit_bytes=60 * 1024 * 1024,
        ),
    )(pair, half, target, live, own_pos, fix, values, *pieces, *fixed)


def local(block_values, block_columns, row_counts, prolong_blocks, aggregates):
    panel_length = row_counts.shape[0]
    slots_here = block_values.shape[1]
    slot_total = panel_length * slots_here
    block_size = block_values.shape[2]
    group_size = lax.axis_size("grp")
    panel_total = lax.axis_size("blk")
    coarse_count = CB * panel_total
    me = lax.axis_index("blk")
    group_me = lax.axis_index("grp")
    share_rows = prolong_blocks.shape[0]
    local_pairs = (
        prolong_blocks.reshape(share_rows // 2, 2, block_size, block_size)
        .transpose(0, 2, 1, 3)
        .reshape(share_rows // 2, block_size, 2 * block_size)
    )
    agg_row = (
        jnp.zeros((1, block_size, 2 * block_size), jnp.bfloat16)
        .at[0, 0, :share_rows]
        .set(aggregates.astype(jnp.bfloat16))
    )
    local_ext = jnp.concatenate([local_pairs, agg_row], axis=0)
    piece_rows = local_ext.shape[0]
    received = [local_ext]
    for k in range(1, group_size):
        received.append(
            lax.ppermute(
                local_ext, "grp", [(i, (i + k) % group_size) for i in range(group_size)]
            )
        )
    n = panel_total
    down_skip = ({(n - 1, 0)}, {(n - 1, 0), (0, 1)})
    up_skip = ({(0, n - 1)}, {(0, n - 1), (n - 1, n - 2)})

    def ring(piece, step, hop, full):
        skip = set() if full else (down_skip if step == 1 else up_skip)[hop]
        route = [((i - step) % n, i) for i in range(n)]
        route = [pair for pair in route if pair not in skip]
        return lax.ppermute(piece, "blk", route)

    down1 = [ring(piece, 1, 0, k == 0) for k, piece in enumerate(received)]
    up1 = [ring(piece, -1, 0, k == 0) for k, piece in enumerate(received)]
    down2 = [ring(piece, 1, 1, k == 0) for k, piece in enumerate(down1)]
    up2 = [ring(piece, -1, 1, k == 0) for k, piece in enumerate(up1)]
    pieces = down2 + down1 + received + up1 + up2
    low_end = me <= 1
    fix_first = jnp.where(low_end, down2[0], up2[0])
    fix_second = jnp.where(me == 0, down1[0], up1[0])
    fix_src = jnp.stack([fix_first, fix_second])
    ends = [0, 1, n - 2, n - 1]
    fixed = []
    for k in range(1, group_size):
        route = [
            (b * group_size + g, b * group_size + (g + k) % group_size)
            for b in ends
            for g in range(group_size)
        ]
        fixed.append(lax.ppermute(fix_src, ("blk", "grp"), route))
    minus = jnp.int32(-1)
    fix = jnp.stack([
        jnp.where(low_end, 0, minus),
        jnp.where(me == 0, 1, minus),
        minus,
        jnp.where(me == n - 1, 1, minus),
        jnp.where(me >= n - 2, 0, minus),
    ]).astype(jnp.int32)
    agg_rows = []
    for d in range(5):
        for k in range(group_size):
            row = pieces[d * group_size + k][share_rows // 2, 0, :share_rows]
            if k > 0:
                row = jnp.where(
                    fix[d] >= 0,
                    jnp.where(
                        fix[d] == 0,
                        fixed[k - 1][0, share_rows // 2, 0, :share_rows],
                        fixed[k - 1][1, share_rows // 2, 0, :share_rows],
                    ),
                    row,
                )
            agg_rows.append(row)
    flat_aggs = jnp.stack(agg_rows).astype(jnp.int32).reshape(-1)

    def placed(d, r):
        k = jnp.mod(group_me - r // share_rows, group_size)
        return d * group_size + k, r % share_rows

    wanted = block_columns.reshape(slot_total)
    column_panel = wanted // panel_length
    distance = jnp.mod(column_panel - me + 2, panel_total)
    piece_of, within = placed(distance, wanted % panel_length)
    window_pair = piece_of * piece_rows + within // 2
    fetched_aggs = jnp.take(flat_aggs, piece_of * share_rows + within, axis=0)
    own_piece, own_within = placed(2, jnp.arange(panel_length, dtype=jnp.int32))
    own_pos = own_piece * piece_rows + own_within // 2
    own_aggs = jnp.take(flat_aggs, own_piece * share_rows + own_within, axis=0)
    slot_ids = lax.axis_index("grp") * slots_here + jnp.arange(slots_here, dtype=jnp.int32)
    live = (slot_ids[None, :] < row_counts[:, None]).astype(jnp.int32).reshape(slot_total)
    local_coarse = own_aggs - me * CB
    target = fetched_aggs * CB + jnp.broadcast_to(
        local_coarse[:, None], (panel_length, slots_here)
    ).reshape(slot_total)
    summed = coarse_partial(
        window_pair.astype(jnp.int32),
        (within % 2).astype(jnp.int32),
        target.astype(jnp.int32),
        live,
        own_pos,
        fix,
        block_values,
        pieces,
        fixed,
        coarse_count * CB,
    )
    share = coarse_count // group_size
    summed = summed.reshape(group_size, share, CB // 2, block_size, 2 * block_size)
    total = jnp.take(summed, group_me, axis=0)
    for k in range(1, group_size):
        outgoing = jnp.take(summed, jnp.mod(group_me + k, group_size), axis=0)
        total = total + lax.ppermute(
            outgoing, "grp", [(i, (i + k) % group_size) for i in range(group_size)]
        )
    total = total.reshape(share, CB // 2, block_size, 2, block_size)
    return total.transpose(0, 1, 3, 2, 4).reshape(share, CB, block_size, block_size)


def solution(mesh):
    return jax.shard_map(
        local,
        mesh=mesh,
        in_specs=(
            P("blk", "grp", None, None),
            P("blk", "grp"),
            P("blk"),
            P(("blk", "grp"), None, None),
            P(("blk", "grp")),
        ),
        out_specs=P("grp", "blk", None, None),
        check_vma=False,
    )
```

```python
import functools

import jax
import jax.numpy as jnp
from jax import lax
from jax.experimental import pallas as pl
from jax.experimental.pallas import tpu as pltpu
from jax.sharding import PartitionSpec as P

CB = 4
ROWS_PER_STEP = 16


def passed_along(block, axis, distance):
    devices = range(lax.axis_size(axis))
    route = [((i - distance) % len(devices), i) for i in devices]
    return lax.ppermute(block, axis, route)


def coarse_kernel(
    pair_ref, half_ref, target_ref, live_ref, own_pos_ref, fix_ref, values_ref, *rest
):
    out_ref, acc_ref, window, sems = rest[-4:]
    n_pieces = sems.shape[0]
    groups = n_pieces // 5
    pieces = rest[:n_pieces]
    fixed = rest[n_pieces:-4]
    step = pl.program_id(0)
    rows_here, slots, bs, _ = values_ref.shape
    piece_rows = pieces[0].shape[0]
    lanes = window.shape[2]

    @pl.when(step == 0)
    def _():
        copies = []
        for j, piece in enumerate(pieces):
            dst = window.at[pl.ds(j * piece_rows, piece_rows)]
            cp = pltpu.make_async_copy(piece, dst, sems.at[j])
            d, k = divmod(j, groups)
            if k == 0:
                cp.start()
            else:
                flag = fix_ref[d]

                @pl.when(flag < 0)
                def _():
                    cp.start()

                for slot in range(2):
                    @pl.when(flag == slot)
                    def _():
                        pltpu.make_async_copy(
                            fixed[k - 1].at[slot], dst, sems.at[j]
                        ).start()

            copies.append(cp)
        acc_ref[...] = jnp.zeros_like(acc_ref)
        for cp in copies:
            cp.wait()

    lane_half = lax.broadcasted_iota(jnp.int32, (bs, lanes), 1) // bs

    def row_body(r, carry):
        row = step * rows_here + r
        own_pair = window[own_pos_ref[row]].astype(jnp.float32)
        spread = jnp.concatenate([own_pair, jnp.zeros_like(own_pair)], axis=0).T
        own_t = jnp.where(row % 2 == 0, spread[:bs], spread[bs:])[:, :bs]
        own_t = own_t.astype(jnp.bfloat16)
        results = []
        for s in range(slots):
            n = row * slots + s
            pair = window[pair_ref[n]]
            picked = jnp.where(lane_half == half_ref[n], pair, jnp.zeros_like(pair))
            product = jnp.dot(
                values_ref[r, s], picked, preferred_element_type=jnp.float32
            )
            product = jnp.where(live_ref[n] > 0, product, 0.0).astype(jnp.bfloat16)
            results.append(
                jnp.dot(own_t, product, preferred_element_type=jnp.float32)
            )
        for s in range(slots):
            t = target_ref[row * slots + s]
            acc_ref[t] = acc_ref[t] + results[s]
        return carry

    lax.fori_loop(0, rows_here, row_body, 0, unroll=2)

    @pl.when(step == pl.num_programs(0) - 1)
    def _():
        def pack(m, carry):
            first = acc_ref[2 * m]
            second = acc_ref[2 * m + 1]
            first = first + pltpu.roll(first, bs, 1)
            second = second + pltpu.roll(second, bs, 1)
            out_ref[m] = jnp.where(lane_half == 0, first, second)
            return carry

        lax.fori_loop(0, out_ref.shape[0], pack, 0)


def coarse_partial(pair, half, target, live, own_pos, fix, values, pieces, fixed, n_targets):
    panel_length, slots, bs, _ = values.shape
    rows_per_step = min(ROWS_PER_STEP, panel_length)
    grid = (panel_length // rows_per_step,)
    piece_rows, _, lanes = pieces[0].shape
    return pl.pallas_call(
        coarse_kernel,
        out_shape=jax.ShapeDtypeStruct((n_targets // 2, bs, lanes), jnp.float32),
        grid_spec=pltpu.PrefetchScalarGridSpec(
            num_scalar_prefetch=6,
            grid=grid,
            in_specs=[
                pl.BlockSpec((rows_per_step, slots, bs, bs), lambda i, *_: (i, 0, 0, 0)),
            ]
            + [pl.BlockSpec(memory_space=pl.ANY)] * (len(pieces) + len(fixed)),
            out_specs=pl.BlockSpec((n_targets // 2, bs, lanes), lambda i, *_: (0, 0, 0)),
            scratch_shapes=[
                pltpu.VMEM((n_targets, bs, lanes), jnp.float32),
                pltpu.VMEM((len(pieces) * piece_rows, bs, lanes), jnp.bfloat16),
                pltpu.SemaphoreType.DMA((len(pieces),)),
            ],
        ),
        compiler_params=pltpu.CompilerParams(
            dimension_semantics=("arbitrary",),
            vmem_limit_bytes=60 * 1024 * 1024,
        ),
    )(pair, half, target, live, own_pos, fix, values, *pieces, *fixed)


def local(block_values, block_columns, row_counts, prolong_blocks, aggregates):
    panel_length = row_counts.shape[0]
    slots_here = block_values.shape[1]
    slot_total = panel_length * slots_here
    block_size = block_values.shape[2]
    group_size = lax.axis_size("grp")
    panel_total = lax.axis_size("blk")
    coarse_count = CB * panel_total
    me = lax.axis_index("blk")
    group_me = lax.axis_index("grp")
    share_rows = prolong_blocks.shape[0]
    local_pairs = (
        prolong_blocks.reshape(share_rows // 2, 2, block_size, block_size)
        .transpose(0, 2, 1, 3)
        .reshape(share_rows // 2, block_size, 2 * block_size)
    )
    agg_row = (
        jnp.zeros((1, block_size, 2 * block_size), jnp.bfloat16)
        .at[0, 0, :share_rows]
        .set(aggregates.astype(jnp.bfloat16))
    )
    local_ext = jnp.concatenate([local_pairs, agg_row], axis=0)
    piece_rows = local_ext.shape[0]
    received = [local_ext]
    for k in range(1, group_size):
        received.append(
            lax.ppermute(
                local_ext, "grp", [(i, (i + k) % group_size) for i in range(group_size)]
            )
        )
    n = panel_total
    down_skip = ({(n - 1, 0)}, {(n - 1, 0), (0, 1)})
    up_skip = ({(0, n - 1)}, {(0, n - 1), (n - 1, n - 2)})

    def ring(piece, step, hop, full):
        skip = set() if full else (down_skip if step == 1 else up_skip)[hop]
        route = [((i - step) % n, i) for i in range(n)]
        route = [pair for pair in route if pair not in skip]
        return lax.ppermute(piece, "blk", route)

    down1 = [ring(piece, 1, 0, k == 0) for k, piece in enumerate(received)]
    up1 = [ring(piece, -1, 0, k == 0) for k, piece in enumerate(received)]
    down2 = [ring(piece, 1, 1, k == 0) for k, piece in enumerate(down1)]
    up2 = [ring(piece, -1, 1, k == 0) for k, piece in enumerate(up1)]
    pieces = down2 + down1 + received + up1 + up2
    low_end = me <= 1
    fix_first = jnp.where(low_end, down2[0], up2[0])
    fix_second = jnp.where(me == 0, down1[0], up1[0])
    fix_src = jnp.stack([fix_first, fix_second])
    ends = [0, 1, n - 2, n - 1]
    fixed = []
    for k in range(1, group_size):
        route = [
            (b * group_size + g, b * group_size + (g + k) % group_size)
            for b in ends
            for g in range(group_size)
        ]
        fixed.append(lax.ppermute(fix_src, ("blk", "grp"), route))
    minus = jnp.int32(-1)
    fix = jnp.stack([
        jnp.where(low_end, 0, minus),
        jnp.where(me == 0, 1, minus),
        minus,
        jnp.where(me == n - 1, 1, minus),
        jnp.where(me >= n - 2, 0, minus),
    ]).astype(jnp.int32)
    agg_rows = []
    for d in range(5):
        for k in range(group_size):
            row = pieces[d * group_size + k][share_rows // 2, 0, :share_rows]
            if k > 0:
                row = jnp.where(
                    fix[d] >= 0,
                    jnp.where(
                        fix[d] == 0,
                        fixed[k - 1][0, share_rows // 2, 0, :share_rows],
                        fixed[k - 1][1, share_rows // 2, 0, :share_rows],
                    ),
                    row,
                )
            agg_rows.append(row)
    flat_aggs = jnp.stack(agg_rows).astype(jnp.int32).reshape(-1)

    def placed(d, r):
        k = jnp.mod(group_me - r // share_rows, group_size)
        return d * group_size + k, r % share_rows

    wanted = block_columns.reshape(slot_total)
    column_panel = wanted // panel_length
    distance = jnp.mod(column_panel - me + 2, panel_total)
    piece_of, within = placed(distance, wanted % panel_length)
    window_pair = piece_of * piece_rows + within // 2
    fetched_aggs = jnp.take(flat_aggs, piece_of * share_rows + within, axis=0)
    own_piece, own_within = placed(2, jnp.arange(panel_length, dtype=jnp.int32))
    own_pos = own_piece * piece_rows + own_within // 2
    own_aggs = jnp.take(flat_aggs, own_piece * share_rows + own_within, axis=0)
    slot_ids = lax.axis_index("grp") * slots_here + jnp.arange(slots_here, dtype=jnp.int32)
    live = (slot_ids[None, :] < row_counts[:, None]).astype(jnp.int32).reshape(slot_total)
    local_coarse = own_aggs - me * CB
    target = fetched_aggs * CB + jnp.broadcast_to(
        local_coarse[:, None], (panel_length, slots_here)
    ).reshape(slot_total)
    summed = coarse_partial(
        window_pair.astype(jnp.int32),
        (within % 2).astype(jnp.int32),
        target.astype(jnp.int32),
        live,
        own_pos,
        fix,
        block_values,
        pieces,
        fixed,
        coarse_count * CB,
    )
    share = coarse_count // group_size
    summed = summed.reshape(group_size, share, CB // 2, block_size, 2 * block_size)
    total = jnp.take(summed, group_me, axis=0)
    for k in range(1, group_size):
        outgoing = jnp.take(summed, jnp.mod(group_me + k, group_size), axis=0)
        incoming = lax.ppermute(
            outgoing.astype(jnp.bfloat16),
            "grp",
            [(i, (i + k) % group_size) for i in range(group_size)],
        )
        total = total + incoming.astype(jnp.float32)
    total = total.reshape(share, CB // 2, block_size, 2, block_size)
    return total.transpose(0, 1, 3, 2, 4).reshape(share, CB, block_size, block_size)


def solution(mesh):
    return jax.shard_map(
        local,
        mesh=mesh,
        in_specs=(
            P("blk", "grp", None, None),
            P("blk", "grp"),
            P("blk"),
            P(("blk", "grp"), None, None),
            P(("blk", "grp")),
        ),
        out_specs=P("grp", "blk", None, None),
        check_vma=False,
    )
```

```python
import functools

import jax
import jax.numpy as jnp
from jax import lax
from jax.experimental import pallas as pl
from jax.experimental.pallas import tpu as pltpu
from jax.sharding import PartitionSpec as P

CB = 4
ROWS_PER_STEP = 48


def passed_along(block, axis, distance):
    devices = range(lax.axis_size(axis))
    route = [((i - distance) % len(devices), i) for i in devices]
    return lax.ppermute(block, axis, route)


def coarse_kernel(
    pair_ref, half_ref, target_ref, live_ref, own_pos_ref, fix_ref, values_ref, *rest
):
    out_ref, acc_ref, window, sems = rest[-4:]
    n_pieces = sems.shape[0]
    groups = n_pieces // 5
    pieces = rest[:n_pieces]
    fixed = rest[n_pieces:-4]
    step = pl.program_id(0)
    rows_here, slots, bs, _ = values_ref.shape
    piece_rows = pieces[0].shape[0]
    lanes = window.shape[2]

    @pl.when(step == 0)
    def _():
        copies = []
        for j, piece in enumerate(pieces):
            dst = window.at[pl.ds(j * piece_rows, piece_rows)]
            cp = pltpu.make_async_copy(piece, dst, sems.at[j])
            d, k = divmod(j, groups)
            if k == 0:
                cp.start()
            else:
                flag = fix_ref[d]

                @pl.when(flag < 0)
                def _():
                    cp.start()

                for slot in range(2):
                    @pl.when(flag == slot)
                    def _():
                        pltpu.make_async_copy(
                            fixed[k - 1].at[slot], dst, sems.at[j]
                        ).start()

            copies.append(cp)
        acc_ref[...] = jnp.zeros_like(acc_ref)
        for cp in copies:
            cp.wait()

    lane_half = lax.broadcasted_iota(jnp.int32, (bs, lanes), 1) // bs

    def row_body(r, carry):
        row = step * rows_here + r
        own_pair = window[own_pos_ref[row]].astype(jnp.float32)
        spread = jnp.concatenate([own_pair, jnp.zeros_like(own_pair)], axis=0).T
        own_t = jnp.where(row % 2 == 0, spread[:bs], spread[bs:])[:, :bs]
        own_t = own_t.astype(jnp.bfloat16)
        results = []
        for s in range(slots):
            n = row * slots + s
            pair = window[pair_ref[n]]
            picked = jnp.where(lane_half == half_ref[n], pair, jnp.zeros_like(pair))
            product = jnp.dot(
                values_ref[r, s], picked, preferred_element_type=jnp.float32
            )
            product = jnp.where(live_ref[n] > 0, product, 0.0).astype(jnp.bfloat16)
            results.append(
                jnp.dot(own_t, product, preferred_element_type=jnp.float32)
            )
        for s in range(slots):
            t = target_ref[row * slots + s]
            acc_ref[t] = acc_ref[t] + results[s]
        return carry

    lax.fori_loop(0, rows_here, row_body, 0, unroll=4)

    @pl.when(step == pl.num_programs(0) - 1)
    def _():
        def pack(m, carry):
            first = acc_ref[2 * m]
            second = acc_ref[2 * m + 1]
            first = first + pltpu.roll(first, bs, 1)
            second = second + pltpu.roll(second, bs, 1)
            out_ref[m] = jnp.where(lane_half == 0, first, second)
            return carry

        lax.fori_loop(0, out_ref.shape[0], pack, 0)


def coarse_partial(pair, half, target, live, own_pos, fix, values, pieces, fixed, n_targets):
    panel_length, slots, bs, _ = values.shape
    rows_per_step = min(ROWS_PER_STEP, panel_length)
    grid = (panel_length // rows_per_step,)
    piece_rows, _, lanes = pieces[0].shape
    return pl.pallas_call(
        coarse_kernel,
        out_shape=jax.ShapeDtypeStruct((n_targets // 2, bs, lanes), jnp.float32),
        grid_spec=pltpu.PrefetchScalarGridSpec(
            num_scalar_prefetch=6,
            grid=grid,
            in_specs=[
                pl.BlockSpec((rows_per_step, slots, bs, bs), lambda i, *_: (i, 0, 0, 0)),
            ]
            + [pl.BlockSpec(memory_space=pl.ANY)] * (len(pieces) + len(fixed)),
            out_specs=pl.BlockSpec((n_targets // 2, bs, lanes), lambda i, *_: (0, 0, 0)),
            scratch_shapes=[
                pltpu.VMEM((n_targets, bs, lanes), jnp.float32),
                pltpu.VMEM((len(pieces) * piece_rows, bs, lanes), jnp.bfloat16),
                pltpu.SemaphoreType.DMA((len(pieces),)),
            ],
        ),
        compiler_params=pltpu.CompilerParams(
            dimension_semantics=("arbitrary",),
            vmem_limit_bytes=60 * 1024 * 1024,
        ),
    )(pair, half, target, live, own_pos, fix, values, *pieces, *fixed)


def local(block_values, block_columns, row_counts, prolong_blocks, aggregates):
    panel_length = row_counts.shape[0]
    slots_here = block_values.shape[1]
    slot_total = panel_length * slots_here
    block_size = block_values.shape[2]
    group_size = lax.axis_size("grp")
    panel_total = lax.axis_size("blk")
    coarse_count = CB * panel_total
    me = lax.axis_index("blk")
    group_me = lax.axis_index("grp")
    share_rows = prolong_blocks.shape[0]
    local_pairs = (
        prolong_blocks.reshape(share_rows // 2, 2, block_size, block_size)
        .transpose(0, 2, 1, 3)
        .reshape(share_rows // 2, block_size, 2 * block_size)
    )
    agg_row = (
        jnp.zeros((1, block_size, 2 * block_size), jnp.bfloat16)
        .at[0, 0, :share_rows]
        .set(aggregates.astype(jnp.bfloat16))
    )
    local_ext = jnp.concatenate([local_pairs, agg_row], axis=0)
    piece_rows = local_ext.shape[0]
    received = [local_ext]
    for k in range(1, group_size):
        received.append(
            lax.ppermute(
                local_ext, "grp", [(i, (i + k) % group_size) for i in range(group_size)]
            )
        )
    n = panel_total
    down_skip = ({(n - 1, 0)}, {(n - 1, 0), (0, 1)})
    up_skip = ({(0, n - 1)}, {(0, n - 1), (n - 1, n - 2)})

    def ring(piece, step, hop, full):
        skip = set() if full else (down_skip if step == 1 else up_skip)[hop]
        route = [((i - step) % n, i) for i in range(n)]
        route = [pair for pair in route if pair not in skip]
        return lax.ppermute(piece, "blk", route)

    down1 = [ring(piece, 1, 0, k == 0) for k, piece in enumerate(received)]
    up1 = [ring(piece, -1, 0, k == 0) for k, piece in enumerate(received)]
    down2 = [ring(piece, 1, 1, k == 0) for k, piece in enumerate(down1)]
    up2 = [ring(piece, -1, 1, k == 0) for k, piece in enumerate(up1)]
    pieces = down2 + down1 + received + up1 + up2
    low_end = me <= 1
    fix_first = jnp.where(low_end, down2[0], up2[0])
    fix_second = jnp.where(me == 0, down1[0], up1[0])
    fix_src = jnp.stack([fix_first, fix_second])
    ends = [0, 1, n - 2, n - 1]
    fixed = []
    for k in range(1, group_size):
        route = [
            (b * group_size + g, b * group_size + (g + k) % group_size)
            for b in ends
            for g in range(group_size)
        ]
        fixed.append(lax.ppermute(fix_src, ("blk", "grp"), route))
    minus = jnp.int32(-1)
    fix = jnp.stack([
        jnp.where(low_end, 0, minus),
        jnp.where(me == 0, 1, minus),
        minus,
        jnp.where(me == n - 1, 1, minus),
        jnp.where(me >= n - 2, 0, minus),
    ]).astype(jnp.int32)
    agg_rows = []
    for d in range(5):
        for k in range(group_size):
            row = pieces[d * group_size + k][share_rows // 2, 0, :share_rows]
            if k > 0:
                row = jnp.where(
                    fix[d] >= 0,
                    jnp.where(
                        fix[d] == 0,
                        fixed[k - 1][0, share_rows // 2, 0, :share_rows],
                        fixed[k - 1][1, share_rows // 2, 0, :share_rows],
                    ),
                    row,
                )
            agg_rows.append(row)
    flat_aggs = jnp.stack(agg_rows).astype(jnp.int32).reshape(-1)

    def placed(d, r):
        k = jnp.mod(group_me - r // share_rows, group_size)
        return d * group_size + k, r % share_rows

    wanted = block_columns.reshape(slot_total)
    column_panel = wanted // panel_length
    distance = jnp.mod(column_panel - me + 2, panel_total)
    piece_of, within = placed(distance, wanted % panel_length)
    window_pair = piece_of * piece_rows + within // 2
    fetched_aggs = jnp.take(flat_aggs, piece_of * share_rows + within, axis=0)
    own_piece, own_within = placed(2, jnp.arange(panel_length, dtype=jnp.int32))
    own_pos = own_piece * piece_rows + own_within // 2
    own_aggs = jnp.take(flat_aggs, own_piece * share_rows + own_within, axis=0)
    slot_ids = lax.axis_index("grp") * slots_here + jnp.arange(slots_here, dtype=jnp.int32)
    live = (slot_ids[None, :] < row_counts[:, None]).astype(jnp.int32).reshape(slot_total)
    local_coarse = own_aggs - me * CB
    target = fetched_aggs * CB + jnp.broadcast_to(
        local_coarse[:, None], (panel_length, slots_here)
    ).reshape(slot_total)
    summed = coarse_partial(
        window_pair.astype(jnp.int32),
        (within % 2).astype(jnp.int32),
        target.astype(jnp.int32),
        live,
        own_pos,
        fix,
        block_values,
        pieces,
        fixed,
        coarse_count * CB,
    )
    share = coarse_count // group_size
    summed = summed.reshape(group_size, share, CB // 2, block_size, 2 * block_size)
    total = jnp.take(summed, group_me, axis=0)
    for k in range(1, group_size):
        outgoing = jnp.take(summed, jnp.mod(group_me + k, group_size), axis=0)
        incoming = lax.ppermute(
            outgoing.astype(jnp.bfloat16),
            "grp",
            [(i, (i + k) % group_size) for i in range(group_size)],
        )
        total = total + incoming.astype(jnp.float32)
    total = total.reshape(share, CB // 2, block_size, 2, block_size)
    return total.transpose(0, 1, 3, 2, 4).reshape(share, CB, block_size, block_size)


def solution(mesh):
    return jax.shard_map(
        local,
        mesh=mesh,
        in_specs=(
            P("blk", "grp", None, None),
            P("blk", "grp"),
            P("blk"),
            P(("blk", "grp"), None, None),
            P(("blk", "grp")),
        ),
        out_specs=P("grp", "blk", None, None),
        check_vma=False,
    )
```

```python
import functools

import jax
import jax.numpy as jnp
from jax import lax
from jax.experimental import pallas as pl
from jax.experimental.pallas import tpu as pltpu
from jax.sharding import PartitionSpec as P

CB = 4
ROWS_PER_STEP = 48


def passed_along(block, axis, distance):
    devices = range(lax.axis_size(axis))
    route = [((i - distance) % len(devices), i) for i in devices]
    return lax.ppermute(block, axis, route)


def coarse_kernel(
    pair_ref, half_ref, target_ref, live_ref, own_pos_ref, fix_ref, values_ref, *rest
):
    out_ref, acc_ref, window, sems = rest[-4:]
    n_pieces = sems.shape[0]
    groups = n_pieces // 5
    pieces = rest[:n_pieces]
    fixed = rest[n_pieces:-4]
    step = pl.program_id(0)
    rows_here, slots, bs, _ = values_ref.shape
    piece_rows = pieces[0].shape[0]
    lanes = window.shape[2]

    @pl.when(step == 0)
    def _():
        copies = []
        for j, piece in enumerate(pieces):
            dst = window.at[pl.ds(j * piece_rows, piece_rows)]
            cp = pltpu.make_async_copy(piece, dst, sems.at[j])
            d, k = divmod(j, groups)
            if k == 0:
                cp.start()
            else:
                flag = fix_ref[d]

                @pl.when(flag < 0)
                def _():
                    cp.start()

                for slot in range(2):
                    @pl.when(flag == slot)
                    def _():
                        pltpu.make_async_copy(
                            fixed[k - 1].at[slot], dst, sems.at[j]
                        ).start()

            copies.append(cp)
        acc_ref[...] = jnp.zeros_like(acc_ref)
        for cp in copies:
            cp.wait()

    lane_half = lax.broadcasted_iota(jnp.int32, (bs, lanes), 1) // bs

    def row_body(r, carry):
        row = step * rows_here + r
        own_pair = window[own_pos_ref[row]].astype(jnp.float32)
        spread = jnp.concatenate([own_pair, jnp.zeros_like(own_pair)], axis=0).T
        own_t = jnp.where(row % 2 == 0, spread[:bs], spread[bs:])[:, :bs]
        own_t = own_t.astype(jnp.bfloat16)
        results = []
        for s in range(slots):
            n = row * slots + s
            pair = window[pair_ref[n]]
            picked = jnp.where(lane_half == half_ref[n], pair, jnp.zeros_like(pair))
            product = jnp.dot(
                values_ref[r, s], picked, preferred_element_type=jnp.float32
            )
            product = jnp.where(live_ref[n] > 0, product, 0.0).astype(jnp.bfloat16)
            results.append(
                jnp.dot(own_t, product, preferred_element_type=jnp.float32)
            )
        for s in range(slots):
            t = target_ref[row * slots + s]
            acc_ref[t] = acc_ref[t] + results[s]
        return carry

    lax.fori_loop(0, rows_here, row_body, 0, unroll=8)

    @pl.when(step == pl.num_programs(0) - 1)
    def _():
        def pack(m, carry):
            first = acc_ref[2 * m]
            second = acc_ref[2 * m + 1]
            first = first + pltpu.roll(first, bs, 1)
            second = second + pltpu.roll(second, bs, 1)
            out_ref[m] = jnp.where(lane_half == 0, first, second)
            return carry

        lax.fori_loop(0, out_ref.shape[0], pack, 0)


def coarse_partial(pair, half, target, live, own_pos, fix, values, pieces, fixed, n_targets):
    panel_length, slots, bs, _ = values.shape
    rows_per_step = min(ROWS_PER_STEP, panel_length)
    grid = (panel_length // rows_per_step,)
    piece_rows, _, lanes = pieces[0].shape
    return pl.pallas_call(
        coarse_kernel,
        out_shape=jax.ShapeDtypeStruct((n_targets // 2, bs, lanes), jnp.float32),
        grid_spec=pltpu.PrefetchScalarGridSpec(
            num_scalar_prefetch=6,
            grid=grid,
            in_specs=[
                pl.BlockSpec((rows_per_step, slots, bs, bs), lambda i, *_: (i, 0, 0, 0)),
            ]
            + [pl.BlockSpec(memory_space=pl.ANY)] * (len(pieces) + len(fixed)),
            out_specs=pl.BlockSpec((n_targets // 2, bs, lanes), lambda i, *_: (0, 0, 0)),
            scratch_shapes=[
                pltpu.VMEM((n_targets, bs, lanes), jnp.float32),
                pltpu.VMEM((len(pieces) * piece_rows, bs, lanes), jnp.bfloat16),
                pltpu.SemaphoreType.DMA((len(pieces),)),
            ],
        ),
        compiler_params=pltpu.CompilerParams(
            dimension_semantics=("arbitrary",),
            vmem_limit_bytes=60 * 1024 * 1024,
        ),
    )(pair, half, target, live, own_pos, fix, values, *pieces, *fixed)


def local(block_values, block_columns, row_counts, prolong_blocks, aggregates):
    panel_length = row_counts.shape[0]
    slots_here = block_values.shape[1]
    slot_total = panel_length * slots_here
    block_size = block_values.shape[2]
    group_size = lax.axis_size("grp")
    panel_total = lax.axis_size("blk")
    coarse_count = CB * panel_total
    me = lax.axis_index("blk")
    group_me = lax.axis_index("grp")
    share_rows = prolong_blocks.shape[0]
    local_pairs = (
        prolong_blocks.reshape(share_rows // 2, 2, block_size, block_size)
        .transpose(0, 2, 1, 3)
        .reshape(share_rows // 2, block_size, 2 * block_size)
    )
    agg_row = (
        jnp.zeros((1, block_size, 2 * block_size), jnp.bfloat16)
        .at[0, 0, :share_rows]
        .set(aggregates.astype(jnp.bfloat16))
    )
    local_ext = jnp.concatenate([local_pairs, agg_row], axis=0)
    piece_rows = local_ext.shape[0]
    received = [local_ext]
    for k in range(1, group_size):
        received.append(
            lax.ppermute(
                local_ext, "grp", [(i, (i + k) % group_size) for i in range(group_size)]
            )
        )
    n = panel_total
    down_skip = ({(n - 1, 0)}, {(n - 1, 0), (0, 1)})
    up_skip = ({(0, n - 1)}, {(0, n - 1), (n - 1, n - 2)})

    def ring(piece, step, hop, full):
        skip = set() if full else (down_skip if step == 1 else up_skip)[hop]
        route = [((i - step) % n, i) for i in range(n)]
        route = [pair for pair in route if pair not in skip]
        return lax.ppermute(piece, "blk", route)

    down1 = [ring(piece, 1, 0, k == 0) for k, piece in enumerate(received)]
    up1 = [ring(piece, -1, 0, k == 0) for k, piece in enumerate(received)]
    down2 = [ring(piece, 1, 1, k == 0) for k, piece in enumerate(down1)]
    up2 = [ring(piece, -1, 1, k == 0) for k, piece in enumerate(up1)]
    pieces = down2 + down1 + received + up1 + up2
    low_end = me <= 1
    fix_first = jnp.where(low_end, down2[0], up2[0])
    fix_second = jnp.where(me == 0, down1[0], up1[0])
    fix_src = jnp.stack([fix_first, fix_second])
    ends = [0, 1, n - 2, n - 1]
    fixed = []
    for k in range(1, group_size):
        route = [
            (b * group_size + g, b * group_size + (g + k) % group_size)
            for b in ends
            for g in range(group_size)
        ]
        fixed.append(lax.ppermute(fix_src, ("blk", "grp"), route))
    minus = jnp.int32(-1)
    fix = jnp.stack([
        jnp.where(low_end, 0, minus),
        jnp.where(me == 0, 1, minus),
        minus,
        jnp.where(me == n - 1, 1, minus),
        jnp.where(me >= n - 2, 0, minus),
    ]).astype(jnp.int32)
    agg_rows = []
    for d in range(5):
        for k in range(group_size):
            row = pieces[d * group_size + k][share_rows // 2, 0, :share_rows]
            if k > 0:
                row = jnp.where(
                    fix[d] >= 0,
                    jnp.where(
                        fix[d] == 0,
                        fixed[k - 1][0, share_rows // 2, 0, :share_rows],
                        fixed[k - 1][1, share_rows // 2, 0, :share_rows],
                    ),
                    row,
                )
            agg_rows.append(row)
    flat_aggs = jnp.stack(agg_rows).astype(jnp.int32).reshape(-1)

    def placed(d, r):
        k = jnp.mod(group_me - r // share_rows, group_size)
        return d * group_size + k, r % share_rows

    wanted = block_columns.reshape(slot_total)
    column_panel = wanted // panel_length
    distance = jnp.mod(column_panel - me + 2, panel_total)
    piece_of, within = placed(distance, wanted % panel_length)
    window_pair = piece_of * piece_rows + within // 2
    fetched_aggs = jnp.take(flat_aggs, piece_of * share_rows + within, axis=0)
    own_piece, own_within = placed(2, jnp.arange(panel_length, dtype=jnp.int32))
    own_pos = own_piece * piece_rows + own_within // 2
    own_aggs = jnp.take(flat_aggs, own_piece * share_rows + own_within, axis=0)
    slot_ids = lax.axis_index("grp") * slots_here + jnp.arange(slots_here, dtype=jnp.int32)
    live = (slot_ids[None, :] < row_counts[:, None]).astype(jnp.int32).reshape(slot_total)
    local_coarse = own_aggs - me * CB
    target = fetched_aggs * CB + jnp.broadcast_to(
        local_coarse[:, None], (panel_length, slots_here)
    ).reshape(slot_total)
    summed = coarse_partial(
        window_pair.astype(jnp.int32),
        (within % 2).astype(jnp.int32),
        target.astype(jnp.int32),
        live,
        own_pos,
        fix,
        block_values,
        pieces,
        fixed,
        coarse_count * CB,
    )
    share = coarse_count // group_size
    summed = summed.reshape(group_size, share, CB // 2, block_size, 2 * block_size)
    total = jnp.take(summed, group_me, axis=0)
    for k in range(1, group_size):
        outgoing = jnp.take(summed, jnp.mod(group_me + k, group_size), axis=0)
        incoming = lax.ppermute(
            outgoing.astype(jnp.bfloat16),
            "grp",
            [(i, (i + k) % group_size) for i in range(group_size)],
        )
        total = total + incoming.astype(jnp.float32)
    total = total.reshape(share, CB // 2, block_size, 2, block_size)
    return total.transpose(0, 1, 3, 2, 4).reshape(share, CB, block_size, block_size)


def solution(mesh):
    return jax.shard_map(
        local,
        mesh=mesh,
        in_specs=(
            P("blk", "grp", None, None),
            P("blk", "grp"),
            P("blk"),
            P(("blk", "grp"), None, None),
            P(("blk", "grp")),
        ),
        out_specs=P("grp", "blk", None, None),
        check_vma=False,
    )
```

```python
import functools

import jax
import jax.numpy as jnp
from jax import lax
from jax.experimental import pallas as pl
from jax.experimental.pallas import tpu as pltpu
from jax.sharding import PartitionSpec as P

CB = 4
ROWS_PER_STEP = 48


def passed_along(block, axis, distance):
    devices = range(lax.axis_size(axis))
    route = [((i - distance) % len(devices), i) for i in devices]
    return lax.ppermute(block, axis, route)


def coarse_kernel(
    pair_ref, half_ref, target_ref, live_ref, own_pos_ref, fix_ref, values_ref, *rest
):
    out_ref, acc_ref, window, sems = rest[-4:]
    n_pieces = sems.shape[0]
    groups = n_pieces // 5
    pieces = rest[:n_pieces]
    fixed = rest[n_pieces:-4]
    step = pl.program_id(0)
    rows_here, slots, bs, _ = values_ref.shape
    piece_rows = pieces[0].shape[0]
    lanes = window.shape[2]

    @pl.when(step == 0)
    def _():
        copies = []
        for j, piece in enumerate(pieces):
            dst = window.at[pl.ds(j * piece_rows, piece_rows)]
            cp = pltpu.make_async_copy(piece, dst, sems.at[j])
            d, k = divmod(j, groups)
            if k == 0:
                cp.start()
            else:
                flag = fix_ref[d]

                @pl.when(flag < 0)
                def _():
                    cp.start()

                for slot in range(2):
                    @pl.when(flag == slot)
                    def _():
                        pltpu.make_async_copy(
                            fixed[k - 1].at[slot], dst, sems.at[j]
                        ).start()

            copies.append(cp)
        acc_ref[...] = jnp.zeros_like(acc_ref)
        for cp in copies:
            cp.wait()

    lane_half = lax.broadcasted_iota(jnp.int32, (bs, lanes), 1) // bs

    def row_body(r, carry):
        row = step * rows_here + r
        own_pair = window[own_pos_ref[row]].astype(jnp.float32)
        spread = jnp.concatenate([own_pair, jnp.zeros_like(own_pair)], axis=0).T
        own_t = jnp.where(row % 2 == 0, spread[:bs], spread[bs:])[:, :bs]
        own_t = own_t.astype(jnp.bfloat16)
        results = []
        for s in range(slots):
            n = row * slots + s
            pair = window[pair_ref[n]]
            picked = jnp.where(lane_half == half_ref[n], pair, jnp.zeros_like(pair))
            product = jnp.dot(
                values_ref[r, s], picked, preferred_element_type=jnp.float32
            )
            product = jnp.where(live_ref[n] > 0, product, 0.0).astype(jnp.bfloat16)
            results.append(
                jnp.dot(own_t, product, preferred_element_type=jnp.float32)
            )
        for s in range(slots):
            t = target_ref[row * slots + s]
            acc_ref[t] = acc_ref[t] + results[s]
        return carry

    lax.fori_loop(0, rows_here, row_body, 0, unroll=16)

    @pl.when(step == pl.num_programs(0) - 1)
    def _():
        def pack(m, carry):
            first = acc_ref[2 * m]
            second = acc_ref[2 * m + 1]
            first = first + pltpu.roll(first, bs, 1)
            second = second + pltpu.roll(second, bs, 1)
            out_ref[m] = jnp.where(lane_half == 0, first, second)
            return carry

        lax.fori_loop(0, out_ref.shape[0], pack, 0)


def coarse_partial(pair, half, target, live, own_pos, fix, values, pieces, fixed, n_targets):
    panel_length, slots, bs, _ = values.shape
    rows_per_step = min(ROWS_PER_STEP, panel_length)
    grid = (panel_length // rows_per_step,)
    piece_rows, _, lanes = pieces[0].shape
    return pl.pallas_call(
        coarse_kernel,
        out_shape=jax.ShapeDtypeStruct((n_targets // 2, bs, lanes), jnp.float32),
        grid_spec=pltpu.PrefetchScalarGridSpec(
            num_scalar_prefetch=6,
            grid=grid,
            in_specs=[
                pl.BlockSpec((rows_per_step, slots, bs, bs), lambda i, *_: (i, 0, 0, 0)),
            ]
            + [pl.BlockSpec(memory_space=pl.ANY)] * (len(pieces) + len(fixed)),
            out_specs=pl.BlockSpec((n_targets // 2, bs, lanes), lambda i, *_: (0, 0, 0)),
            scratch_shapes=[
                pltpu.VMEM((n_targets, bs, lanes), jnp.float32),
                pltpu.VMEM((len(pieces) * piece_rows, bs, lanes), jnp.bfloat16),
                pltpu.SemaphoreType.DMA((len(pieces),)),
            ],
        ),
        compiler_params=pltpu.CompilerParams(
            dimension_semantics=("arbitrary",),
            vmem_limit_bytes=60 * 1024 * 1024,
        ),
    )(pair, half, target, live, own_pos, fix, values, *pieces, *fixed)


def local(block_values, block_columns, row_counts, prolong_blocks, aggregates):
    panel_length = row_counts.shape[0]
    slots_here = block_values.shape[1]
    slot_total = panel_length * slots_here
    block_size = block_values.shape[2]
    group_size = lax.axis_size("grp")
    panel_total = lax.axis_size("blk")
    coarse_count = CB * panel_total
    me = lax.axis_index("blk")
    group_me = lax.axis_index("grp")
    share_rows = prolong_blocks.shape[0]
    local_pairs = (
        prolong_blocks.reshape(share_rows // 2, 2, block_size, block_size)
        .transpose(0, 2, 1, 3)
        .reshape(share_rows // 2, block_size, 2 * block_size)
    )
    agg_row = (
        jnp.zeros((1, block_size, 2 * block_size), jnp.bfloat16)
        .at[0, 0, :share_rows]
        .set(aggregates.astype(jnp.bfloat16))
    )
    local_ext = jnp.concatenate([local_pairs, agg_row], axis=0)
    piece_rows = local_ext.shape[0]
    received = [local_ext]
    for k in range(1, group_size):
        received.append(
            lax.ppermute(
                local_ext, "grp", [(i, (i + k) % group_size) for i in range(group_size)]
            )
        )
    n = panel_total
    down_skip = ({(n - 1, 0)}, {(n - 1, 0), (0, 1)})
    up_skip = ({(0, n - 1)}, {(0, n - 1), (n - 1, n - 2)})

    def ring(piece, step, hop, full):
        skip = set() if full else (down_skip if step == 1 else up_skip)[hop]
        route = [((i - step) % n, i) for i in range(n)]
        route = [pair for pair in route if pair not in skip]
        return lax.ppermute(piece, "blk", route)

    down1 = [ring(piece, 1, 0, k == 0) for k, piece in enumerate(received)]
    up1 = [ring(piece, -1, 0, k == 0) for k, piece in enumerate(received)]
    down2 = [ring(piece, 1, 1, k == 0) for k, piece in enumerate(down1)]
    up2 = [ring(piece, -1, 1, k == 0) for k, piece in enumerate(up1)]
    pieces = down2 + down1 + received + up1 + up2
    low_end = me <= 1
    fix_first = jnp.where(low_end, down2[0], up2[0])
    fix_second = jnp.where(me == 0, down1[0], up1[0])
    fix_src = jnp.stack([fix_first, fix_second])
    ends = [0, 1, n - 2, n - 1]
    fixed = []
    for k in range(1, group_size):
        route = [
            (b * group_size + g, b * group_size + (g + k) % group_size)
            for b in ends
            for g in range(group_size)
        ]
        fixed.append(lax.ppermute(fix_src, ("blk", "grp"), route))
    minus = jnp.int32(-1)
    fix = jnp.stack([
        jnp.where(low_end, 0, minus),
        jnp.where(me == 0, 1, minus),
        minus,
        jnp.where(me == n - 1, 1, minus),
        jnp.where(me >= n - 2, 0, minus),
    ]).astype(jnp.int32)
    agg_rows = []
    for d in range(5):
        for k in range(group_size):
            row = pieces[d * group_size + k][share_rows // 2, 0, :share_rows]
            if k > 0:
                row = jnp.where(
                    fix[d] >= 0,
                    jnp.where(
                        fix[d] == 0,
                        fixed[k - 1][0, share_rows // 2, 0, :share_rows],
                        fixed[k - 1][1, share_rows // 2, 0, :share_rows],
                    ),
                    row,
                )
            agg_rows.append(row)
    flat_aggs = jnp.stack(agg_rows).astype(jnp.int32).reshape(-1)

    def placed(d, r):
        k = jnp.mod(group_me - r // share_rows, group_size)
        return d * group_size + k, r % share_rows

    wanted = block_columns.reshape(slot_total)
    column_panel = wanted // panel_length
    distance = jnp.mod(column_panel - me + 2, panel_total)
    piece_of, within = placed(distance, wanted % panel_length)
    window_pair = piece_of * piece_rows + within // 2
    fetched_aggs = jnp.take(flat_aggs, piece_of * share_rows + within, axis=0)
    own_piece, own_within = placed(2, jnp.arange(panel_length, dtype=jnp.int32))
    own_pos = own_piece * piece_rows + own_within // 2
    own_aggs = jnp.take(flat_aggs, own_piece * share_rows + own_within, axis=0)
    slot_ids = lax.axis_index("grp") * slots_here + jnp.arange(slots_here, dtype=jnp.int32)
    live = (slot_ids[None, :] < row_counts[:, None]).astype(jnp.int32).reshape(slot_total)
    local_coarse = own_aggs - me * CB
    target = fetched_aggs * CB + jnp.broadcast_to(
        local_coarse[:, None], (panel_length, slots_here)
    ).reshape(slot_total)
    summed = coarse_partial(
        window_pair.astype(jnp.int32),
        (within % 2).astype(jnp.int32),
        target.astype(jnp.int32),
        live,
        own_pos,
        fix,
        block_values,
        pieces,
        fixed,
        coarse_count * CB,
    )
    share = coarse_count // group_size
    summed = summed.reshape(group_size, share, CB // 2, block_size, 2 * block_size)
    total = jnp.take(summed, group_me, axis=0)
    for k in range(1, group_size):
        outgoing = jnp.take(summed, jnp.mod(group_me + k, group_size), axis=0)
        incoming = lax.ppermute(
            outgoing.astype(jnp.bfloat16),
            "grp",
            [(i, (i + k) % group_size) for i in range(group_size)],
        )
        total = total + incoming.astype(jnp.float32)
    total = total.reshape(share, CB // 2, block_size, 2, block_size)
    return total.transpose(0, 1, 3, 2, 4).reshape(share, CB, block_size, block_size)


def solution(mesh):
    return jax.shard_map(
        local,
        mesh=mesh,
        in_specs=(
            P("blk", "grp", None, None),
            P("blk", "grp"),
            P("blk"),
            P(("blk", "grp"), None, None),
            P(("blk", "grp")),
        ),
        out_specs=P("grp", "blk", None, None),
        check_vma=False,
    )
```

```python
import functools

import jax
import jax.numpy as jnp
from jax import lax
from jax.experimental import pallas as pl
from jax.experimental.pallas import tpu as pltpu
from jax.sharding import PartitionSpec as P

CB = 4
ROWS_PER_STEP = 48


def passed_along(block, axis, distance):
    devices = range(lax.axis_size(axis))
    route = [((i - distance) % len(devices), i) for i in devices]
    return lax.ppermute(block, axis, route)


def coarse_kernel(
    pair_ref, half_ref, target_ref, live_ref, own_pos_ref, fix_ref, values_ref, *rest
):
    window, sems = rest[-2:]
    n_pieces = sems.shape[0]
    groups = n_pieces // 5
    pieces = rest[:n_pieces]
    n_fixed = groups - 1
    fixed = rest[n_pieces : n_pieces + n_fixed]
    out_ref = rest[n_pieces + n_fixed]
    accs = rest[n_pieces + n_fixed + 1 : -2]
    step = pl.program_id(0)
    rows_here, slots, bs, _ = values_ref.shape
    piece_rows = pieces[0].shape[0]
    lanes = window.shape[2]

    @pl.when(step == 0)
    def _():
        copies = []
        for j, piece in enumerate(pieces):
            dst = window.at[pl.ds(j * piece_rows, piece_rows)]
            cp = pltpu.make_async_copy(piece, dst, sems.at[j])
            d, k = divmod(j, groups)
            if k == 0:
                cp.start()
            else:
                flag = fix_ref[d]

                @pl.when(flag < 0)
                def _():
                    cp.start()

                for slot in range(2):
                    @pl.when(flag == slot)
                    def _():
                        pltpu.make_async_copy(
                            fixed[k - 1].at[slot], dst, sems.at[j]
                        ).start()

            copies.append(cp)
        for acc_ref in accs:
            acc_ref[...] = jnp.zeros_like(acc_ref)
        for cp in copies:
            cp.wait()

    lane_half = lax.broadcasted_iota(jnp.int32, (bs, lanes), 1) // bs

    def row_body(r, carry):
        row = step * rows_here + r
        own_pair = window[own_pos_ref[row]].astype(jnp.float32)
        spread = jnp.concatenate([own_pair, jnp.zeros_like(own_pair)], axis=0).T
        own_t = jnp.where(row % 2 == 0, spread[:bs], spread[bs:])[:, :bs]
        own_t = own_t.astype(jnp.bfloat16)
        results = []
        for s in range(slots):
            n = row * slots + s
            pair = window[pair_ref[n]]
            picked = jnp.where(lane_half == half_ref[n], pair, jnp.zeros_like(pair))
            product = jnp.dot(
                values_ref[r, s], picked, preferred_element_type=jnp.float32
            )
            product = jnp.where(live_ref[n] > 0, product, 0.0).astype(jnp.bfloat16)
            results.append(
                jnp.dot(own_t, product, preferred_element_type=jnp.float32)
            )
        for s in range(slots):
            t = target_ref[row * slots + s]
            accs[s][t] = accs[s][t] + results[s]
        return carry

    lax.fori_loop(0, rows_here, row_body, 0, unroll=16)

    @pl.when(step == pl.num_programs(0) - 1)
    def _():
        def pack(m, carry):
            first = sum(acc_ref[2 * m] for acc_ref in accs)
            second = sum(acc_ref[2 * m + 1] for acc_ref in accs)
            first = first + pltpu.roll(first, bs, 1)
            second = second + pltpu.roll(second, bs, 1)
            out_ref[m] = jnp.where(lane_half == 0, first, second)
            return carry

        lax.fori_loop(0, out_ref.shape[0], pack, 0)


def coarse_partial(pair, half, target, live, own_pos, fix, values, pieces, fixed, n_targets):
    panel_length, slots, bs, _ = values.shape
    rows_per_step = min(ROWS_PER_STEP, panel_length)
    grid = (panel_length // rows_per_step,)
    piece_rows, _, lanes = pieces[0].shape
    return pl.pallas_call(
        coarse_kernel,
        out_shape=jax.ShapeDtypeStruct((n_targets // 2, bs, lanes), jnp.float32),
        grid_spec=pltpu.PrefetchScalarGridSpec(
            num_scalar_prefetch=6,
            grid=grid,
            in_specs=[
                pl.BlockSpec((rows_per_step, slots, bs, bs), lambda i, *_: (i, 0, 0, 0)),
            ]
            + [pl.BlockSpec(memory_space=pl.ANY)] * (len(pieces) + len(fixed)),
            out_specs=pl.BlockSpec((n_targets // 2, bs, lanes), lambda i, *_: (0, 0, 0)),
            scratch_shapes=[pltpu.VMEM((n_targets, bs, lanes), jnp.float32)] * slots
            + [
                pltpu.VMEM((len(pieces) * piece_rows, bs, lanes), jnp.bfloat16),
                pltpu.SemaphoreType.DMA((len(pieces),)),
            ],
        ),
        compiler_params=pltpu.CompilerParams(
            dimension_semantics=("arbitrary",),
            vmem_limit_bytes=60 * 1024 * 1024,
        ),
    )(pair, half, target, live, own_pos, fix, values, *pieces, *fixed)


def local(block_values, block_columns, row_counts, prolong_blocks, aggregates):
    panel_length = row_counts.shape[0]
    slots_here = block_values.shape[1]
    slot_total = panel_length * slots_here
    block_size = block_values.shape[2]
    group_size = lax.axis_size("grp")
    panel_total = lax.axis_size("blk")
    coarse_count = CB * panel_total
    me = lax.axis_index("blk")
    group_me = lax.axis_index("grp")
    share_rows = prolong_blocks.shape[0]
    local_pairs = (
        prolong_blocks.reshape(share_rows // 2, 2, block_size, block_size)
        .transpose(0, 2, 1, 3)
        .reshape(share_rows // 2, block_size, 2 * block_size)
    )
    agg_row = (
        jnp.zeros((1, block_size, 2 * block_size), jnp.bfloat16)
        .at[0, 0, :share_rows]
        .set(aggregates.astype(jnp.bfloat16))
    )
    local_ext = jnp.concatenate([local_pairs, agg_row], axis=0)
    piece_rows = local_ext.shape[0]
    received = [local_ext]
    for k in range(1, group_size):
        received.append(
            lax.ppermute(
                local_ext, "grp", [(i, (i + k) % group_size) for i in range(group_size)]
            )
        )
    n = panel_total
    down_skip = ({(n - 1, 0)}, {(n - 1, 0), (0, 1)})
    up_skip = ({(0, n - 1)}, {(0, n - 1), (n - 1, n - 2)})

    def ring(piece, step, hop, full):
        skip = set() if full else (down_skip if step == 1 else up_skip)[hop]
        route = [((i - step) % n, i) for i in range(n)]
        route = [pair for pair in route if pair not in skip]
        return lax.ppermute(piece, "blk", route)

    down1 = [ring(piece, 1, 0, k == 0) for k, piece in enumerate(received)]
    up1 = [ring(piece, -1, 0, k == 0) for k, piece in enumerate(received)]
    down2 = [ring(piece, 1, 1, k == 0) for k, piece in enumerate(down1)]
    up2 = [ring(piece, -1, 1, k == 0) for k, piece in enumerate(up1)]
    pieces = down2 + down1 + received + up1 + up2
    low_end = me <= 1
    fix_first = jnp.where(low_end, down2[0], up2[0])
    fix_second = jnp.where(me == 0, down1[0], up1[0])
    fix_src = jnp.stack([fix_first, fix_second])
    ends = [0, 1, n - 2, n - 1]
    fixed = []
    for k in range(1, group_size):
        route = [
            (b * group_size + g, b * group_size + (g + k) % group_size)
            for b in ends
            for g in range(group_size)
        ]
        fixed.append(lax.ppermute(fix_src, ("blk", "grp"), route))
    minus = jnp.int32(-1)
    fix = jnp.stack([
        jnp.where(low_end, 0, minus),
        jnp.where(me == 0, 1, minus),
        minus,
        jnp.where(me == n - 1, 1, minus),
        jnp.where(me >= n - 2, 0, minus),
    ]).astype(jnp.int32)
    agg_rows = []
    for d in range(5):
        for k in range(group_size):
            row = pieces[d * group_size + k][share_rows // 2, 0, :share_rows]
            if k > 0:
                row = jnp.where(
                    fix[d] >= 0,
                    jnp.where(
                        fix[d] == 0,
                        fixed[k - 1][0, share_rows // 2, 0, :share_rows],
                        fixed[k - 1][1, share_rows // 2, 0, :share_rows],
                    ),
                    row,
                )
            agg_rows.append(row)
    flat_aggs = jnp.stack(agg_rows).astype(jnp.int32).reshape(-1)

    def placed(d, r):
        k = jnp.mod(group_me - r // share_rows, group_size)
        return d * group_size + k, r % share_rows

    wanted = block_columns.reshape(slot_total)
    column_panel = wanted // panel_length
    distance = jnp.mod(column_panel - me + 2, panel_total)
    piece_of, within = placed(distance, wanted % panel_length)
    window_pair = piece_of * piece_rows + within // 2
    fetched_aggs = jnp.take(flat_aggs, piece_of * share_rows + within, axis=0)
    own_piece, own_within = placed(2, jnp.arange(panel_length, dtype=jnp.int32))
    own_pos = own_piece * piece_rows + own_within // 2
    own_aggs = jnp.take(flat_aggs, own_piece * share_rows + own_within, axis=0)
    slot_ids = lax.axis_index("grp") * slots_here + jnp.arange(slots_here, dtype=jnp.int32)
    live = (slot_ids[None, :] < row_counts[:, None]).astype(jnp.int32).reshape(slot_total)
    local_coarse = own_aggs - me * CB
    target = fetched_aggs * CB + jnp.broadcast_to(
        local_coarse[:, None], (panel_length, slots_here)
    ).reshape(slot_total)
    summed = coarse_partial(
        window_pair.astype(jnp.int32),
        (within % 2).astype(jnp.int32),
        target.astype(jnp.int32),
        live,
        own_pos,
        fix,
        block_values,
        pieces,
        fixed,
        coarse_count * CB,
    )
    share = coarse_count // group_size
    summed = summed.reshape(group_size, share, CB // 2, block_size, 2 * block_size)
    total = jnp.take(summed, group_me, axis=0)
    for k in range(1, group_size):
        outgoing = jnp.take(summed, jnp.mod(group_me + k, group_size), axis=0)
        incoming = lax.ppermute(
            outgoing.astype(jnp.bfloat16),
            "grp",
            [(i, (i + k) % group_size) for i in range(group_size)],
        )
        total = total + incoming.astype(jnp.float32)
    total = total.reshape(share, CB // 2, block_size, 2, block_size)
    return total.transpose(0, 1, 3, 2, 4).reshape(share, CB, block_size, block_size)


def solution(mesh):
    return jax.shard_map(
        local,
        mesh=mesh,
        in_specs=(
            P("blk", "grp", None, None),
            P("blk", "grp"),
            P("blk"),
            P(("blk", "grp"), None, None),
            P(("blk", "grp")),
        ),
        out_specs=P("grp", "blk", None, None),
        check_vma=False,
    )
```

```python
import functools

import jax
import jax.numpy as jnp
from jax import lax
from jax.experimental import pallas as pl
from jax.experimental.pallas import tpu as pltpu
from jax.sharding import PartitionSpec as P

CB = 4
ROWS_PER_STEP = 48


def passed_along(block, axis, distance):
    devices = range(lax.axis_size(axis))
    route = [((i - distance) % len(devices), i) for i in devices]
    return lax.ppermute(block, axis, route)


def coarse_kernel(
    pair_ref, half_ref, target_ref, live_ref, own_pos_ref, fix_ref, values_ref, *rest
):
    window, sems = rest[-2:]
    n_pieces = sems.shape[0]
    groups = n_pieces // 5
    pieces = rest[:n_pieces]
    n_fixed = groups - 1
    fixed = rest[n_pieces : n_pieces + n_fixed]
    out_ref = rest[n_pieces + n_fixed]
    accs = rest[n_pieces + n_fixed + 1 : -2]
    step = pl.program_id(0)
    rows_here, slots, bs, _ = values_ref.shape
    piece_rows = pieces[0].shape[0]
    lanes = window.shape[2]

    @pl.when(step == 0)
    def _():
        copies = []
        for j, piece in enumerate(pieces):
            dst = window.at[pl.ds(j * piece_rows, piece_rows)]
            cp = pltpu.make_async_copy(piece, dst, sems.at[j])
            d, k = divmod(j, groups)
            if k == 0:
                cp.start()
            else:
                flag = fix_ref[d]

                @pl.when(flag < 0)
                def _():
                    cp.start()

                for slot in range(2):
                    @pl.when(flag == slot)
                    def _():
                        pltpu.make_async_copy(
                            fixed[k - 1].at[slot], dst, sems.at[j]
                        ).start()

            copies.append(cp)
        for acc_ref in accs:
            acc_ref[...] = jnp.zeros_like(acc_ref)
        for cp in copies:
            cp.wait()

    lane_half = lax.broadcasted_iota(jnp.int32, (bs, lanes), 1) // bs

    def row_body(r, carry):
        row = step * rows_here + r
        own_pair = window[own_pos_ref[row]].astype(jnp.float32)
        spread = jnp.concatenate([own_pair, jnp.zeros_like(own_pair)], axis=0).T
        own_t = jnp.where(row % 2 == 0, spread[:bs], spread[bs:])[:, :bs]
        own_t = own_t.astype(jnp.bfloat16)
        results = []
        for s in range(slots):
            n = row * slots + s
            pair = window[pair_ref[n]]
            picked = jnp.where(lane_half == half_ref[n], pair, jnp.zeros_like(pair))
            product = jnp.dot(
                values_ref[r, s], picked, preferred_element_type=jnp.float32
            )
            product = jnp.where(live_ref[n] > 0, product, 0.0).astype(jnp.bfloat16)
            results.append(
                jnp.dot(own_t, product, preferred_element_type=jnp.float32)
            )
        for s in range(slots):
            t = target_ref[row * slots + s]
            accs[s][t] = accs[s][t] + results[s]
        return carry

    lax.fori_loop(0, rows_here, row_body, 0, unroll=16)

    @pl.when(step == pl.num_programs(0) - 1)
    def _():
        def pack(m, carry):
            first = sum(acc_ref[2 * m] for acc_ref in accs)
            second = sum(acc_ref[2 * m + 1] for acc_ref in accs)
            first = first + pltpu.roll(first, bs, 1)
            second = second + pltpu.roll(second, bs, 1)
            out_ref[m] = jnp.where(lane_half == 0, first, second)
            return carry

        lax.fori_loop(0, out_ref.shape[0], pack, 0)


def coarse_partial(pair, half, target, live, own_pos, fix, values, pieces, fixed, n_targets):
    panel_length, slots, bs, _ = values.shape
    rows_per_step = min(ROWS_PER_STEP, panel_length)
    grid = (panel_length // rows_per_step,)
    piece_rows, _, lanes = pieces[0].shape
    return pl.pallas_call(
        coarse_kernel,
        out_shape=jax.ShapeDtypeStruct((n_targets // 2, bs, lanes), jnp.float32),
        grid_spec=pltpu.PrefetchScalarGridSpec(
            num_scalar_prefetch=6,
            grid=grid,
            in_specs=[
                pl.BlockSpec((rows_per_step, slots, bs, bs), lambda i, *_: (i, 0, 0, 0)),
            ]
            + [pl.BlockSpec(memory_space=pl.ANY)] * (len(pieces) + len(fixed)),
            out_specs=pl.BlockSpec((n_targets // 2, bs, lanes), lambda i, *_: (0, 0, 0)),
            scratch_shapes=[pltpu.VMEM((n_targets, bs, lanes), jnp.float32)] * slots
            + [
                pltpu.VMEM((len(pieces) * piece_rows, bs, lanes), jnp.bfloat16),
                pltpu.SemaphoreType.DMA((len(pieces),)),
            ],
        ),
        compiler_params=pltpu.CompilerParams(
            dimension_semantics=("arbitrary",),
            vmem_limit_bytes=60 * 1024 * 1024,
        ),
    )(pair, half, target, live, own_pos, fix, values, *pieces, *fixed)


def local(block_values, block_columns, row_counts, prolong_blocks, aggregates):
    panel_length = row_counts.shape[0]
    slots_here = block_values.shape[1]
    slot_total = panel_length * slots_here
    block_size = block_values.shape[2]
    group_size = lax.axis_size("grp")
    panel_total = lax.axis_size("blk")
    coarse_count = CB * panel_total
    me = lax.axis_index("blk")
    group_me = lax.axis_index("grp")
    share_rows = prolong_blocks.shape[0]
    local_pairs = (
        prolong_blocks.reshape(share_rows // 2, 2, block_size, block_size)
        .transpose(0, 2, 1, 3)
        .reshape(share_rows // 2, block_size, 2 * block_size)
    )
    agg_row = (
        jnp.zeros((1, block_size, 2 * block_size), jnp.bfloat16)
        .at[0, 0, :share_rows]
        .set(aggregates.astype(jnp.bfloat16))
    )
    local_ext = jnp.concatenate([local_pairs, agg_row], axis=0)
    piece_rows = local_ext.shape[0]
    received = [local_ext]
    for k in range(1, group_size):
        received.append(
            lax.ppermute(
                local_ext, "grp", [(i, (i + k) % group_size) for i in range(group_size)]
            )
        )
    n = panel_total
    down_skip = ({(n - 1, 0)}, {(n - 1, 0), (0, 1)})
    up_skip = ({(0, n - 1)}, {(0, n - 1), (n - 1, n - 2)})

    def ring(piece, step, hop, full):
        skip = set() if full else (down_skip if step == 1 else up_skip)[hop]
        route = [((i - step) % n, i) for i in range(n)]
        route = [pair for pair in route if pair not in skip]
        return lax.ppermute(piece, "blk", route)

    down1 = [ring(piece, 1, 0, k == 0) for k, piece in enumerate(received)]
    up1 = [ring(piece, -1, 0, k == 0) for k, piece in enumerate(received)]
    down2 = [ring(piece, 1, 1, k == 0) for k, piece in enumerate(down1)]
    up2 = [ring(piece, -1, 1, k == 0) for k, piece in enumerate(up1)]
    pieces = down2 + down1 + received + up1 + up2
    low_end = me <= 1
    fix_first = jnp.where(low_end, down2[0], up2[0])
    fix_second = jnp.where(me == 0, down1[0], up1[0])
    fix_src = jnp.stack([fix_first, fix_second])
    ends = [0, 1, n - 2, n - 1]
    fixed = []
    for k in range(1, group_size):
        route = [
            (b * group_size + g, b * group_size + (g + k) % group_size)
            for b in ends
            for g in range(group_size)
        ]
        fixed.append(lax.ppermute(fix_src, ("blk", "grp"), route))
    minus = jnp.int32(-1)
    fix = jnp.stack([
        jnp.where(low_end, 0, minus),
        jnp.where(me == 0, 1, minus),
        minus,
        jnp.where(me == n - 1, 1, minus),
        jnp.where(me >= n - 2, 0, minus),
    ]).astype(jnp.int32)
    agg_rows = []
    for d in range(5):
        for k in range(group_size):
            row = pieces[d * group_size + k][share_rows // 2, 0, :share_rows]
            if k > 0:
                row = jnp.where(
                    fix[d] >= 0,
                    jnp.where(
                        fix[d] == 0,
                        fixed[k - 1][0, share_rows // 2, 0, :share_rows],
                        fixed[k - 1][1, share_rows // 2, 0, :share_rows],
                    ),
                    row,
                )
            agg_rows.append(row)
    flat_aggs = jnp.stack(agg_rows).astype(jnp.int32).reshape(-1)

    def placed(d, r):
        k = jnp.mod(group_me - r // share_rows, group_size)
        return d * group_size + k, r % share_rows

    wanted = block_columns.reshape(slot_total)
    column_panel = wanted // panel_length
    distance = jnp.mod(column_panel - me + 2, panel_total)
    piece_of, within = placed(distance, wanted % panel_length)
    window_pair = piece_of * piece_rows + within // 2
    fetched_aggs = jnp.take(flat_aggs, piece_of * share_rows + within, axis=0)
    own_piece, own_within = placed(2, jnp.arange(panel_length, dtype=jnp.int32))
    own_pos = own_piece * piece_rows + own_within // 2
    own_aggs = jnp.take(flat_aggs, own_piece * share_rows + own_within, axis=0)
    slot_ids = lax.axis_index("grp") * slots_here + jnp.arange(slots_here, dtype=jnp.int32)
    live = (slot_ids[None, :] < row_counts[:, None]).astype(jnp.int32).reshape(slot_total)
    local_coarse = own_aggs - me * CB
    target = fetched_aggs * CB + jnp.broadcast_to(
        local_coarse[:, None], (panel_length, slots_here)
    ).reshape(slot_total)
    block_values, _ = lax.optimization_barrier((block_values, down1[-1]))
    summed = coarse_partial(
        window_pair.astype(jnp.int32),
        (within % 2).astype(jnp.int32),
        target.astype(jnp.int32),
        live,
        own_pos,
        fix,
        block_values,
        pieces,
        fixed,
        coarse_count * CB,
    )
    share = coarse_count // group_size
    summed = summed.reshape(group_size, share, CB // 2, block_size, 2 * block_size)
    total = jnp.take(summed, group_me, axis=0)
    for k in range(1, group_size):
        outgoing = jnp.take(summed, jnp.mod(group_me + k, group_size), axis=0)
        incoming = lax.ppermute(
            outgoing.astype(jnp.bfloat16),
            "grp",
            [(i, (i + k) % group_size) for i in range(group_size)],
        )
        total = total + incoming.astype(jnp.float32)
    total = total.reshape(share, CB // 2, block_size, 2, block_size)
    return total.transpose(0, 1, 3, 2, 4).reshape(share, CB, block_size, block_size)


def solution(mesh):
    return jax.shard_map(
        local,
        mesh=mesh,
        in_specs=(
            P("blk", "grp", None, None),
            P("blk", "grp"),
            P("blk"),
            P(("blk", "grp"), None, None),
            P(("blk", "grp")),
        ),
        out_specs=P("grp", "blk", None, None),
        check_vma=False,
    )
```

```python
import functools

import jax
import jax.numpy as jnp
from jax import lax
from jax.experimental import pallas as pl
from jax.experimental.pallas import tpu as pltpu
from jax.sharding import PartitionSpec as P

CB = 4
ROWS_PER_STEP = 48


def passed_along(block, axis, distance):
    devices = range(lax.axis_size(axis))
    route = [((i - distance) % len(devices), i) for i in devices]
    return lax.ppermute(block, axis, route)


def coarse_kernel(
    pair_ref, half_ref, agg_at_ref, own_agg_at_ref, aggs_ref, base_ref, live_ref,
    own_pos_ref, fix_ref, values_ref, *rest
):
    window, sems = rest[-2:]
    n_pieces = sems.shape[0]
    groups = n_pieces // 5
    pieces = rest[:n_pieces]
    n_fixed = groups - 1
    fixed = rest[n_pieces : n_pieces + n_fixed]
    out_ref = rest[n_pieces + n_fixed]
    accs = rest[n_pieces + n_fixed + 1 : -2]
    step = pl.program_id(0)
    rows_here, slots, bs, _ = values_ref.shape
    piece_rows = pieces[0].shape[0]
    lanes = window.shape[2]

    @pl.when(step == 0)
    def _():
        copies = []
        for j, piece in enumerate(pieces):
            dst = window.at[pl.ds(j * piece_rows, piece_rows)]
            cp = pltpu.make_async_copy(piece, dst, sems.at[j])
            d, k = divmod(j, groups)
            if k == 0:
                cp.start()
            else:
                flag = fix_ref[d]

                @pl.when(flag < 0)
                def _():
                    cp.start()

                for slot in range(2):
                    @pl.when(flag == slot)
                    def _():
                        pltpu.make_async_copy(
                            fixed[k - 1].at[slot], dst, sems.at[j]
                        ).start()

            copies.append(cp)
        for acc_ref in accs:
            acc_ref[...] = jnp.zeros_like(acc_ref)
        for cp in copies:
            cp.wait()

    lane_half = lax.broadcasted_iota(jnp.int32, (bs, lanes), 1) // bs

    def row_body(r, carry):
        row = step * rows_here + r
        own_pair = window[own_pos_ref[row]].astype(jnp.float32)
        spread = jnp.concatenate([own_pair, jnp.zeros_like(own_pair)], axis=0).T
        own_t = jnp.where(row % 2 == 0, spread[:bs], spread[bs:])[:, :bs]
        own_t = own_t.astype(jnp.bfloat16)
        results = []
        for s in range(slots):
            n = row * slots + s
            pair = window[pair_ref[n]]
            picked = jnp.where(lane_half == half_ref[n], pair, jnp.zeros_like(pair))
            product = jnp.dot(
                values_ref[r, s], picked, preferred_element_type=jnp.float32
            )
            product = jnp.where(live_ref[n] > 0, product, 0.0).astype(jnp.bfloat16)
            results.append(
                jnp.dot(own_t, product, preferred_element_type=jnp.float32)
            )
        own_coarse = aggs_ref[own_agg_at_ref[row]] - base_ref[0]
        for s in range(slots):
            t = aggs_ref[agg_at_ref[row * slots + s]] * CB + own_coarse
            accs[s][t] = accs[s][t] + results[s]
        return carry

    lax.fori_loop(0, rows_here, row_body, 0, unroll=16)

    @pl.when(step == pl.num_programs(0) - 1)
    def _():
        def pack(m, carry):
            first = sum(acc_ref[2 * m] for acc_ref in accs)
            second = sum(acc_ref[2 * m + 1] for acc_ref in accs)
            first = first + pltpu.roll(first, bs, 1)
            second = second + pltpu.roll(second, bs, 1)
            out_ref[m] = jnp.where(lane_half == 0, first, second)
            return carry

        lax.fori_loop(0, out_ref.shape[0], pack, 0)


def coarse_partial(pair, half, agg_at, own_agg_at, aggs, base, live, own_pos, fix, values, pieces, fixed, n_targets):
    panel_length, slots, bs, _ = values.shape
    rows_per_step = min(ROWS_PER_STEP, panel_length)
    grid = (panel_length // rows_per_step,)
    piece_rows, _, lanes = pieces[0].shape
    return pl.pallas_call(
        coarse_kernel,
        out_shape=jax.ShapeDtypeStruct((n_targets // 2, bs, lanes), jnp.float32),
        grid_spec=pltpu.PrefetchScalarGridSpec(
            num_scalar_prefetch=9,
            grid=grid,
            in_specs=[
                pl.BlockSpec((rows_per_step, slots, bs, bs), lambda i, *_: (i, 0, 0, 0)),
            ]
            + [pl.BlockSpec(memory_space=pl.ANY)] * (len(pieces) + len(fixed)),
            out_specs=pl.BlockSpec((n_targets // 2, bs, lanes), lambda i, *_: (0, 0, 0)),
            scratch_shapes=[pltpu.VMEM((n_targets, bs, lanes), jnp.float32)] * slots
            + [
                pltpu.VMEM((len(pieces) * piece_rows, bs, lanes), jnp.bfloat16),
                pltpu.SemaphoreType.DMA((len(pieces),)),
            ],
        ),
        compiler_params=pltpu.CompilerParams(
            dimension_semantics=("arbitrary",),
            vmem_limit_bytes=60 * 1024 * 1024,
        ),
    )(pair, half, agg_at, own_agg_at, aggs, base, live, own_pos, fix, values, *pieces, *fixed)


def local(block_values, block_columns, row_counts, prolong_blocks, aggregates):
    panel_length = row_counts.shape[0]
    slots_here = block_values.shape[1]
    slot_total = panel_length * slots_here
    block_size = block_values.shape[2]
    group_size = lax.axis_size("grp")
    panel_total = lax.axis_size("blk")
    coarse_count = CB * panel_total
    me = lax.axis_index("blk")
    group_me = lax.axis_index("grp")
    share_rows = prolong_blocks.shape[0]
    local_pairs = (
        prolong_blocks.reshape(share_rows // 2, 2, block_size, block_size)
        .transpose(0, 2, 1, 3)
        .reshape(share_rows // 2, block_size, 2 * block_size)
    )
    agg_row = (
        jnp.zeros((1, block_size, 2 * block_size), jnp.bfloat16)
        .at[0, 0, :share_rows]
        .set(aggregates.astype(jnp.bfloat16))
    )
    local_ext = jnp.concatenate([local_pairs, agg_row], axis=0)
    piece_rows = local_ext.shape[0]
    received = [local_ext]
    for k in range(1, group_size):
        received.append(
            lax.ppermute(
                local_ext, "grp", [(i, (i + k) % group_size) for i in range(group_size)]
            )
        )
    n = panel_total
    down_skip = ({(n - 1, 0)}, {(n - 1, 0), (0, 1)})
    up_skip = ({(0, n - 1)}, {(0, n - 1), (n - 1, n - 2)})

    def ring(piece, step, hop, full):
        skip = set() if full else (down_skip if step == 1 else up_skip)[hop]
        route = [((i - step) % n, i) for i in range(n)]
        route = [pair for pair in route if pair not in skip]
        return lax.ppermute(piece, "blk", route)

    down1 = [ring(piece, 1, 0, k == 0) for k, piece in enumerate(received)]
    up1 = [ring(piece, -1, 0, k == 0) for k, piece in enumerate(received)]
    down2 = [ring(piece, 1, 1, k == 0) for k, piece in enumerate(down1)]
    up2 = [ring(piece, -1, 1, k == 0) for k, piece in enumerate(up1)]
    pieces = down2 + down1 + received + up1 + up2
    low_end = me <= 1
    fix_first = jnp.where(low_end, down2[0], up2[0])
    fix_second = jnp.where(me == 0, down1[0], up1[0])
    fix_src = jnp.stack([fix_first, fix_second])
    ends = [0, 1, n - 2, n - 1]
    fixed = []
    for k in range(1, group_size):
        route = [
            (b * group_size + g, b * group_size + (g + k) % group_size)
            for b in ends
            for g in range(group_size)
        ]
        fixed.append(lax.ppermute(fix_src, ("blk", "grp"), route))
    minus = jnp.int32(-1)
    fix = jnp.stack([
        jnp.where(low_end, 0, minus),
        jnp.where(me == 0, 1, minus),
        minus,
        jnp.where(me == n - 1, 1, minus),
        jnp.where(me >= n - 2, 0, minus),
    ]).astype(jnp.int32)
    agg_rows = []
    for d in range(5):
        for k in range(group_size):
            row = pieces[d * group_size + k][share_rows // 2, 0, :share_rows]
            if k > 0:
                row = jnp.where(
                    fix[d] >= 0,
                    jnp.where(
                        fix[d] == 0,
                        fixed[k - 1][0, share_rows // 2, 0, :share_rows],
                        fixed[k - 1][1, share_rows // 2, 0, :share_rows],
                    ),
                    row,
                )
            agg_rows.append(row)
    flat_aggs = jnp.stack(agg_rows).astype(jnp.int32).reshape(-1)

    def placed(d, r):
        k = jnp.mod(group_me - r // share_rows, group_size)
        return d * group_size + k, r % share_rows

    wanted = block_columns.reshape(slot_total)
    column_panel = wanted // panel_length
    distance = jnp.mod(column_panel - me + 2, panel_total)
    piece_of, within = placed(distance, wanted % panel_length)
    window_pair = piece_of * piece_rows + within // 2
    own_piece, own_within = placed(2, jnp.arange(panel_length, dtype=jnp.int32))
    own_pos = own_piece * piece_rows + own_within // 2
    slot_ids = lax.axis_index("grp") * slots_here + jnp.arange(slots_here, dtype=jnp.int32)
    live = (slot_ids[None, :] < row_counts[:, None]).astype(jnp.int32).reshape(slot_total)
    block_values, _ = lax.optimization_barrier((block_values, down1[-1]))
    summed = coarse_partial(
        window_pair.astype(jnp.int32),
        (within % 2).astype(jnp.int32),
        (piece_of * share_rows + within).astype(jnp.int32),
        (own_piece * share_rows + own_within).astype(jnp.int32),
        flat_aggs,
        jnp.reshape(me * CB, (1,)).astype(jnp.int32),
        live,
        own_pos,
        fix,
        block_values,
        pieces,
        fixed,
        coarse_count * CB,
    )
    share = coarse_count // group_size
    summed = summed.reshape(group_size, share, CB // 2, block_size, 2 * block_size)
    total = jnp.take(summed, group_me, axis=0)
    for k in range(1, group_size):
        outgoing = jnp.take(summed, jnp.mod(group_me + k, group_size), axis=0)
        incoming = lax.ppermute(
            outgoing.astype(jnp.bfloat16),
            "grp",
            [(i, (i + k) % group_size) for i in range(group_size)],
        )
        total = total + incoming.astype(jnp.float32)
    total = total.reshape(share, CB // 2, block_size, 2, block_size)
    return total.transpose(0, 1, 3, 2, 4).reshape(share, CB, block_size, block_size)


def solution(mesh):
    return jax.shard_map(
        local,
        mesh=mesh,
        in_specs=(
            P("blk", "grp", None, None),
            P("blk", "grp"),
            P("blk"),
            P(("blk", "grp"), None, None),
            P(("blk", "grp")),
        ),
        out_specs=P("grp", "blk", None, None),
        check_vma=False,
    )
```

```python
import functools

import jax
import jax.numpy as jnp
from jax import lax
from jax.experimental import pallas as pl
from jax.experimental.pallas import tpu as pltpu
from jax.sharding import PartitionSpec as P

CB = 4
ROWS_PER_STEP = 96


def passed_along(block, axis, distance):
    devices = range(lax.axis_size(axis))
    route = [((i - distance) % len(devices), i) for i in devices]
    return lax.ppermute(block, axis, route)


def coarse_kernel(
    pair_ref, half_ref, agg_at_ref, own_agg_at_ref, aggs_ref, base_ref, live_ref,
    own_pos_ref, fix_ref, values_ref, *rest
):
    window, sems = rest[-2:]
    n_pieces = sems.shape[0]
    groups = n_pieces // 5
    pieces = rest[:n_pieces]
    n_fixed = groups - 1
    fixed = rest[n_pieces : n_pieces + n_fixed]
    out_ref = rest[n_pieces + n_fixed]
    accs = rest[n_pieces + n_fixed + 1 : -2]
    step = pl.program_id(0)
    rows_here, slots, bs, _ = values_ref.shape
    piece_rows = pieces[0].shape[0]
    lanes = window.shape[2]

    @pl.when(step == 0)
    def _():
        copies = []
        for j, piece in enumerate(pieces):
            dst = window.at[pl.ds(j * piece_rows, piece_rows)]
            cp = pltpu.make_async_copy(piece, dst, sems.at[j])
            d, k = divmod(j, groups)
            if k == 0:
                cp.start()
            else:
                flag = fix_ref[d]

                @pl.when(flag < 0)
                def _():
                    cp.start()

                for slot in range(2):
                    @pl.when(flag == slot)
                    def _():
                        pltpu.make_async_copy(
                            fixed[k - 1].at[slot], dst, sems.at[j]
                        ).start()

            copies.append(cp)
        for acc_ref in accs:
            acc_ref[...] = jnp.zeros_like(acc_ref)
        for cp in copies:
            cp.wait()

    lane_half = lax.broadcasted_iota(jnp.int32, (bs, lanes), 1) // bs

    def row_body(r, carry):
        row = step * rows_here + r
        own_pair = window[own_pos_ref[row]].astype(jnp.float32)
        spread = jnp.concatenate([own_pair, jnp.zeros_like(own_pair)], axis=0).T
        own_t = jnp.where(row % 2 == 0, spread[:bs], spread[bs:])[:, :bs]
        own_t = own_t.astype(jnp.bfloat16)
        results = []
        for s in range(slots):
            n = row * slots + s
            pair = window[pair_ref[n]]
            picked = jnp.where(lane_half == half_ref[n], pair, jnp.zeros_like(pair))
            product = jnp.dot(
                values_ref[r, s], picked, preferred_element_type=jnp.float32
            )
            product = jnp.where(live_ref[n] > 0, product, 0.0).astype(jnp.bfloat16)
            results.append(
                jnp.dot(own_t, product, preferred_element_type=jnp.float32)
            )
        own_coarse = aggs_ref[own_agg_at_ref[row]] - base_ref[0]
        for s in range(slots):
            t = aggs_ref[agg_at_ref[row * slots + s]] * CB + own_coarse
            accs[s][t] = accs[s][t] + results[s]
        return carry

    lax.fori_loop(0, rows_here, row_body, 0, unroll=16)

    @pl.when(step == pl.num_programs(0) - 1)
    def _():
        def pack(m, carry):
            first = sum(acc_ref[2 * m] for acc_ref in accs)
            second = sum(acc_ref[2 * m + 1] for acc_ref in accs)
            first = first + pltpu.roll(first, bs, 1)
            second = second + pltpu.roll(second, bs, 1)
            out_ref[m] = jnp.where(lane_half == 0, first, second)
            return carry

        lax.fori_loop(0, out_ref.shape[0], pack, 0)


def coarse_partial(pair, half, agg_at, own_agg_at, aggs, base, live, own_pos, fix, values, pieces, fixed, n_targets):
    panel_length, slots, bs, _ = values.shape
    rows_per_step = min(ROWS_PER_STEP, panel_length)
    grid = (panel_length // rows_per_step,)
    piece_rows, _, lanes = pieces[0].shape
    return pl.pallas_call(
        coarse_kernel,
        out_shape=jax.ShapeDtypeStruct((n_targets // 2, bs, lanes), jnp.float32),
        grid_spec=pltpu.PrefetchScalarGridSpec(
            num_scalar_prefetch=9,
            grid=grid,
            in_specs=[
                pl.BlockSpec((rows_per_step, slots, bs, bs), lambda i, *_: (i, 0, 0, 0)),
            ]
            + [pl.BlockSpec(memory_space=pl.ANY)] * (len(pieces) + len(fixed)),
            out_specs=pl.BlockSpec((n_targets // 2, bs, lanes), lambda i, *_: (0, 0, 0)),
            scratch_shapes=[pltpu.VMEM((n_targets, bs, lanes), jnp.float32)] * slots
            + [
                pltpu.VMEM((len(pieces) * piece_rows, bs, lanes), jnp.bfloat16),
                pltpu.SemaphoreType.DMA((len(pieces),)),
            ],
        ),
        compiler_params=pltpu.CompilerParams(
            dimension_semantics=("arbitrary",),
            vmem_limit_bytes=60 * 1024 * 1024,
        ),
    )(pair, half, agg_at, own_agg_at, aggs, base, live, own_pos, fix, values, *pieces, *fixed)


def local(block_values, block_columns, row_counts, prolong_blocks, aggregates):
    panel_length = row_counts.shape[0]
    slots_here = block_values.shape[1]
    slot_total = panel_length * slots_here
    block_size = block_values.shape[2]
    group_size = lax.axis_size("grp")
    panel_total = lax.axis_size("blk")
    coarse_count = CB * panel_total
    me = lax.axis_index("blk")
    group_me = lax.axis_index("grp")
    share_rows = prolong_blocks.shape[0]
    local_pairs = (
        prolong_blocks.reshape(share_rows // 2, 2, block_size, block_size)
        .transpose(0, 2, 1, 3)
        .reshape(share_rows // 2, block_size, 2 * block_size)
    )
    agg_row = (
        jnp.zeros((1, block_size, 2 * block_size), jnp.bfloat16)
        .at[0, 0, :share_rows]
        .set(aggregates.astype(jnp.bfloat16))
    )
    local_ext = jnp.concatenate([local_pairs, agg_row], axis=0)
    piece_rows = local_ext.shape[0]
    received = [local_ext]
    for k in range(1, group_size):
        received.append(
            lax.ppermute(
                local_ext, "grp", [(i, (i + k) % group_size) for i in range(group_size)]
            )
        )
    n = panel_total
    down_skip = ({(n - 1, 0)}, {(n - 1, 0), (0, 1)})
    up_skip = ({(0, n - 1)}, {(0, n - 1), (n - 1, n - 2)})

    def ring(piece, step, hop, full):
        skip = set() if full else (down_skip if step == 1 else up_skip)[hop]
        route = [((i - step) % n, i) for i in range(n)]
        route = [pair for pair in route if pair not in skip]
        return lax.ppermute(piece, "blk", route)

    down1 = [ring(piece, 1, 0, k == 0) for k, piece in enumerate(received)]
    up1 = [ring(piece, -1, 0, k == 0) for k, piece in enumerate(received)]
    down2 = [ring(piece, 1, 1, k == 0) for k, piece in enumerate(down1)]
    up2 = [ring(piece, -1, 1, k == 0) for k, piece in enumerate(up1)]
    pieces = down2 + down1 + received + up1 + up2
    low_end = me <= 1
    fix_first = jnp.where(low_end, down2[0], up2[0])
    fix_second = jnp.where(me == 0, down1[0], up1[0])
    fix_src = jnp.stack([fix_first, fix_second])
    ends = [0, 1, n - 2, n - 1]
    fixed = []
    for k in range(1, group_size):
        route = [
            (b * group_size + g, b * group_size + (g + k) % group_size)
            for b in ends
            for g in range(group_size)
        ]
        fixed.append(lax.ppermute(fix_src, ("blk", "grp"), route))
    minus = jnp.int32(-1)
    fix = jnp.stack([
        jnp.where(low_end, 0, minus),
        jnp.where(me == 0, 1, minus),
        minus,
        jnp.where(me == n - 1, 1, minus),
        jnp.where(me >= n - 2, 0, minus),
    ]).astype(jnp.int32)
    agg_rows = []
    for d in range(5):
        for k in range(group_size):
            row = pieces[d * group_size + k][share_rows // 2, 0, :share_rows]
            if k > 0:
                row = jnp.where(
                    fix[d] >= 0,
                    jnp.where(
                        fix[d] == 0,
                        fixed[k - 1][0, share_rows // 2, 0, :share_rows],
                        fixed[k - 1][1, share_rows // 2, 0, :share_rows],
                    ),
                    row,
                )
            agg_rows.append(row)
    flat_aggs = jnp.stack(agg_rows).astype(jnp.int32).reshape(-1)

    def placed(d, r):
        k = jnp.mod(group_me - r // share_rows, group_size)
        return d * group_size + k, r % share_rows

    wanted = block_columns.reshape(slot_total)
    column_panel = wanted // panel_length
    distance = jnp.mod(column_panel - me + 2, panel_total)
    piece_of, within = placed(distance, wanted % panel_length)
    window_pair = piece_of * piece_rows + within // 2
    own_piece, own_within = placed(2, jnp.arange(panel_length, dtype=jnp.int32))
    own_pos = own_piece * piece_rows + own_within // 2
    slot_ids = lax.axis_index("grp") * slots_here + jnp.arange(slots_here, dtype=jnp.int32)
    live = (slot_ids[None, :] < row_counts[:, None]).astype(jnp.int32).reshape(slot_total)
    block_values, _ = lax.optimization_barrier((block_values, down1[-1]))
    summed = coarse_partial(
        window_pair.astype(jnp.int32),
        (within % 2).astype(jnp.int32),
        (piece_of * share_rows + within).astype(jnp.int32),
        (own_piece * share_rows + own_within).astype(jnp.int32),
        flat_aggs,
        jnp.reshape(me * CB, (1,)).astype(jnp.int32),
        live,
        own_pos,
        fix,
        block_values,
        pieces,
        fixed,
        coarse_count * CB,
    )
    share = coarse_count // group_size
    summed = summed.reshape(group_size, share, CB // 2, block_size, 2 * block_size)
    total = jnp.take(summed, group_me, axis=0)
    for k in range(1, group_size):
        outgoing = jnp.take(summed, jnp.mod(group_me + k, group_size), axis=0)
        incoming = lax.ppermute(
            outgoing.astype(jnp.bfloat16),
            "grp",
            [(i, (i + k) % group_size) for i in range(group_size)],
        )
        total = total + incoming.astype(jnp.float32)
    total = total.reshape(share, CB // 2, block_size, 2, block_size)
    return total.transpose(0, 1, 3, 2, 4).reshape(share, CB, block_size, block_size)


def solution(mesh):
    return jax.shard_map(
        local,
        mesh=mesh,
        in_specs=(
            P("blk", "grp", None, None),
            P("blk", "grp"),
            P("blk"),
            P(("blk", "grp"), None, None),
            P(("blk", "grp")),
        ),
        out_specs=P("grp", "blk", None, None),
        check_vma=False,
    )
```

```python
import functools

import jax
import jax.numpy as jnp
from jax import lax
from jax.experimental import pallas as pl
from jax.experimental.pallas import tpu as pltpu
from jax.sharding import PartitionSpec as P

CB = 4
ROWS_PER_STEP = 48


def passed_along(block, axis, distance):
    devices = range(lax.axis_size(axis))
    route = [((i - distance) % len(devices), i) for i in devices]
    return lax.ppermute(block, axis, route)


def coarse_kernel(
    pair_ref, half_ref, agg_at_ref, own_agg_at_ref, aggs_ref, base_ref, live_ref,
    own_pos_ref, fix_ref, values_ref, *rest
):
    window, sems = rest[-2:]
    n_pieces = sems.shape[0]
    groups = n_pieces // 5
    pieces = rest[:n_pieces]
    n_fixed = groups - 1
    fixed = rest[n_pieces : n_pieces + n_fixed]
    out_ref = rest[n_pieces + n_fixed]
    accs = rest[n_pieces + n_fixed + 1 : -2]
    step = pl.program_id(0)
    rows_here, slots, bs, _ = values_ref.shape
    piece_rows = pieces[0].shape[0]
    lanes = window.shape[2]

    @pl.when(step == 0)
    def _():
        copies = []
        for j, piece in enumerate(pieces):
            dst = window.at[pl.ds(j * piece_rows, piece_rows)]
            cp = pltpu.make_async_copy(piece, dst, sems.at[j])
            d, k = divmod(j, groups)
            if k == 0:
                cp.start()
            else:
                flag = fix_ref[d]

                @pl.when(flag < 0)
                def _():
                    cp.start()

                for slot in range(2):
                    @pl.when(flag == slot)
                    def _():
                        pltpu.make_async_copy(
                            fixed[k - 1].at[slot], dst, sems.at[j]
                        ).start()

            copies.append(cp)
        for acc_ref in accs:
            acc_ref[...] = jnp.zeros_like(acc_ref)
        for cp in copies:
            cp.wait()

    lane_half = lax.broadcasted_iota(jnp.int32, (bs, lanes), 1) // bs

    def row_body(r, carry):
        row = step * rows_here + r
        own_pair = window[own_pos_ref[row]].astype(jnp.float32)
        spread = jnp.concatenate([own_pair, jnp.zeros_like(own_pair)], axis=0).T
        own_t = jnp.where(row % 2 == 0, spread[:bs], spread[bs:])[:, :bs]
        own_t = own_t.astype(jnp.bfloat16)
        results = []
        for s in range(slots):
            n = row * slots + s
            pair = window[pair_ref[n]]
            picked = jnp.where(lane_half == half_ref[n], pair, jnp.zeros_like(pair))
            product = jnp.dot(
                values_ref[r, s], picked, preferred_element_type=jnp.float32
            )
            product = jnp.where(live_ref[n] > 0, product, 0.0).astype(jnp.bfloat16)
            results.append(
                jnp.dot(own_t, product, preferred_element_type=jnp.float32)
            )
        own_coarse = aggs_ref[own_agg_at_ref[row]] - base_ref[0]
        for s in range(slots):
            t = aggs_ref[agg_at_ref[row * slots + s]] * CB + own_coarse
            accs[s][t] = accs[s][t] + results[s]
        return carry

    lax.fori_loop(0, rows_here, row_body, 0, unroll=rows_here)

    @pl.when(step == pl.num_programs(0) - 1)
    def _():
        def pack(m, carry):
            first = sum(acc_ref[2 * m] for acc_ref in accs)
            second = sum(acc_ref[2 * m + 1] for acc_ref in accs)
            first = first + pltpu.roll(first, bs, 1)
            second = second + pltpu.roll(second, bs, 1)
            out_ref[m] = jnp.where(lane_half == 0, first, second)
            return carry

        lax.fori_loop(0, out_ref.shape[0], pack, 0)


def coarse_partial(pair, half, agg_at, own_agg_at, aggs, base, live, own_pos, fix, values, pieces, fixed, n_targets):
    panel_length, slots, bs, _ = values.shape
    rows_per_step = min(ROWS_PER_STEP, panel_length)
    grid = (panel_length // rows_per_step,)
    piece_rows, _, lanes = pieces[0].shape
    return pl.pallas_call(
        coarse_kernel,
        out_shape=jax.ShapeDtypeStruct((n_targets // 2, bs, lanes), jnp.float32),
        grid_spec=pltpu.PrefetchScalarGridSpec(
            num_scalar_prefetch=9,
            grid=grid,
            in_specs=[
                pl.BlockSpec((rows_per_step, slots, bs, bs), lambda i, *_: (i, 0, 0, 0)),
            ]
            + [pl.BlockSpec(memory_space=pl.ANY)] * (len(pieces) + len(fixed)),
            out_specs=pl.BlockSpec((n_targets // 2, bs, lanes), lambda i, *_: (0, 0, 0)),
            scratch_shapes=[pltpu.VMEM((n_targets, bs, lanes), jnp.float32)] * slots
            + [
                pltpu.VMEM((len(pieces) * piece_rows, bs, lanes), jnp.bfloat16),
                pltpu.SemaphoreType.DMA((len(pieces),)),
            ],
        ),
        compiler_params=pltpu.CompilerParams(
            dimension_semantics=("arbitrary",),
            vmem_limit_bytes=60 * 1024 * 1024,
        ),
    )(pair, half, agg_at, own_agg_at, aggs, base, live, own_pos, fix, values, *pieces, *fixed)


def local(block_values, block_columns, row_counts, prolong_blocks, aggregates):
    panel_length = row_counts.shape[0]
    slots_here = block_values.shape[1]
    slot_total = panel_length * slots_here
    block_size = block_values.shape[2]
    group_size = lax.axis_size("grp")
    panel_total = lax.axis_size("blk")
    coarse_count = CB * panel_total
    me = lax.axis_index("blk")
    group_me = lax.axis_index("grp")
    share_rows = prolong_blocks.shape[0]
    local_pairs = (
        prolong_blocks.reshape(share_rows // 2, 2, block_size, block_size)
        .transpose(0, 2, 1, 3)
        .reshape(share_rows // 2, block_size, 2 * block_size)
    )
    agg_row = (
        jnp.zeros((1, block_size, 2 * block_size), jnp.bfloat16)
        .at[0, 0, :share_rows]
        .set(aggregates.astype(jnp.bfloat16))
    )
    local_ext = jnp.concatenate([local_pairs, agg_row], axis=0)
    piece_rows = local_ext.shape[0]
    received = [local_ext]
    for k in range(1, group_size):
        received.append(
            lax.ppermute(
                local_ext, "grp", [(i, (i + k) % group_size) for i in range(group_size)]
            )
        )
    n = panel_total
    down_skip = ({(n - 1, 0)}, {(n - 1, 0), (0, 1)})
    up_skip = ({(0, n - 1)}, {(0, n - 1), (n - 1, n - 2)})

    def ring(piece, step, hop, full):
        skip = set() if full else (down_skip if step == 1 else up_skip)[hop]
        route = [((i - step) % n, i) for i in range(n)]
        route = [pair for pair in route if pair not in skip]
        return lax.ppermute(piece, "blk", route)

    down1 = [ring(piece, 1, 0, k == 0) for k, piece in enumerate(received)]
    up1 = [ring(piece, -1, 0, k == 0) for k, piece in enumerate(received)]
    down2 = [ring(piece, 1, 1, k == 0) for k, piece in enumerate(down1)]
    up2 = [ring(piece, -1, 1, k == 0) for k, piece in enumerate(up1)]
    pieces = down2 + down1 + received + up1 + up2
    low_end = me <= 1
    fix_first = jnp.where(low_end, down2[0], up2[0])
    fix_second = jnp.where(me == 0, down1[0], up1[0])
    fix_src = jnp.stack([fix_first, fix_second])
    ends = [0, 1, n - 2, n - 1]
    fixed = []
    for k in range(1, group_size):
        route = [
            (b * group_size + g, b * group_size + (g + k) % group_size)
            for b in ends
            for g in range(group_size)
        ]
        fixed.append(lax.ppermute(fix_src, ("blk", "grp"), route))
    minus = jnp.int32(-1)
    fix = jnp.stack([
        jnp.where(low_end, 0, minus),
        jnp.where(me == 0, 1, minus),
        minus,
        jnp.where(me == n - 1, 1, minus),
        jnp.where(me >= n - 2, 0, minus),
    ]).astype(jnp.int32)
    agg_rows = []
    for d in range(5):
        for k in range(group_size):
            row = pieces[d * group_size + k][share_rows // 2, 0, :share_rows]
            if k > 0:
                row = jnp.where(
                    fix[d] >= 0,
                    jnp.where(
                        fix[d] == 0,
                        fixed[k - 1][0, share_rows // 2, 0, :share_rows],
                        fixed[k - 1][1, share_rows // 2, 0, :share_rows],
                    ),
                    row,
                )
            agg_rows.append(row)
    flat_aggs = jnp.stack(agg_rows).astype(jnp.int32).reshape(-1)

    def placed(d, r):
        k = jnp.mod(group_me - r // share_rows, group_size)
        return d * group_size + k, r % share_rows

    wanted = block_columns.reshape(slot_total)
    column_panel = wanted // panel_length
    distance = jnp.mod(column_panel - me + 2, panel_total)
    piece_of, within = placed(distance, wanted % panel_length)
    window_pair = piece_of * piece_rows + within // 2
    own_piece, own_within = placed(2, jnp.arange(panel_length, dtype=jnp.int32))
    own_pos = own_piece * piece_rows + own_within // 2
    slot_ids = lax.axis_index("grp") * slots_here + jnp.arange(slots_here, dtype=jnp.int32)
    live = (slot_ids[None, :] < row_counts[:, None]).astype(jnp.int32).reshape(slot_total)
    block_values, _ = lax.optimization_barrier((block_values, down1[-1]))
    summed = coarse_partial(
        window_pair.astype(jnp.int32),
        (within % 2).astype(jnp.int32),
        (piece_of * share_rows + within).astype(jnp.int32),
        (own_piece * share_rows + own_within).astype(jnp.int32),
        flat_aggs,
        jnp.reshape(me * CB, (1,)).astype(jnp.int32),
        live,
        own_pos,
        fix,
        block_values,
        pieces,
        fixed,
        coarse_count * CB,
    )
    share = coarse_count // group_size
    summed = summed.reshape(group_size, share, CB // 2, block_size, 2 * block_size)
    total = jnp.take(summed, group_me, axis=0)
    for k in range(1, group_size):
        outgoing = jnp.take(summed, jnp.mod(group_me + k, group_size), axis=0)
        incoming = lax.ppermute(
            outgoing.astype(jnp.bfloat16),
            "grp",
            [(i, (i + k) % group_size) for i in range(group_size)],
        )
        total = total + incoming.astype(jnp.float32)
    total = total.reshape(share, CB // 2, block_size, 2, block_size)
    return total.transpose(0, 1, 3, 2, 4).reshape(share, CB, block_size, block_size)


def solution(mesh):
    return jax.shard_map(
        local,
        mesh=mesh,
        in_specs=(
            P("blk", "grp", None, None),
            P("blk", "grp"),
            P("blk"),
            P(("blk", "grp"), None, None),
            P(("blk", "grp")),
        ),
        out_specs=P("grp", "blk", None, None),
        check_vma=False,
    )
```

```python
import functools

import jax
import jax.numpy as jnp
from jax import lax
from jax.experimental import pallas as pl
from jax.experimental.pallas import tpu as pltpu
from jax.sharding import PartitionSpec as P

CB = 4
ROWS_PER_STEP = 64


def passed_along(block, axis, distance):
    devices = range(lax.axis_size(axis))
    route = [((i - distance) % len(devices), i) for i in devices]
    return lax.ppermute(block, axis, route)


def coarse_kernel(
    pair_ref, half_ref, agg_at_ref, own_agg_at_ref, aggs_ref, base_ref, live_ref,
    own_pos_ref, fix_ref, values_ref, *rest
):
    window, sems = rest[-2:]
    n_pieces = sems.shape[0]
    groups = n_pieces // 5
    pieces = rest[:n_pieces]
    n_fixed = groups - 1
    fixed = rest[n_pieces : n_pieces + n_fixed]
    out_ref = rest[n_pieces + n_fixed]
    accs = rest[n_pieces + n_fixed + 1 : -2]
    step = pl.program_id(0)
    rows_here, slots, bs, _ = values_ref.shape
    piece_rows = pieces[0].shape[0]
    lanes = window.shape[2]

    @pl.when(step == 0)
    def _():
        copies = []
        for j, piece in enumerate(pieces):
            dst = window.at[pl.ds(j * piece_rows, piece_rows)]
            cp = pltpu.make_async_copy(piece, dst, sems.at[j])
            d, k = divmod(j, groups)
            if k == 0:
                cp.start()
            else:
                flag = fix_ref[d]

                @pl.when(flag < 0)
                def _():
                    cp.start()

                for slot in range(2):
                    @pl.when(flag == slot)
                    def _():
                        pltpu.make_async_copy(
                            fixed[k - 1].at[slot], dst, sems.at[j]
                        ).start()

            copies.append(cp)
        for acc_ref in accs:
            acc_ref[...] = jnp.zeros_like(acc_ref)
        for cp in copies:
            cp.wait()

    lane_half = lax.broadcasted_iota(jnp.int32, (bs, lanes), 1) // bs

    def row_body(r, carry):
        row = step * rows_here + r
        own_pair = window[own_pos_ref[row]].astype(jnp.float32)
        spread = jnp.concatenate([own_pair, jnp.zeros_like(own_pair)], axis=0).T
        own_t = jnp.where(row % 2 == 0, spread[:bs], spread[bs:])[:, :bs]
        own_t = own_t.astype(jnp.bfloat16)
        results = []
        for s in range(slots):
            n = row * slots + s
            pair = window[pair_ref[n]]
            picked = jnp.where(lane_half == half_ref[n], pair, jnp.zeros_like(pair))
            product = jnp.dot(
                values_ref[r, s], picked, preferred_element_type=jnp.float32
            )
            product = jnp.where(live_ref[n] > 0, product, 0.0).astype(jnp.bfloat16)
            results.append(
                jnp.dot(own_t, product, preferred_element_type=jnp.float32)
            )
        own_coarse = aggs_ref[own_agg_at_ref[row]] - base_ref[0]
        for s in range(slots):
            t = aggs_ref[agg_at_ref[row * slots + s]] * CB + own_coarse
            accs[s][t] = accs[s][t] + results[s]
        return carry

    lax.fori_loop(0, rows_here, row_body, 0, unroll=rows_here)

    @pl.when(step == pl.num_programs(0) - 1)
    def _():
        def pack(m, carry):
            first = sum(acc_ref[2 * m] for acc_ref in accs)
            second = sum(acc_ref[2 * m + 1] for acc_ref in accs)
            first = first + pltpu.roll(first, bs, 1)
            second = second + pltpu.roll(second, bs, 1)
            out_ref[m] = jnp.where(lane_half == 0, first, second)
            return carry

        lax.fori_loop(0, out_ref.shape[0], pack, 0)


def coarse_partial(pair, half, agg_at, own_agg_at, aggs, base, live, own_pos, fix, values, pieces, fixed, n_targets):
    panel_length, slots, bs, _ = values.shape
    rows_per_step = min(ROWS_PER_STEP, panel_length)
    grid = (panel_length // rows_per_step,)
    piece_rows, _, lanes = pieces[0].shape
    return pl.pallas_call(
        coarse_kernel,
        out_shape=jax.ShapeDtypeStruct((n_targets // 2, bs, lanes), jnp.float32),
        grid_spec=pltpu.PrefetchScalarGridSpec(
            num_scalar_prefetch=9,
            grid=grid,
            in_specs=[
                pl.BlockSpec((rows_per_step, slots, bs, bs), lambda i, *_: (i, 0, 0, 0)),
            ]
            + [pl.BlockSpec(memory_space=pl.ANY)] * (len(pieces) + len(fixed)),
            out_specs=pl.BlockSpec((n_targets // 2, bs, lanes), lambda i, *_: (0, 0, 0)),
            scratch_shapes=[pltpu.VMEM((n_targets, bs, lanes), jnp.float32)] * slots
            + [
                pltpu.VMEM((len(pieces) * piece_rows, bs, lanes), jnp.bfloat16),
                pltpu.SemaphoreType.DMA((len(pieces),)),
            ],
        ),
        compiler_params=pltpu.CompilerParams(
            dimension_semantics=("arbitrary",),
            vmem_limit_bytes=60 * 1024 * 1024,
        ),
    )(pair, half, agg_at, own_agg_at, aggs, base, live, own_pos, fix, values, *pieces, *fixed)


def local(block_values, block_columns, row_counts, prolong_blocks, aggregates):
    panel_length = row_counts.shape[0]
    slots_here = block_values.shape[1]
    slot_total = panel_length * slots_here
    block_size = block_values.shape[2]
    group_size = lax.axis_size("grp")
    panel_total = lax.axis_size("blk")
    coarse_count = CB * panel_total
    me = lax.axis_index("blk")
    group_me = lax.axis_index("grp")
    share_rows = prolong_blocks.shape[0]
    local_pairs = (
        prolong_blocks.reshape(share_rows // 2, 2, block_size, block_size)
        .transpose(0, 2, 1, 3)
        .reshape(share_rows // 2, block_size, 2 * block_size)
    )
    agg_row = (
        jnp.zeros((1, block_size, 2 * block_size), jnp.bfloat16)
        .at[0, 0, :share_rows]
        .set(aggregates.astype(jnp.bfloat16))
    )
    local_ext = jnp.concatenate([local_pairs, agg_row], axis=0)
    piece_rows = local_ext.shape[0]
    received = [local_ext]
    for k in range(1, group_size):
        received.append(
            lax.ppermute(
                local_ext, "grp", [(i, (i + k) % group_size) for i in range(group_size)]
            )
        )
    n = panel_total
    down_skip = ({(n - 1, 0)}, {(n - 1, 0), (0, 1)})
    up_skip = ({(0, n - 1)}, {(0, n - 1), (n - 1, n - 2)})

    def ring(piece, step, hop, full):
        skip = set() if full else (down_skip if step == 1 else up_skip)[hop]
        route = [((i - step) % n, i) for i in range(n)]
        route = [pair for pair in route if pair not in skip]
        return lax.ppermute(piece, "blk", route)

    down1 = [ring(piece, 1, 0, k == 0) for k, piece in enumerate(received)]
    up1 = [ring(piece, -1, 0, k == 0) for k, piece in enumerate(received)]
    down2 = [ring(piece, 1, 1, k == 0) for k, piece in enumerate(down1)]
    up2 = [ring(piece, -1, 1, k == 0) for k, piece in enumerate(up1)]
    pieces = down2 + down1 + received + up1 + up2
    low_end = me <= 1
    fix_first = jnp.where(low_end, down2[0], up2[0])
    fix_second = jnp.where(me == 0, down1[0], up1[0])
    fix_src = jnp.stack([fix_first, fix_second])
    ends = [0, 1, n - 2, n - 1]
    fixed = []
    for k in range(1, group_size):
        route = [
            (b * group_size + g, b * group_size + (g + k) % group_size)
            for b in ends
            for g in range(group_size)
        ]
        fixed.append(lax.ppermute(fix_src, ("blk", "grp"), route))
    minus = jnp.int32(-1)
    fix = jnp.stack([
        jnp.where(low_end, 0, minus),
        jnp.where(me == 0, 1, minus),
        minus,
        jnp.where(me == n - 1, 1, minus),
        jnp.where(me >= n - 2, 0, minus),
    ]).astype(jnp.int32)
    agg_rows = []
    for d in range(5):
        for k in range(group_size):
            row = pieces[d * group_size + k][share_rows // 2, 0, :share_rows]
            if k > 0:
                row = jnp.where(
                    fix[d] >= 0,
                    jnp.where(
                        fix[d] == 0,
                        fixed[k - 1][0, share_rows // 2, 0, :share_rows],
                        fixed[k - 1][1, share_rows // 2, 0, :share_rows],
                    ),
                    row,
                )
            agg_rows.append(row)
    flat_aggs = jnp.stack(agg_rows).astype(jnp.int32).reshape(-1)

    def placed(d, r):
        k = jnp.mod(group_me - r // share_rows, group_size)
        return d * group_size + k, r % share_rows

    wanted = block_columns.reshape(slot_total)
    column_panel = wanted // panel_length
    distance = jnp.mod(column_panel - me + 2, panel_total)
    piece_of, within = placed(distance, wanted % panel_length)
    window_pair = piece_of * piece_rows + within // 2
    own_piece, own_within = placed(2, jnp.arange(panel_length, dtype=jnp.int32))
    own_pos = own_piece * piece_rows + own_within // 2
    slot_ids = lax.axis_index("grp") * slots_here + jnp.arange(slots_here, dtype=jnp.int32)
    live = (slot_ids[None, :] < row_counts[:, None]).astype(jnp.int32).reshape(slot_total)
    block_values, _ = lax.optimization_barrier((block_values, down1[-1]))
    summed = coarse_partial(
        window_pair.astype(jnp.int32),
        (within % 2).astype(jnp.int32),
        (piece_of * share_rows + within).astype(jnp.int32),
        (own_piece * share_rows + own_within).astype(jnp.int32),
        flat_aggs,
        jnp.reshape(me * CB, (1,)).astype(jnp.int32),
        live,
        own_pos,
        fix,
        block_values,
        pieces,
        fixed,
        coarse_count * CB,
    )
    share = coarse_count // group_size
    summed = summed.reshape(group_size, share, CB // 2, block_size, 2 * block_size)
    total = jnp.take(summed, group_me, axis=0)
    for k in range(1, group_size):
        outgoing = jnp.take(summed, jnp.mod(group_me + k, group_size), axis=0)
        incoming = lax.ppermute(
            outgoing.astype(jnp.bfloat16),
            "grp",
            [(i, (i + k) % group_size) for i in range(group_size)],
        )
        total = total + incoming.astype(jnp.float32)
    total = total.reshape(share, CB // 2, block_size, 2, block_size)
    return total.transpose(0, 1, 3, 2, 4).reshape(share, CB, block_size, block_size)


def solution(mesh):
    return jax.shard_map(
        local,
        mesh=mesh,
        in_specs=(
            P("blk", "grp", None, None),
            P("blk", "grp"),
            P("blk"),
            P(("blk", "grp"), None, None),
            P(("blk", "grp")),
        ),
        out_specs=P("grp", "blk", None, None),
        check_vma=False,
    )
```

```python
import functools

import jax
import jax.numpy as jnp
from jax import lax
from jax.experimental import pallas as pl
from jax.experimental.pallas import tpu as pltpu
from jax.sharding import PartitionSpec as P

CB = 4
ROWS_PER_STEP = 48


def passed_along(block, axis, distance):
    devices = range(lax.axis_size(axis))
    route = [((i - distance) % len(devices), i) for i in devices]
    return lax.ppermute(block, axis, route)


def coarse_kernel(
    pair_ref, half_ref, agg_at_ref, own_agg_at_ref, aggs_ref, base_ref, live_ref,
    own_pos_ref, fix_ref, values_ref, *rest
):
    window, sems = rest[-2:]
    n_pieces = sems.shape[0]
    groups = n_pieces // 5
    pieces = rest[:n_pieces]
    n_fixed = groups - 1
    fixed = rest[n_pieces : n_pieces + n_fixed]
    out_ref = rest[n_pieces + n_fixed]
    accs = rest[n_pieces + n_fixed + 1 : -2]
    step = pl.program_id(0)
    rows_here, slots, bs, _ = values_ref.shape
    piece_rows = pieces[0].shape[0]
    lanes = window.shape[2]

    @pl.when(step == 0)
    def _():
        copies = []
        for j, piece in enumerate(pieces):
            dst = window.at[pl.ds(j * piece_rows, piece_rows)]
            cp = pltpu.make_async_copy(piece, dst, sems.at[j])
            d, k = divmod(j, groups)
            if k == 0:
                cp.start()
            else:
                flag = fix_ref[d]

                @pl.when(flag < 0)
                def _():
                    cp.start()

                for slot in range(2):
                    @pl.when(flag == slot)
                    def _():
                        pltpu.make_async_copy(
                            fixed[k - 1].at[slot], dst, sems.at[j]
                        ).start()

            copies.append(cp)
        for acc_ref in accs:
            acc_ref[...] = jnp.zeros_like(acc_ref)
        for cp in copies:
            cp.wait()

    lane_half = lax.broadcasted_iota(jnp.int32, (bs, lanes), 1) // bs

    def row_body(r, carry):
        row = step * rows_here + r
        own_pair = window[own_pos_ref[row]].astype(jnp.float32)
        spread = jnp.concatenate([own_pair, jnp.zeros_like(own_pair)], axis=0).T
        own_t = jnp.where(row % 2 == 0, spread[:bs], spread[bs:])[:, :bs]
        own_t = own_t.astype(jnp.bfloat16)
        results = []
        for s in range(slots):
            n = row * slots + s
            pair = window[pair_ref[n]]
            keep = (lane_half == half_ref[n]) & (live_ref[n] > 0)
            picked = jnp.where(keep, pair, jnp.zeros_like(pair))
            product = jnp.dot(
                values_ref[r, s], picked, preferred_element_type=jnp.float32
            ).astype(jnp.bfloat16)
            results.append(
                jnp.dot(own_t, product, preferred_element_type=jnp.float32)
            )
        own_coarse = aggs_ref[own_agg_at_ref[row]] - base_ref[0]
        for s in range(slots):
            t = aggs_ref[agg_at_ref[row * slots + s]] * CB + own_coarse
            accs[s][t] = accs[s][t] + results[s]
        return carry

    lax.fori_loop(0, rows_here, row_body, 0, unroll=rows_here)

    @pl.when(step == pl.num_programs(0) - 1)
    def _():
        def pack(m, carry):
            first = sum(acc_ref[2 * m] for acc_ref in accs)
            second = sum(acc_ref[2 * m + 1] for acc_ref in accs)
            first = first + pltpu.roll(first, bs, 1)
            second = second + pltpu.roll(second, bs, 1)
            out_ref[m] = jnp.where(lane_half == 0, first, second)
            return carry

        lax.fori_loop(0, out_ref.shape[0], pack, 0)


def coarse_partial(pair, half, agg_at, own_agg_at, aggs, base, live, own_pos, fix, values, pieces, fixed, n_targets):
    panel_length, slots, bs, _ = values.shape
    rows_per_step = min(ROWS_PER_STEP, panel_length)
    grid = (panel_length // rows_per_step,)
    piece_rows, _, lanes = pieces[0].shape
    return pl.pallas_call(
        coarse_kernel,
        out_shape=jax.ShapeDtypeStruct((n_targets // 2, bs, lanes), jnp.float32),
        grid_spec=pltpu.PrefetchScalarGridSpec(
            num_scalar_prefetch=9,
            grid=grid,
            in_specs=[
                pl.BlockSpec((rows_per_step, slots, bs, bs), lambda i, *_: (i, 0, 0, 0)),
            ]
            + [pl.BlockSpec(memory_space=pl.ANY)] * (len(pieces) + len(fixed)),
            out_specs=pl.BlockSpec((n_targets // 2, bs, lanes), lambda i, *_: (0, 0, 0)),
            scratch_shapes=[pltpu.VMEM((n_targets, bs, lanes), jnp.float32)] * slots
            + [
                pltpu.VMEM((len(pieces) * piece_rows, bs, lanes), jnp.bfloat16),
                pltpu.SemaphoreType.DMA((len(pieces),)),
            ],
        ),
        compiler_params=pltpu.CompilerParams(
            dimension_semantics=("arbitrary",),
            vmem_limit_bytes=60 * 1024 * 1024,
        ),
    )(pair, half, agg_at, own_agg_at, aggs, base, live, own_pos, fix, values, *pieces, *fixed)


def local(block_values, block_columns, row_counts, prolong_blocks, aggregates):
    panel_length = row_counts.shape[0]
    slots_here = block_values.shape[1]
    slot_total = panel_length * slots_here
    block_size = block_values.shape[2]
    group_size = lax.axis_size("grp")
    panel_total = lax.axis_size("blk")
    coarse_count = CB * panel_total
    me = lax.axis_index("blk")
    group_me = lax.axis_index("grp")
    share_rows = prolong_blocks.shape[0]
    local_pairs = (
        prolong_blocks.reshape(share_rows // 2, 2, block_size, block_size)
        .transpose(0, 2, 1, 3)
        .reshape(share_rows // 2, block_size, 2 * block_size)
    )
    agg_row = (
        jnp.zeros((1, block_size, 2 * block_size), jnp.bfloat16)
        .at[0, 0, :share_rows]
        .set(aggregates.astype(jnp.bfloat16))
    )
    local_ext = jnp.concatenate([local_pairs, agg_row], axis=0)
    piece_rows = local_ext.shape[0]
    received = [local_ext]
    for k in range(1, group_size):
        received.append(
            lax.ppermute(
                local_ext, "grp", [(i, (i + k) % group_size) for i in range(group_size)]
            )
        )
    n = panel_total
    down_skip = ({(n - 1, 0)}, {(n - 1, 0), (0, 1)})
    up_skip = ({(0, n - 1)}, {(0, n - 1), (n - 1, n - 2)})

    def ring(piece, step, hop, full):
        skip = set() if full else (down_skip if step == 1 else up_skip)[hop]
        route = [((i - step) % n, i) for i in range(n)]
        route = [pair for pair in route if pair not in skip]
        return lax.ppermute(piece, "blk", route)

    down1 = [ring(piece, 1, 0, k == 0) for k, piece in enumerate(received)]
    up1 = [ring(piece, -1, 0, k == 0) for k, piece in enumerate(received)]
    down2 = [ring(piece, 1, 1, k == 0) for k, piece in enumerate(down1)]
    up2 = [ring(piece, -1, 1, k == 0) for k, piece in enumerate(up1)]
    pieces = down2 + down1 + received + up1 + up2
    low_end = me <= 1
    fix_first = jnp.where(low_end, down2[0], up2[0])
    fix_second = jnp.where(me == 0, down1[0], up1[0])
    fix_src = jnp.stack([fix_first, fix_second])
    ends = [0, 1, n - 2, n - 1]
    fixed = []
    for k in range(1, group_size):
        route = [
            (b * group_size + g, b * group_size + (g + k) % group_size)
            for b in ends
            for g in range(group_size)
        ]
        fixed.append(lax.ppermute(fix_src, ("blk", "grp"), route))
    minus = jnp.int32(-1)
    fix = jnp.stack([
        jnp.where(low_end, 0, minus),
        jnp.where(me == 0, 1, minus),
        minus,
        jnp.where(me == n - 1, 1, minus),
        jnp.where(me >= n - 2, 0, minus),
    ]).astype(jnp.int32)
    agg_rows = []
    for d in range(5):
        for k in range(group_size):
            row = pieces[d * group_size + k][share_rows // 2, 0, :share_rows]
            if k > 0:
                row = jnp.where(
                    fix[d] >= 0,
                    jnp.where(
                        fix[d] == 0,
                        fixed[k - 1][0, share_rows // 2, 0, :share_rows],
                        fixed[k - 1][1, share_rows // 2, 0, :share_rows],
                    ),
                    row,
                )
            agg_rows.append(row)
    flat_aggs = jnp.stack(agg_rows).astype(jnp.int32).reshape(-1)

    def placed(d, r):
        k = jnp.mod(group_me - r // share_rows, group_size)
        return d * group_size + k, r % share_rows

    wanted = block_columns.reshape(slot_total)
    column_panel = wanted // panel_length
    distance = jnp.mod(column_panel - me + 2, panel_total)
    piece_of, within = placed(distance, wanted % panel_length)
    window_pair = piece_of * piece_rows + within // 2
    own_piece, own_within = placed(2, jnp.arange(panel_length, dtype=jnp.int32))
    own_pos = own_piece * piece_rows + own_within // 2
    slot_ids = lax.axis_index("grp") * slots_here + jnp.arange(slots_here, dtype=jnp.int32)
    live = (slot_ids[None, :] < row_counts[:, None]).astype(jnp.int32).reshape(slot_total)
    block_values, _ = lax.optimization_barrier((block_values, down1[-1]))
    summed = coarse_partial(
        window_pair.astype(jnp.int32),
        (within % 2).astype(jnp.int32),
        (piece_of * share_rows + within).astype(jnp.int32),
        (own_piece * share_rows + own_within).astype(jnp.int32),
        flat_aggs,
        jnp.reshape(me * CB, (1,)).astype(jnp.int32),
        live,
        own_pos,
        fix,
        block_values,
        pieces,
        fixed,
        coarse_count * CB,
    )
    share = coarse_count // group_size
    summed = summed.reshape(group_size, share, CB // 2, block_size, 2 * block_size)
    total = jnp.take(summed, group_me, axis=0)
    for k in range(1, group_size):
        outgoing = jnp.take(summed, jnp.mod(group_me + k, group_size), axis=0)
        incoming = lax.ppermute(
            outgoing.astype(jnp.bfloat16),
            "grp",
            [(i, (i + k) % group_size) for i in range(group_size)],
        )
        total = total + incoming.astype(jnp.float32)
    total = total.reshape(share, CB // 2, block_size, 2, block_size)
    return total.transpose(0, 1, 3, 2, 4).reshape(share, CB, block_size, block_size)


def solution(mesh):
    return jax.shard_map(
        local,
        mesh=mesh,
        in_specs=(
            P("blk", "grp", None, None),
            P("blk", "grp"),
            P("blk"),
            P(("blk", "grp"), None, None),
            P(("blk", "grp")),
        ),
        out_specs=P("grp", "blk", None, None),
        check_vma=False,
    )
```
